32 devices in a mesh: groups: 2 (over y), req: 4 (over z), head: 2 (over x), sub: 2 (over core).
Axes of the slice: x: 2, y: 2, z: 4, core: 2. Of those that a mesh axis runs over, the one named last changes fastest.
Arguments:
- hidden_in: bfloat16 [1024, 8192], P(('groups', 'req')), parts along dimension 0, may hold values from -3 to 3
- q_weight: bfloat16 [8192, 8192], P('req', ('head', 'sub')), may hold values from -0.0625 to 0.0625
- q_gain: float32 [128], replicated, may hold values from 0.1 to 1.9
- key_cache: bfloat16 [8, 1601, 1024], P(('groups', 'req'), None, 'head'), parts along dimension 0, may hold values from -64 to 64
- value_cache: bfloat16 [8, 1601, 1024], P(('groups', 'req'), None, 'head'), parts along dimension 0, may hold values from -8 to 8
- out_weight: bfloat16 [8192, 8192], P(('head', 'sub'), 'req'), may hold values from -0.09375 to 0.09375
- req_image: int32 [1024], P(('groups', 'req')), parts along dimension 0, may hold values from 0 to 3, as said below
- image_count: int32 [1024], P(('groups', 'req')), parts along dimension 0, may hold values from 0 to 1, as said below
- image_home: int32 [8], P('groups'), parts along dimension 0, may hold values from 0 to 3, as said below
Outputs:
- layer_out: bfloat16 [1024, 8192], P(('groups', 'req'), ('head', 'sub')), parts along dimension 0
The draws below stay inside these ranges and needn't reach their ends.
There are 2 independent parts, one for each index of `groups`. The reference program is written for one: setup_inputs(seed, part) draws one part's arguments, and reference() takes and returns one part's arrays. A program takes and returns all parts, laid end to end along the dimension named above; an argument that names none is the same for every part. Nothing has to cross between parts.
Inputs may be any that keep to these rules, and one draw needn't show every extreme that they name: Requests with image_count 0 attend to nothing; in each aligned block of 128 requests at most a quarter have image_count 0. In each aligned block of 128 requests, at most 64 requests with image_count 1 have one and the same value of image_home[req_image]; in every block exactly 64 of them share one value, and that value is the same for all blocks. `image_home`: each cache row holds exactly one image.
All inputs are finite; a program needn't handle non-finite values.
Results may differ from the reference program's by a relative error of at most 0.025.
Values may be sent and summed in bfloat16 or wider, within the bound.
No kernel may reach another device: no remote copies, remote signals or barrier semaphores. Data moves between devices by JAX's collectives and lax.ppermute only.
A program may use at most 128 MiB of HBM per device.

```python
import jax
import jax.numpy as jnp
from jax import lax

D = 8192
HQ = 64
KVH = 8
HD = 128
TOK = 1601
R_DEV = 128
REQS = 512
IMAGES = 4
CAP = 64
N_REQ = 4
N_HEAD = 2
N_SUB = 2


def routing_tables(key):
    base_key = jax.random.fold_in(key, 29)
    key_hot, key_blocks = jax.random.split(base_key, 2)
    key_home = jax.random.fold_in(jax.random.fold_in(key, 97), 5)
    image_home = jax.random.permutation(key_home, IMAGES).astype(jnp.int32)
    image_at_row = jnp.zeros((IMAGES,), jnp.int32).at[image_home].set(jnp.arange(IMAGES, dtype=jnp.int32))
    hottest = jax.random.randint(key_hot, (), 0, IMAGES).astype(jnp.int32)
    others = (hottest + 1 + jnp.arange(IMAGES - 1, dtype=jnp.int32)) % IMAGES
    spread = jnp.repeat(others, CAP)

    def one_block(block_key):
        key_perm, key_skip, key_order, key_free = jax.random.split(block_key, 4)
        tickets = jnp.concatenate([jnp.zeros((CAP,), jnp.int32) + hottest, jax.random.permutation(key_perm, spread)])
        skipped = jax.random.randint(key_skip, (), 0, R_DEV // 4 + 1).astype(jnp.int32)
        visit_order = jax.random.permutation(key_order, R_DEV).astype(jnp.int32)
        rank_of = jnp.zeros((R_DEV,), jnp.int32).at[visit_order].set(jnp.arange(R_DEV, dtype=jnp.int32))
        counts = (rank_of >= skipped).astype(jnp.int32)
        ticket_index = jnp.clip(rank_of - skipped, 0, tickets.shape[0] - 1)
        home_pick = tickets[ticket_index]
        unused_image = jax.random.randint(key_free, (R_DEV,), 0, IMAGES).astype(jnp.int32)
        chosen_image = jnp.where(counts == 1, image_at_row[home_pick], unused_image)
        return (chosen_image, counts)
    block_keys = jax.random.split(key_blocks, IMAGES)
    images, counts = jax.vmap(one_block)(block_keys)
    return (images.reshape(-1).astype(jnp.int32), counts.reshape(-1).astype(jnp.int32), image_home)


def draw_req_image(key, part):
    return routing_tables(key)[0]


def draw_image_count(key, part):
    return routing_tables(key)[1]


def draw_image_home(key, part):
    return routing_tables(key)[2]


def draw_key_cache(key, part):
    cache_shape = (IMAGES, TOK, KVH * HD)
    drawn = jnp.clip(2.0 * jax.random.normal(jax.random.fold_in(key, 4), cache_shape, jnp.float32), -8.0, 8.0)
    return drawn.astype(jnp.bfloat16)


def with_spikes(entries, key, source, target, blocks, factor):
    def block_of(position):
        return (jnp.arange(entries.shape[position]) // (entries.shape[position] // blocks)).reshape((-1,) + (1,) * (entries.ndim - 1 - position))

    near = jax.random.permutation(key, blocks)[block_of(target)]
    far = (block_of(target) + blocks // 2) % blocks
    return jnp.where((block_of(source) == near) | (block_of(source) == far), factor * entries, entries)


def shard_levels(key, dims, pieces, low, largest):
    def one(dim, blocks):
        draws = jax.random.uniform(jax.random.fold_in(jax.random.fold_in(key, 6), dim), (blocks,), jnp.float32, low / len(pieces), largest / len(pieces))
        return jnp.repeat(jnp.exp(draws), dims[dim] // blocks).reshape((-1,) + (1,) * (len(dims) - dim - 1))

    level = one(*pieces[0])
    for cut in pieces[1:]:
        level = level * one(*cut)
    return level


def centred(own_key, dims, deviation, reach, cuts=(), kind=jnp.bfloat16):
    factor_of = shard_levels(own_key, dims, cuts, -0.22, 0.18) if cuts else 1.0
    entries = jax.random.normal(own_key, dims, jnp.float32) * deviation * factor_of
    return jnp.minimum(jnp.maximum(entries, -reach), reach).astype(kind)


def bell_draw_with(stream_key, shape, width, most, shards, heavy, kind=jnp.bfloat16):
    result = width * jax.random.normal(stream_key, shape, jnp.float32)
    if shards:
        result = result * shard_levels(stream_key, shape, shards, -0.22, 0.18)
    return jnp.clip(with_spikes(result, jax.random.fold_in(stream_key, 3), *heavy), -most, most).astype(kind)


def setup_inputs(seed: int = 0, part: int = 0) -> dict:
    seeds = jax.random.split(jax.random.key(seed), 10)
    part_keys = jax.random.split(jax.random.fold_in(seeds[9], part), 10)
    return {
        "hidden_in": centred(part_keys[0], (REQS, D), 0.5, 3.0, ((0, 4),)),
        "q_weight": centred(seeds[1], (D, HQ * HD), D ** -0.5, 0.0625, ((0, 4), (1, 4))),
        "q_gain": jnp.clip(1.0 + 0.18 * jax.random.normal(seeds[2], (HD,), jnp.float32), 0.1, 1.9),
        "key_cache": draw_key_cache(jax.random.fold_in(jax.random.fold_in(seeds[9], part), 71), part),
        "value_cache": centred(part_keys[4], (IMAGES, TOK, KVH * HD), 2.0, 8.0, ((0, 4), (2, 2))),
        "out_weight": bell_draw_with(seeds[5], (HQ * HD, D), (HQ * HD) ** -0.5, 0.09375, ((0, 4), (1, 4)), (0, 1, 4, 2.0)),
        "req_image": draw_req_image(jax.random.fold_in(jax.random.fold_in(seeds[9], part), 71), part),
        "image_count": draw_image_count(jax.random.fold_in(jax.random.fold_in(seeds[9], part), 71), part),
        "image_home": draw_image_home(jax.random.fold_in(jax.random.fold_in(seeds[9], part), 71), part),
    }


def normalize_heads(queries, q_gain, head_dim):
    row_count = queries.shape[0]
    per_head = queries.astype(jnp.float32).reshape(row_count, -1, head_dim)
    inv_rms = lax.rsqrt(lax.optimization_barrier(jnp.mean(per_head * per_head, axis=2, keepdims=True)) + 1e-05)
    return (per_head * inv_rms * q_gain).reshape(row_count, -1).astype(jnp.bfloat16)

def reference(hidden_in, q_weight, q_gain, key_cache, value_cache, out_weight, req_image, image_count, image_home):
    row_total = hidden_in.shape[0]
    feat_block = D // N_REQ
    q_width = HQ * HD

    def add_block(running, block_index):
        column_part = lax.dynamic_slice_in_dim(hidden_in, block_index * feat_block, feat_block, 1)
        weight_part = lax.dynamic_slice_in_dim(q_weight, block_index * feat_block, feat_block, 0)
        partial_value = lax.optimization_barrier(jnp.dot(column_part, weight_part, preferred_element_type=jnp.float32).astype(jnp.bfloat16))
        return (running + partial_value.astype(jnp.float32), None)
    query_sum, _ = lax.scan(add_block, jnp.zeros((row_total, q_width), jnp.float32), jnp.arange(N_REQ, dtype=jnp.int32))
    queries = lax.optimization_barrier(query_sum.astype(jnp.bfloat16))
    normalized = normalize_heads(queries, q_gain, HD)
    home_row = image_home[req_image].astype(jnp.int32)
    group_size = HQ // KVH
    request_block = 8

    def attend_block(block_args):
        rows_here, queries_here, counts_here = block_args
        key_rows = key_cache[rows_here].astype(jnp.float32).reshape(request_block, TOK, KVH, HD)
        value_rows = value_cache[rows_here].astype(jnp.float32).reshape(request_block, TOK, KVH, HD)
        query_part = queries_here.astype(jnp.float32).reshape(request_block, KVH, group_size, HD)
        scores = jnp.einsum('bkgd,btkd->bkgt', query_part, key_rows) * HD ** (-0.5)
        scores = scores - lax.optimization_barrier(jnp.max(scores, axis=3, keepdims=True))
        weights = jnp.exp(scores)
        probs = (weights / lax.optimization_barrier(jnp.sum(weights, axis=3, keepdims=True))).astype(jnp.bfloat16)
        mixed_heads = jnp.einsum('bkgt,btkd->bkgd', probs.astype(jnp.float32), value_rows)
        mixed_heads = mixed_heads.astype(jnp.bfloat16).reshape(request_block, q_width)
        return jnp.where(counts_here[:, None] == 1, mixed_heads, jnp.zeros_like(mixed_heads))
    attended = lax.map(attend_block, (home_row.reshape(-1, request_block), normalized.reshape(-1, request_block, q_width), image_count.reshape(-1, request_block)))
    attended = attended.reshape(row_total, q_width)
    group_cols = q_width // (N_HEAD * N_SUB)

    def add_group(running, group_index):
        column_part = lax.dynamic_slice_in_dim(attended, group_index * group_cols, group_cols, 1)
        weight_part = lax.dynamic_slice_in_dim(out_weight, group_index * group_cols, group_cols, 0)
        partial_value = lax.optimization_barrier(jnp.dot(column_part, weight_part, preferred_element_type=jnp.float32).astype(jnp.bfloat16))
        return (running + partial_value.astype(jnp.float32), None)
    head_total, _ = lax.scan(add_group, jnp.zeros((row_total, D), jnp.float32), jnp.arange(N_HEAD * N_SUB, dtype=jnp.int32))
    return (hidden_in.astype(jnp.float32) + head_total).astype(jnp.bfloat16)
```

```python
import jax
import jax.numpy as jnp
from jax import lax
from jax.sharding import PartitionSpec as P

HQ = 64
KVH = 8


def normalize_heads(queries, q_gain, head_dim):
    row_count = queries.shape[0]
    per_head = queries.astype(jnp.float32).reshape(row_count, -1, head_dim)
    inv_rms = lax.rsqrt(jnp.mean(per_head * per_head, axis=2, keepdims=True) + 1e-05)
    return (per_head * inv_rms * q_gain).reshape(row_count, -1).astype(jnp.bfloat16)


def local(
    hidden_in,
    q_weight,
    q_gain,
    key_cache,
    value_cache,
    out_weight,
    req_image,
    image_count,
    image_home,
):
    req_count = lax.axis_size("req")
    local_rows = hidden_in.shape[0]
    q_cols = q_weight.shape[1]
    head_dim = q_gain.shape[0]
    group_size = HQ // KVH
    heads_here = q_cols // head_dim
    sub_count = lax.axis_size("sub")
    sub_index = lax.axis_index("sub")
    block_width = hidden_in.shape[1] // req_count
    part_width = block_width // sub_count
    by_block = hidden_in.reshape(local_rows, req_count, sub_count, part_width)
    my_part = lax.dynamic_index_in_dim(by_block, sub_index, axis=2, keepdims=False)
    spread_part = lax.all_to_all(my_part, "req", split_axis=1, concat_axis=0, tiled=True)
    spread_cols = lax.all_gather(
        spread_part.reshape(req_count * local_rows, part_width), "sub", axis=1, tiled=True
    )
    query_sum = lax.psum_scatter(
        jnp.dot(spread_cols, q_weight, preferred_element_type=jnp.float32).astype(jnp.bfloat16),
        "req",
        scatter_dimension=0,
        tiled=True,
    )
    queries = lax.optimization_barrier(query_sum)
    normalized = normalize_heads(queries, q_gain, head_dim)
    capacity = 2 * local_rows // req_count
    slot_total = req_count * capacity
    table_ids = lax.broadcasted_iota(jnp.int32, (local_rows, image_home.shape[0]), 1)
    home_rows = jnp.sum(jnp.where(req_image[:, None] == table_ids, image_home[None, :], 0), axis=1)
    wanted = image_count == 1
    dest_ids = lax.broadcasted_iota(jnp.int32, (local_rows, req_count), 1)
    to_dest = ((home_rows[:, None] == dest_ids) & wanted[:, None]).astype(jnp.int32)
    earlier = jnp.cumsum(to_dest, axis=0) - to_dest
    position = home_rows * capacity + jnp.sum(earlier * to_dest, axis=1)
    slot_ids = lax.broadcasted_iota(jnp.int32, (slot_total, local_rows), 0)
    dispatch = ((slot_ids == position[None, :]) & wanted[None, :]).astype(jnp.bfloat16)
    outgoing = jnp.dot(dispatch, normalized, preferred_element_type=jnp.float32).astype(
        jnp.bfloat16
    )
    outgoing = outgoing.reshape(req_count, capacity, q_cols)
    kv_count = max(1, heads_here // group_size)
    per_kv = heads_here // kv_count
    kv_first = sub_index * heads_here // group_size
    keys_here = lax.dynamic_slice_in_dim(
        key_cache[0], kv_first * head_dim, kv_count * head_dim, 1
    ).reshape(-1, kv_count, head_dim)
    values_here = lax.dynamic_slice_in_dim(
        value_cache[0], kv_first * head_dim, kv_count * head_dim, 1
    ).reshape(-1, kv_count, head_dim)
    score_scale = head_dim ** (-0.5)
    arrived = lax.all_to_all(outgoing, "req", split_axis=0, concat_axis=0, tiled=True)
    sources = arrived.shape[0]
    slot_count = arrived.shape[1]
    flat_rows = arrived.reshape(sources * slot_count, kv_count, per_kv, head_dim)
    scores = (
        jnp.einsum("mkgd,tkd->kgmt", flat_rows, keys_here, preferred_element_type=jnp.float32)
        * score_scale
    )
    row_peak = jnp.max(scores, axis=3, keepdims=True)
    weights = jnp.exp(scores - row_peak)
    probs = (weights / jnp.sum(weights, axis=3, keepdims=True)).astype(jnp.bfloat16)
    mixed_heads = jnp.einsum(
        "kgmt,tkd->mkgd", probs, values_here, preferred_element_type=jnp.float32
    )
    replies = mixed_heads.astype(jnp.bfloat16).reshape(sources, slot_count, q_cols)
    returned = lax.all_to_all(replies, "req", split_axis=0, concat_axis=0, tiled=True)
    attended = lax.dot_general(
        dispatch,
        returned.reshape(slot_total, q_cols),
        (((0,), (0,)), ((), ())),
        preferred_element_type=jnp.float32,
    ).astype(jnp.bfloat16)
    partial_cols = jnp.dot(
        lax.all_gather(attended, "req", axis=0, tiled=True),
        out_weight,
        preferred_element_type=jnp.float32,
    ).astype(jnp.bfloat16)
    hs_count = lax.axis_size("head") * sub_count
    hs_index = lax.axis_index("head") * sub_count + sub_index
    req_index = lax.axis_index("req")
    owner_sums = lax.psum_scatter(
        partial_cols, ("head", "sub"), scatter_dimension=0, tiled=True
    )
    per_hs = req_count // hs_count
    out_block = partial_cols.shape[1]
    owner_sums = owner_sums.reshape(per_hs, local_rows, out_block)
    arrived_blocks = []
    for step in range(per_hs):
        chunk = lax.dynamic_index_in_dim(
            owner_sums, (req_index + step) % per_hs, axis=0, keepdims=False
        )
        pairs = []
        for c in range(req_count):
            for j in range(hs_count):
                k = j * per_hs + (c + step) % per_hs
                pairs.append((c * hs_count + j, k * hs_count + c // per_hs))
        arrived_blocks.append(lax.ppermute(chunk, ("req", "head", "sub"), pairs))
    stacked = jnp.stack(arrived_blocks)
    order = (req_index % per_hs - jnp.arange(per_hs)) % per_hs
    head_total = jnp.take(stacked, order, axis=0)
    head_total = jnp.transpose(head_total, (1, 0, 2)).reshape(local_rows, per_hs * out_block)
    head_total = head_total.astype(jnp.float32)
    out_width = head_total.shape[1]
    residual = lax.dynamic_slice_in_dim(hidden_in, hs_index * out_width, out_width, 1)
    return (residual.astype(jnp.float32) + head_total).astype(jnp.bfloat16)


def solution(mesh):
    in_specs = (
        P(("groups", "req"), None),
        P("req", ("head", "sub")),
        P(),
        P(("groups", "req"), None, "head"),
        P(("groups", "req"), None, "head"),
        P(("head", "sub"), "req"),
        P(("groups", "req")),
        P(("groups", "req")),
        P("groups"),
    )
    out_specs = P(("groups", "req"), ("head", "sub"))
    return jax.shard_map(local, mesh=mesh, in_specs=in_specs, out_specs=out_specs, check_vma=False)
```

```python
import jax
import jax.numpy as jnp
from jax import lax
from jax.sharding import PartitionSpec as P

HQ = 64
KVH = 8


def normalize_heads(queries, q_gain, head_dim):
    row_count = queries.shape[0]
    per_head = queries.astype(jnp.float32).reshape(row_count, -1, head_dim)
    inv_rms = lax.rsqrt(jnp.mean(per_head * per_head, axis=2, keepdims=True) + 1e-05)
    return (per_head * inv_rms * q_gain).reshape(row_count, -1).astype(jnp.bfloat16)


def local(
    hidden_in,
    q_weight,
    q_gain,
    key_cache,
    value_cache,
    out_weight,
    req_image,
    image_count,
    image_home,
):
    req_count = lax.axis_size("req")
    local_rows = hidden_in.shape[0]
    q_cols = q_weight.shape[1]
    head_dim = q_gain.shape[0]
    group_size = HQ // KVH
    heads_here = q_cols // head_dim
    sub_count = lax.axis_size("sub")
    sub_index = lax.axis_index("sub")
    block_width = hidden_in.shape[1] // req_count
    part_width = block_width // sub_count
    by_block = hidden_in.reshape(local_rows, req_count, sub_count, part_width)
    my_part = lax.dynamic_index_in_dim(by_block, sub_index, axis=2, keepdims=False)
    spread_part = lax.all_to_all(my_part, "req", split_axis=1, concat_axis=0, tiled=True)
    spread_part = spread_part.reshape(req_count * local_rows, part_width)
    spread_cols = jnp.zeros((req_count * local_rows, block_width), spread_part.dtype)
    spread_cols = lax.dynamic_update_slice_in_dim(
        spread_cols, spread_part, sub_index * part_width, 1
    )
    for shift in range(1, sub_count):
        other_part = lax.ppermute(
            spread_part, "sub", [(i, (i + shift) % sub_count) for i in range(sub_count)]
        )
        spread_cols = lax.dynamic_update_slice_in_dim(
            spread_cols, other_part, ((sub_index - shift) % sub_count) * part_width, 1
        )
    query_sum = lax.psum_scatter(
        jnp.dot(spread_cols, q_weight, preferred_element_type=jnp.float32).astype(jnp.bfloat16),
        "req",
        scatter_dimension=0,
        tiled=True,
    )
    queries = lax.optimization_barrier(query_sum)
    normalized = normalize_heads(queries, q_gain, head_dim)
    capacity = 2 * local_rows // req_count
    slot_total = req_count * capacity
    table_ids = lax.broadcasted_iota(jnp.int32, (local_rows, image_home.shape[0]), 1)
    home_rows = jnp.sum(jnp.where(req_image[:, None] == table_ids, image_home[None, :], 0), axis=1)
    wanted = image_count == 1
    dest_ids = lax.broadcasted_iota(jnp.int32, (local_rows, req_count), 1)
    to_dest = ((home_rows[:, None] == dest_ids) & wanted[:, None]).astype(jnp.int32)
    earlier = jnp.cumsum(to_dest, axis=0) - to_dest
    position = home_rows * capacity + jnp.sum(earlier * to_dest, axis=1)
    slot_ids = lax.broadcasted_iota(jnp.int32, (slot_total, local_rows), 0)
    dispatch = ((slot_ids == position[None, :]) & wanted[None, :]).astype(jnp.bfloat16)
    outgoing = jnp.dot(dispatch, normalized, preferred_element_type=jnp.float32).astype(
        jnp.bfloat16
    )
    outgoing = outgoing.reshape(req_count, capacity, q_cols)
    kv_count = max(1, heads_here // group_size)
    per_kv = heads_here // kv_count
    kv_first = sub_index * heads_here // group_size
    keys_here = lax.dynamic_slice_in_dim(
        key_cache[0], kv_first * head_dim, kv_count * head_dim, 1
    ).reshape(-1, kv_count, head_dim)
    values_here = lax.dynamic_slice_in_dim(
        value_cache[0], kv_first * head_dim, kv_count * head_dim, 1
    ).reshape(-1, kv_count, head_dim)
    score_scale = head_dim ** (-0.5)
    arrived = lax.all_to_all(outgoing, "req", split_axis=0, concat_axis=0, tiled=True)
    sources = arrived.shape[0]
    slot_count = arrived.shape[1]
    flat_rows = arrived.reshape(sources * slot_count, kv_count, per_kv, head_dim)
    scores = (
        jnp.einsum("mkgd,tkd->kgmt", flat_rows, keys_here, preferred_element_type=jnp.float32)
        * score_scale
    )
    row_peak = jnp.max(scores, axis=3, keepdims=True)
    weights = jnp.exp(scores - row_peak)
    probs = (weights / jnp.sum(weights, axis=3, keepdims=True)).astype(jnp.bfloat16)
    mixed_heads = jnp.einsum(
        "kgmt,tkd->mkgd", probs, values_here, preferred_element_type=jnp.float32
    )
    replies = mixed_heads.astype(jnp.bfloat16).reshape(sources, slot_count, q_cols)
    returned = lax.all_to_all(replies, "req", split_axis=0, concat_axis=0, tiled=True)
    attended = lax.dot_general(
        dispatch,
        returned.reshape(slot_total, q_cols),
        (((0,), (0,)), ((), ())),
        preferred_element_type=jnp.float32,
    ).astype(jnp.bfloat16)
    partial_cols = jnp.dot(
        lax.all_gather(attended, "req", axis=0, tiled=True),
        out_weight,
        preferred_element_type=jnp.float32,
    ).astype(jnp.bfloat16)
    hs_count = lax.axis_size("head") * sub_count
    hs_index = lax.axis_index("head") * sub_count + sub_index
    req_index = lax.axis_index("req")
    head_count = lax.axis_size("head")
    by_group = partial_cols.reshape(sub_count, -1, partial_cols.shape[1])
    owner_sums = lax.psum_scatter(by_group, "sub", scatter_dimension=0, tiled=True)
    owner_sums = owner_sums.reshape(head_count, -1, partial_cols.shape[1])
    owner_sums = lax.psum_scatter(owner_sums, "head", scatter_dimension=0, tiled=True)
    per_hs = req_count // hs_count
    out_block = partial_cols.shape[1]
    owner_sums = owner_sums.reshape(per_hs, local_rows, out_block)
    arrived_blocks = []
    for step in range(per_hs):
        chunk = lax.dynamic_index_in_dim(
            owner_sums, (req_index + step) % per_hs, axis=0, keepdims=False
        )
        pairs = []
        for c in range(req_count):
            for h in range(head_count):
                for u in range(sub_count):
                    j = u * head_count + h
                    k = j * per_hs + (c + step) % per_hs
                    src = c * hs_count + h * sub_count + u
                    pairs.append((src, k * hs_count + c // per_hs))
        arrived_blocks.append(lax.ppermute(chunk, ("req", "head", "sub"), pairs))
    stacked = jnp.stack(arrived_blocks)
    order = (req_index % per_hs - jnp.arange(per_hs)) % per_hs
    head_total = jnp.take(stacked, order, axis=0)
    head_total = jnp.transpose(head_total, (1, 0, 2)).reshape(local_rows, per_hs * out_block)
    head_total = head_total.astype(jnp.float32)
    out_width = head_total.shape[1]
    residual = lax.dynamic_slice_in_dim(hidden_in, hs_index * out_width, out_width, 1)
    return (residual.astype(jnp.float32) + head_total).astype(jnp.bfloat16)


def solution(mesh):
    in_specs = (
        P(("groups", "req"), None),
        P("req", ("head", "sub")),
        P(),
        P(("groups", "req"), None, "head"),
        P(("groups", "req"), None, "head"),
        P(("head", "sub"), "req"),
        P(("groups", "req")),
        P(("groups", "req")),
        P("groups"),
    )
    out_specs = P(("groups", "req"), ("head", "sub"))
    return jax.shard_map(local, mesh=mesh, in_specs=in_specs, out_specs=out_specs, check_vma=False)
```

```python
import jax
import jax.numpy as jnp
from jax import lax
from jax.sharding import PartitionSpec as P

HQ = 64
KVH = 8


def normalize_heads(queries, q_gain, head_dim):
    row_count = queries.shape[0]
    per_head = queries.astype(jnp.float32).reshape(row_count, -1, head_dim)
    inv_rms = lax.rsqrt(jnp.mean(per_head * per_head, axis=2, keepdims=True) + 1e-05)
    return (per_head * inv_rms * q_gain).reshape(row_count, -1).astype(jnp.bfloat16)


def exchange_sum(parts, axis, count, index):
    total = lax.dynamic_index_in_dim(parts, index, axis=0, keepdims=False).astype(jnp.float32)
    for shift in range(1, count):
        outgoing = lax.dynamic_index_in_dim(parts, (index + shift) % count, axis=0, keepdims=False)
        incoming = lax.ppermute(outgoing, axis, [(i, (i + shift) % count) for i in range(count)])
        total = total + incoming.astype(jnp.float32)
    return total.astype(jnp.bfloat16)


def local(
    hidden_in,
    q_weight,
    q_gain,
    key_cache,
    value_cache,
    out_weight,
    req_image,
    image_count,
    image_home,
):
    req_count = lax.axis_size("req")
    local_rows = hidden_in.shape[0]
    q_cols = q_weight.shape[1]
    head_dim = q_gain.shape[0]
    group_size = HQ // KVH
    heads_here = q_cols // head_dim
    sub_count = lax.axis_size("sub")
    sub_index = lax.axis_index("sub")
    block_width = hidden_in.shape[1] // req_count
    part_width = block_width // sub_count
    by_block = hidden_in.reshape(local_rows, req_count, sub_count, part_width)
    my_part = lax.dynamic_index_in_dim(by_block, sub_index, axis=2, keepdims=False)
    spread_part = lax.all_to_all(my_part, "req", split_axis=1, concat_axis=0, tiled=True)
    spread_part = spread_part.reshape(req_count * local_rows, part_width)
    spread_cols = jnp.zeros((req_count * local_rows, block_width), spread_part.dtype)
    spread_cols = lax.dynamic_update_slice_in_dim(
        spread_cols, spread_part, sub_index * part_width, 1
    )
    for shift in range(1, sub_count):
        other_part = lax.ppermute(
            spread_part, "sub", [(i, (i + shift) % sub_count) for i in range(sub_count)]
        )
        spread_cols = lax.dynamic_update_slice_in_dim(
            spread_cols, other_part, ((sub_index - shift) % sub_count) * part_width, 1
        )
    query_sum = lax.psum_scatter(
        jnp.dot(spread_cols, q_weight, preferred_element_type=jnp.float32).astype(jnp.bfloat16),
        "req",
        scatter_dimension=0,
        tiled=True,
    )
    queries = lax.optimization_barrier(query_sum)
    normalized = normalize_heads(queries, q_gain, head_dim)
    capacity = 2 * local_rows // req_count
    slot_total = req_count * capacity
    table_ids = lax.broadcasted_iota(jnp.int32, (local_rows, image_home.shape[0]), 1)
    home_rows = jnp.sum(jnp.where(req_image[:, None] == table_ids, image_home[None, :], 0), axis=1)
    wanted = image_count == 1
    dest_ids = lax.broadcasted_iota(jnp.int32, (local_rows, req_count), 1)
    to_dest = ((home_rows[:, None] == dest_ids) & wanted[:, None]).astype(jnp.int32)
    earlier = jnp.cumsum(to_dest, axis=0) - to_dest
    position = home_rows * capacity + jnp.sum(earlier * to_dest, axis=1)
    slot_ids = lax.broadcasted_iota(jnp.int32, (slot_total, local_rows), 0)
    dispatch = ((slot_ids == position[None, :]) & wanted[None, :]).astype(jnp.bfloat16)
    outgoing = jnp.dot(dispatch, normalized, preferred_element_type=jnp.float32).astype(
        jnp.bfloat16
    )
    outgoing = outgoing.reshape(req_count, capacity, q_cols)
    kv_count = max(1, heads_here // group_size)
    per_kv = heads_here // kv_count
    kv_first = sub_index * heads_here // group_size
    keys_here = lax.dynamic_slice_in_dim(
        key_cache[0], kv_first * head_dim, kv_count * head_dim, 1
    ).reshape(-1, kv_count, head_dim)
    values_here = lax.dynamic_slice_in_dim(
        value_cache[0], kv_first * head_dim, kv_count * head_dim, 1
    ).reshape(-1, kv_count, head_dim)
    score_scale = head_dim ** (-0.5)
    arrived = lax.all_to_all(outgoing, "req", split_axis=0, concat_axis=0, tiled=True)
    sources = arrived.shape[0]
    slot_count = arrived.shape[1]
    flat_rows = arrived.reshape(sources * slot_count, kv_count, per_kv, head_dim)
    scores = (
        jnp.einsum("mkgd,tkd->kgmt", flat_rows, keys_here, preferred_element_type=jnp.float32)
        * score_scale
    )
    row_peak = jnp.max(scores, axis=3, keepdims=True)
    weights = jnp.exp(scores - row_peak)
    probs = (weights / jnp.sum(weights, axis=3, keepdims=True)).astype(jnp.bfloat16)
    mixed_heads = jnp.einsum(
        "kgmt,tkd->mkgd", probs, values_here, preferred_element_type=jnp.float32
    )
    replies = mixed_heads.astype(jnp.bfloat16).reshape(sources, slot_count, q_cols)
    returned = lax.all_to_all(replies, "req", split_axis=0, concat_axis=0, tiled=True)
    attended = lax.dot_general(
        dispatch,
        returned.reshape(slot_total, q_cols),
        (((0,), (0,)), ((), ())),
        preferred_element_type=jnp.float32,
    ).astype(jnp.bfloat16)
    partial_cols = jnp.dot(
        lax.all_gather(attended, "req", axis=0, tiled=True),
        out_weight,
        preferred_element_type=jnp.float32,
    ).astype(jnp.bfloat16)
    hs_count = lax.axis_size("head") * sub_count
    hs_index = lax.axis_index("head") * sub_count + sub_index
    req_index = lax.axis_index("req")
    head_count = lax.axis_size("head")
    by_group = partial_cols.reshape(sub_count, -1, partial_cols.shape[1])
    owner_sums = exchange_sum(by_group, "sub", sub_count, sub_index)
    owner_sums = owner_sums.reshape(head_count, -1, partial_cols.shape[1])
    owner_sums = exchange_sum(owner_sums, "head", head_count, lax.axis_index("head"))
    per_hs = req_count // hs_count
    out_block = partial_cols.shape[1]
    owner_sums = owner_sums.reshape(per_hs, local_rows, out_block)
    arrived_blocks = []
    for step in range(per_hs):
        chunk = lax.dynamic_index_in_dim(
            owner_sums, (req_index + step) % per_hs, axis=0, keepdims=False
        )
        pairs = []
        for c in range(req_count):
            for h in range(head_count):
                for u in range(sub_count):
                    j = u * head_count + h
                    k = j * per_hs + (c + step) % per_hs
                    src = c * hs_count + h * sub_count + u
                    pairs.append((src, k * hs_count + c // per_hs))
        arrived_blocks.append(lax.ppermute(chunk, ("req", "head", "sub"), pairs))
    stacked = jnp.stack(arrived_blocks)
    order = (req_index % per_hs - jnp.arange(per_hs)) % per_hs
    head_total = jnp.take(stacked, order, axis=0)
    head_total = jnp.transpose(head_total, (1, 0, 2)).reshape(local_rows, per_hs * out_block)
    head_total = head_total.astype(jnp.float32)
    out_width = head_total.shape[1]
    residual = lax.dynamic_slice_in_dim(hidden_in, hs_index * out_width, out_width, 1)
    return (residual.astype(jnp.float32) + head_total).astype(jnp.bfloat16)


def solution(mesh):
    in_specs = (
        P(("groups", "req"), None),
        P("req", ("head", "sub")),
        P(),
        P(("groups", "req"), None, "head"),
        P(("groups", "req"), None, "head"),
        P(("head", "sub"), "req"),
        P(("groups", "req")),
        P(("groups", "req")),
        P("groups"),
    )
    out_specs = P(("groups", "req"), ("head", "sub"))
    return jax.shard_map(local, mesh=mesh, in_specs=in_specs, out_specs=out_specs, check_vma=False)
```

```python
import functools

import jax
import jax.numpy as jnp
from jax import lax
from jax.sharding import PartitionSpec as P
from jax.experimental import pallas as pl

HQ = 64
KVH = 8


def normalize_heads(queries, q_gain, head_dim):
    row_count = queries.shape[0]
    per_head = queries.astype(jnp.float32).reshape(row_count, -1, head_dim)
    inv_rms = lax.rsqrt(jnp.mean(per_head * per_head, axis=2, keepdims=True) + 1e-05)
    return (per_head * inv_rms * q_gain).reshape(row_count, -1).astype(jnp.bfloat16)


def exchange_sum(parts, axis, count, index):
    total = lax.dynamic_index_in_dim(parts, index, axis=0, keepdims=False).astype(jnp.float32)
    for shift in range(1, count):
        outgoing = lax.dynamic_index_in_dim(parts, (index + shift) % count, axis=0, keepdims=False)
        incoming = lax.ppermute(outgoing, axis, [(i, (i + shift) % count) for i in range(count)])
        total = total + incoming.astype(jnp.float32)
    return total.astype(jnp.bfloat16)


def attend_kernel(q_ref, k_ref, v_ref, o_ref, *, per_kv, head_dim, token_count):
    keys = k_ref[...]
    values = v_ref[...]
    rows = q_ref.shape[0]
    valid = lax.broadcasted_iota(jnp.int32, (rows, keys.shape[0]), 1) < token_count
    score_scale = head_dim ** (-0.5)
    for g in range(per_kv):
        query = q_ref[:, g * head_dim:(g + 1) * head_dim]
        scores = lax.dot_general(
            query, keys, (((1,), (1,)), ((), ())), preferred_element_type=jnp.float32
        ) * score_scale
        scores = jnp.where(valid, scores, -jnp.inf)
        peak = jnp.max(scores, axis=1, keepdims=True)
        weights = jnp.exp(scores - peak)
        probs = (weights / jnp.sum(weights, axis=1, keepdims=True)).astype(jnp.bfloat16)
        mixed = jnp.dot(probs, values, preferred_element_type=jnp.float32)
        o_ref[:, g * head_dim:(g + 1) * head_dim] = mixed.astype(o_ref.dtype)


def attend(rows_in, keys, values, kv_count, per_kv, head_dim, token_count):
    rows, width = rows_in.shape
    padded_tokens = keys.shape[0]
    group_width = per_kv * head_dim
    kernel = functools.partial(
        attend_kernel, per_kv=per_kv, head_dim=head_dim, token_count=token_count
    )
    flops = 4 * rows * padded_tokens * head_dim * per_kv * kv_count
    moved = 2 * (2 * rows * width + 2 * padded_tokens * head_dim * kv_count)
    return pl.pallas_call(
        kernel,
        grid=(kv_count,),
        in_specs=[
            pl.BlockSpec((rows, group_width), lambda k: (0, k)),
            pl.BlockSpec((padded_tokens, head_dim), lambda k: (0, k)),
            pl.BlockSpec((padded_tokens, head_dim), lambda k: (0, k)),
        ],
        out_specs=pl.BlockSpec((rows, group_width), lambda k: (0, k)),
        out_shape=jax.ShapeDtypeStruct((rows, width), jnp.bfloat16),
        cost_estimate=pl.CostEstimate(
            flops=flops,
            transcendentals=rows * padded_tokens * per_kv * kv_count,
            bytes_accessed=moved,
        ),
    )(rows_in, keys, values)


def local(
    hidden_in,
    q_weight,
    q_gain,
    key_cache,
    value_cache,
    out_weight,
    req_image,
    image_count,
    image_home,
):
    req_count = lax.axis_size("req")
    local_rows = hidden_in.shape[0]
    q_cols = q_weight.shape[1]
    head_dim = q_gain.shape[0]
    group_size = HQ // KVH
    heads_here = q_cols // head_dim
    sub_count = lax.axis_size("sub")
    sub_index = lax.axis_index("sub")
    block_width = hidden_in.shape[1] // req_count
    part_width = block_width // sub_count
    by_block = hidden_in.reshape(local_rows, req_count, sub_count, part_width)
    my_part = lax.dynamic_index_in_dim(by_block, sub_index, axis=2, keepdims=False)
    spread_part = lax.all_to_all(my_part, "req", split_axis=1, concat_axis=0, tiled=True)
    spread_part = spread_part.reshape(req_count * local_rows, part_width)
    spread_cols = jnp.zeros((req_count * local_rows, block_width), spread_part.dtype)
    spread_cols = lax.dynamic_update_slice_in_dim(
        spread_cols, spread_part, sub_index * part_width, 1
    )
    for shift in range(1, sub_count):
        other_part = lax.ppermute(
            spread_part, "sub", [(i, (i + shift) % sub_count) for i in range(sub_count)]
        )
        spread_cols = lax.dynamic_update_slice_in_dim(
            spread_cols, other_part, ((sub_index - shift) % sub_count) * part_width, 1
        )
    query_sum = lax.psum_scatter(
        jnp.dot(spread_cols, q_weight, preferred_element_type=jnp.float32).astype(jnp.bfloat16),
        "req",
        scatter_dimension=0,
        tiled=True,
    )
    queries = lax.optimization_barrier(query_sum)
    normalized = normalize_heads(queries, q_gain, head_dim)
    capacity = 2 * local_rows // req_count
    slot_total = req_count * capacity
    table_ids = lax.broadcasted_iota(jnp.int32, (local_rows, image_home.shape[0]), 1)
    home_rows = jnp.sum(jnp.where(req_image[:, None] == table_ids, image_home[None, :], 0), axis=1)
    wanted = image_count == 1
    dest_ids = lax.broadcasted_iota(jnp.int32, (local_rows, req_count), 1)
    to_dest = ((home_rows[:, None] == dest_ids) & wanted[:, None]).astype(jnp.int32)
    earlier = jnp.cumsum(to_dest, axis=0) - to_dest
    position = home_rows * capacity + jnp.sum(earlier * to_dest, axis=1)
    slot_ids = lax.broadcasted_iota(jnp.int32, (slot_total, local_rows), 0)
    dispatch = ((slot_ids == position[None, :]) & wanted[None, :]).astype(jnp.bfloat16)
    outgoing = jnp.dot(dispatch, normalized, preferred_element_type=jnp.float32).astype(
        jnp.bfloat16
    )
    outgoing = outgoing.reshape(req_count, capacity, q_cols)
    kv_count = max(1, heads_here // group_size)
    per_kv = heads_here // kv_count
    kv_first = sub_index * heads_here // group_size
    token_count = key_cache.shape[1]
    padded_tokens = -(-token_count // 128) * 128
    keys_here = jnp.pad(
        lax.dynamic_slice_in_dim(key_cache[0], kv_first * head_dim, kv_count * head_dim, 1),
        ((0, padded_tokens - token_count), (0, 0)),
    )
    values_here = jnp.pad(
        lax.dynamic_slice_in_dim(value_cache[0], kv_first * head_dim, kv_count * head_dim, 1),
        ((0, padded_tokens - token_count), (0, 0)),
    )
    arrived = lax.all_to_all(outgoing, "req", split_axis=0, concat_axis=0, tiled=True)
    sources = arrived.shape[0]
    slot_count = arrived.shape[1]
    flat_rows = arrived.reshape(sources * slot_count, q_cols)
    mixed_heads = attend(flat_rows, keys_here, values_here, kv_count, per_kv, head_dim, token_count)
    replies = mixed_heads.reshape(sources, slot_count, q_cols)
    returned = lax.all_to_all(replies, "req", split_axis=0, concat_axis=0, tiled=True)
    attended = lax.dot_general(
        dispatch,
        returned.reshape(slot_total, q_cols),
        (((0,), (0,)), ((), ())),
        preferred_element_type=jnp.float32,
    ).astype(jnp.bfloat16)
    partial_cols = jnp.dot(
        lax.all_gather(attended, "req", axis=0, tiled=True),
        out_weight,
        preferred_element_type=jnp.float32,
    ).astype(jnp.bfloat16)
    hs_count = lax.axis_size("head") * sub_count
    hs_index = lax.axis_index("head") * sub_count + sub_index
    req_index = lax.axis_index("req")
    head_count = lax.axis_size("head")
    by_group = partial_cols.reshape(sub_count, -1, partial_cols.shape[1])
    owner_sums = exchange_sum(by_group, "sub", sub_count, sub_index)
    owner_sums = owner_sums.reshape(head_count, -1, partial_cols.shape[1])
    owner_sums = exchange_sum(owner_sums, "head", head_count, lax.axis_index("head"))
    per_hs = req_count // hs_count
    out_block = partial_cols.shape[1]
    owner_sums = owner_sums.reshape(per_hs, local_rows, out_block)
    arrived_blocks = []
    for step in range(per_hs):
        chunk = lax.dynamic_index_in_dim(
            owner_sums, (req_index + step) % per_hs, axis=0, keepdims=False
        )
        pairs = []
        for c in range(req_count):
            for h in range(head_count):
                for u in range(sub_count):
                    j = u * head_count + h
                    k = j * per_hs + (c + step) % per_hs
                    src = c * hs_count + h * sub_count + u
                    pairs.append((src, k * hs_count + c // per_hs))
        arrived_blocks.append(lax.ppermute(chunk, ("req", "head", "sub"), pairs))
    stacked = jnp.stack(arrived_blocks)
    order = (req_index % per_hs - jnp.arange(per_hs)) % per_hs
    head_total = jnp.take(stacked, order, axis=0)
    head_total = jnp.transpose(head_total, (1, 0, 2)).reshape(local_rows, per_hs * out_block)
    head_total = head_total.astype(jnp.float32)
    out_width = head_total.shape[1]
    residual = lax.dynamic_slice_in_dim(hidden_in, hs_index * out_width, out_width, 1)
    return (residual.astype(jnp.float32) + head_total).astype(jnp.bfloat16)


def solution(mesh):
    in_specs = (
        P(("groups", "req"), None),
        P("req", ("head", "sub")),
        P(),
        P(("groups", "req"), None, "head"),
        P(("groups", "req"), None, "head"),
        P(("head", "sub"), "req"),
        P(("groups", "req")),
        P(("groups", "req")),
        P("groups"),
    )
    out_specs = P(("groups", "req"), ("head", "sub"))
    return jax.shard_map(local, mesh=mesh, in_specs=in_specs, out_specs=out_specs, check_vma=False)
```

```python
import functools

import jax
import jax.numpy as jnp
from jax import lax
from jax.sharding import PartitionSpec as P
from jax.experimental import pallas as pl

HQ = 64
KVH = 8


def normalize_heads(queries, q_gain, head_dim):
    row_count = queries.shape[0]
    per_head = queries.astype(jnp.float32).reshape(row_count, -1, head_dim)
    inv_rms = lax.rsqrt(jnp.mean(per_head * per_head, axis=2, keepdims=True) + 1e-05)
    return (per_head * inv_rms * q_gain).reshape(row_count, -1).astype(jnp.bfloat16)


def exchange_sum(parts, axis, count, index):
    total = lax.dynamic_index_in_dim(parts, index, axis=0, keepdims=False).astype(jnp.float32)
    for shift in range(1, count):
        outgoing = lax.dynamic_index_in_dim(parts, (index + shift) % count, axis=0, keepdims=False)
        incoming = lax.ppermute(outgoing, axis, [(i, (i + shift) % count) for i in range(count)])
        total = total + incoming.astype(jnp.float32)
    return total.astype(jnp.bfloat16)


def attend_kernel(q_ref, k_ref, v_ref, o_ref, *, per_kv, head_dim, token_count):
    padded_tokens = k_ref.shape[0]
    split = (token_count // 128) * 128
    keys = k_ref[...]
    rows = q_ref.shape[0]
    score_scale = head_dim ** (-0.5)
    for g in range(per_kv):
        query = q_ref[:, g * head_dim:(g + 1) * head_dim]
        scores = lax.dot_general(
            query, keys, (((1,), (1,)), ((), ())), preferred_element_type=jnp.float32
        ) * score_scale
        pieces = [scores[:, :split]] if split else []
        if split < padded_tokens:
            tail = scores[:, split:]
            valid = lax.broadcasted_iota(jnp.int32, tail.shape, 1) < token_count - split
            pieces.append(jnp.where(valid, tail, -jnp.inf))
        peak = jnp.max(pieces[0], axis=1, keepdims=True)
        for piece in pieces[1:]:
            peak = jnp.maximum(peak, jnp.max(piece, axis=1, keepdims=True))
        weights = [jnp.exp(piece - peak) for piece in pieces]
        total = sum(jnp.sum(w, axis=1, keepdims=True) for w in weights)
        inverse = 1.0 / total
        mixed = None
        start = 0
        for w in weights:
            width = w.shape[1]
            probs = (w * inverse).astype(jnp.bfloat16)
            term = jnp.dot(
                probs, v_ref[start:start + width, :], preferred_element_type=jnp.float32
            )
            mixed = term if mixed is None else mixed + term
            start += width
        o_ref[:, g * head_dim:(g + 1) * head_dim] = mixed.astype(o_ref.dtype)


def attend(rows_in, keys, values, kv_count, per_kv, head_dim, token_count):
    rows, width = rows_in.shape
    padded_tokens = keys.shape[0]
    group_width = per_kv * head_dim
    kernel = functools.partial(
        attend_kernel, per_kv=per_kv, head_dim=head_dim, token_count=token_count
    )
    flops = 4 * rows * padded_tokens * head_dim * per_kv * kv_count
    moved = 2 * (2 * rows * width + 2 * padded_tokens * head_dim * kv_count)
    return pl.pallas_call(
        kernel,
        grid=(kv_count,),
        in_specs=[
            pl.BlockSpec((rows, group_width), lambda k: (0, k)),
            pl.BlockSpec((padded_tokens, head_dim), lambda k: (0, k)),
            pl.BlockSpec((padded_tokens, head_dim), lambda k: (0, k)),
        ],
        out_specs=pl.BlockSpec((rows, group_width), lambda k: (0, k)),
        out_shape=jax.ShapeDtypeStruct((rows, width), jnp.bfloat16),
        cost_estimate=pl.CostEstimate(
            flops=flops,
            transcendentals=rows * padded_tokens * per_kv * kv_count,
            bytes_accessed=moved,
        ),
    )(rows_in, keys, values)


def local(
    hidden_in,
    q_weight,
    q_gain,
    key_cache,
    value_cache,
    out_weight,
    req_image,
    image_count,
    image_home,
):
    req_count = lax.axis_size("req")
    local_rows = hidden_in.shape[0]
    q_cols = q_weight.shape[1]
    head_dim = q_gain.shape[0]
    group_size = HQ // KVH
    heads_here = q_cols // head_dim
    sub_count = lax.axis_size("sub")
    sub_index = lax.axis_index("sub")
    block_width = hidden_in.shape[1] // req_count
    part_width = block_width // sub_count
    by_block = hidden_in.reshape(local_rows, req_count, sub_count, part_width)
    my_part = lax.dynamic_index_in_dim(by_block, sub_index, axis=2, keepdims=False)
    spread_part = lax.all_to_all(my_part, "req", split_axis=1, concat_axis=0, tiled=True)
    spread_part = spread_part.reshape(req_count * local_rows, part_width)
    spread_cols = jnp.zeros((req_count * local_rows, block_width), spread_part.dtype)
    spread_cols = lax.dynamic_update_slice_in_dim(
        spread_cols, spread_part, sub_index * part_width, 1
    )
    for shift in range(1, sub_count):
        other_part = lax.ppermute(
            spread_part, "sub", [(i, (i + shift) % sub_count) for i in range(sub_count)]
        )
        spread_cols = lax.dynamic_update_slice_in_dim(
            spread_cols, other_part, ((sub_index - shift) % sub_count) * part_width, 1
        )
    query_sum = lax.psum_scatter(
        jnp.dot(spread_cols, q_weight, preferred_element_type=jnp.float32).astype(jnp.bfloat16),
        "req",
        scatter_dimension=0,
        tiled=True,
    )
    queries = lax.optimization_barrier(query_sum)
    normalized = normalize_heads(queries, q_gain, head_dim)
    capacity = 2 * local_rows // req_count
    slot_total = req_count * capacity
    table_ids = lax.broadcasted_iota(jnp.int32, (local_rows, image_home.shape[0]), 1)
    home_rows = jnp.sum(jnp.where(req_image[:, None] == table_ids, image_home[None, :], 0), axis=1)
    wanted = image_count == 1
    dest_ids = lax.broadcasted_iota(jnp.int32, (local_rows, req_count), 1)
    to_dest = ((home_rows[:, None] == dest_ids) & wanted[:, None]).astype(jnp.int32)
    earlier = jnp.cumsum(to_dest, axis=0) - to_dest
    position = home_rows * capacity + jnp.sum(earlier * to_dest, axis=1)
    slot_ids = lax.broadcasted_iota(jnp.int32, (slot_total, local_rows), 0)
    dispatch = ((slot_ids == position[None, :]) & wanted[None, :]).astype(jnp.bfloat16)
    outgoing = jnp.dot(dispatch, normalized, preferred_element_type=jnp.float32).astype(
        jnp.bfloat16
    )
    outgoing = outgoing.reshape(req_count, capacity, q_cols)
    kv_count = max(1, heads_here // group_size)
    per_kv = heads_here // kv_count
    kv_first = sub_index * heads_here // group_size
    token_count = key_cache.shape[1]
    padded_tokens = -(-token_count // 128) * 128
    keys_here = jnp.pad(
        lax.dynamic_slice_in_dim(key_cache[0], kv_first * head_dim, kv_count * head_dim, 1),
        ((0, padded_tokens - token_count), (0, 0)),
    )
    values_here = jnp.pad(
        lax.dynamic_slice_in_dim(value_cache[0], kv_first * head_dim, kv_count * head_dim, 1),
        ((0, padded_tokens - token_count), (0, 0)),
    )
    arrived = lax.all_to_all(outgoing, "req", split_axis=0, concat_axis=0, tiled=True)
    sources = arrived.shape[0]
    slot_count = arrived.shape[1]
    flat_rows = arrived.reshape(sources * slot_count, q_cols)
    mixed_heads = attend(flat_rows, keys_here, values_here, kv_count, per_kv, head_dim, token_count)
    replies = mixed_heads.reshape(sources, slot_count, q_cols)
    returned = lax.all_to_all(replies, "req", split_axis=0, concat_axis=0, tiled=True)
    attended = lax.dot_general(
        dispatch,
        returned.reshape(slot_total, q_cols),
        (((0,), (0,)), ((), ())),
        preferred_element_type=jnp.float32,
    ).astype(jnp.bfloat16)
    partial_cols = jnp.dot(
        lax.all_gather(attended, "req", axis=0, tiled=True),
        out_weight,
        preferred_element_type=jnp.float32,
    ).astype(jnp.bfloat16)
    hs_count = lax.axis_size("head") * sub_count
    hs_index = lax.axis_index("head") * sub_count + sub_index
    req_index = lax.axis_index("req")
    head_count = lax.axis_size("head")
    by_group = partial_cols.reshape(sub_count, -1, partial_cols.shape[1])
    owner_sums = exchange_sum(by_group, "sub", sub_count, sub_index)
    owner_sums = owner_sums.reshape(head_count, -1, partial_cols.shape[1])
    owner_sums = exchange_sum(owner_sums, "head", head_count, lax.axis_index("head"))
    per_hs = req_count // hs_count
    out_block = partial_cols.shape[1]
    owner_sums = owner_sums.reshape(per_hs, local_rows, out_block)
    arrived_blocks = []
    for step in range(per_hs):
        chunk = lax.dynamic_index_in_dim(
            owner_sums, (req_index + step) % per_hs, axis=0, keepdims=False
        )
        pairs = []
        for c in range(req_count):
            for h in range(head_count):
                for u in range(sub_count):
                    j = u * head_count + h
                    k = j * per_hs + (c + step) % per_hs
                    src = c * hs_count + h * sub_count + u
                    pairs.append((src, k * hs_count + c // per_hs))
        arrived_blocks.append(lax.ppermute(chunk, ("req", "head", "sub"), pairs))
    stacked = jnp.stack(arrived_blocks)
    order = (req_index % per_hs - jnp.arange(per_hs)) % per_hs
    head_total = jnp.take(stacked, order, axis=0)
    head_total = jnp.transpose(head_total, (1, 0, 2)).reshape(local_rows, per_hs * out_block)
    head_total = head_total.astype(jnp.float32)
    out_width = head_total.shape[1]
    residual = lax.dynamic_slice_in_dim(hidden_in, hs_index * out_width, out_width, 1)
    return (residual.astype(jnp.float32) + head_total).astype(jnp.bfloat16)


def solution(mesh):
    in_specs = (
        P(("groups", "req"), None),
        P("req", ("head", "sub")),
        P(),
        P(("groups", "req"), None, "head"),
        P(("groups", "req"), None, "head"),
        P(("head", "sub"), "req"),
        P(("groups", "req")),
        P(("groups", "req")),
        P("groups"),
    )
    out_specs = P(("groups", "req"), ("head", "sub"))
    return jax.shard_map(local, mesh=mesh, in_specs=in_specs, out_specs=out_specs, check_vma=False)
```

```python
import functools

import jax
import jax.numpy as jnp
from jax import lax
from jax.sharding import PartitionSpec as P
from jax.experimental import pallas as pl

HQ = 64
KVH = 8


def normalize_heads(queries, q_gain, head_dim):
    row_count = queries.shape[0]
    per_head = queries.astype(jnp.float32).reshape(row_count, -1, head_dim)
    inv_rms = lax.rsqrt(jnp.mean(per_head * per_head, axis=2, keepdims=True) + 1e-05)
    return (per_head * inv_rms * q_gain).reshape(row_count, -1).astype(jnp.bfloat16)


def exchange_sum(parts, axis, count, index):
    total = lax.dynamic_index_in_dim(parts, index, axis=0, keepdims=False).astype(jnp.float32)
    for shift in range(1, count):
        outgoing = lax.dynamic_index_in_dim(parts, (index + shift) % count, axis=0, keepdims=False)
        incoming = lax.ppermute(outgoing, axis, [(i, (i + shift) % count) for i in range(count)])
        total = total + incoming.astype(jnp.float32)
    return total.astype(jnp.bfloat16)


def attend_kernel(q_ref, k_ref, v_ref, o_ref, *, per_kv, head_dim, token_count):
    padded_tokens = k_ref.shape[1]
    split = (token_count // 128) * 128
    keys = k_ref[...]
    rows = q_ref.shape[0]
    score_scale = head_dim ** (-0.5)
    for g in range(per_kv):
        query = q_ref[:, g * head_dim:(g + 1) * head_dim]
        scores = jnp.dot(query, keys, preferred_element_type=jnp.float32) * score_scale
        pieces = [scores[:, :split]] if split else []
        if split < padded_tokens:
            tail = scores[:, split:]
            valid = lax.broadcasted_iota(jnp.int32, tail.shape, 1) < token_count - split
            pieces.append(jnp.where(valid, tail, -jnp.inf))
        peak = jnp.max(pieces[0], axis=1, keepdims=True)
        for piece in pieces[1:]:
            peak = jnp.maximum(peak, jnp.max(piece, axis=1, keepdims=True))
        weights = [jnp.exp(piece - peak) for piece in pieces]
        total = sum(jnp.sum(w, axis=1, keepdims=True) for w in weights)
        inverse = 1.0 / total
        mixed = None
        start = 0
        for w in weights:
            width = w.shape[1]
            probs = (w * inverse).astype(jnp.bfloat16)
            term = jnp.dot(
                probs, v_ref[start:start + width, :], preferred_element_type=jnp.float32
            )
            mixed = term if mixed is None else mixed + term
            start += width
        o_ref[:, g * head_dim:(g + 1) * head_dim] = mixed.astype(o_ref.dtype)


def attend(rows_in, keys, values, kv_count, per_kv, head_dim, token_count):
    rows, width = rows_in.shape
    padded_tokens = keys.shape[1]
    group_width = per_kv * head_dim
    kernel = functools.partial(
        attend_kernel, per_kv=per_kv, head_dim=head_dim, token_count=token_count
    )
    flops = 4 * rows * padded_tokens * head_dim * per_kv * kv_count
    moved = 2 * (2 * rows * width + 2 * padded_tokens * head_dim * kv_count)
    return pl.pallas_call(
        kernel,
        grid=(kv_count,),
        in_specs=[
            pl.BlockSpec((rows, group_width), lambda k: (0, k)),
            pl.BlockSpec((head_dim, padded_tokens), lambda k: (k, 0)),
            pl.BlockSpec((padded_tokens, head_dim), lambda k: (0, k)),
        ],
        out_specs=pl.BlockSpec((rows, group_width), lambda k: (0, k)),
        out_shape=jax.ShapeDtypeStruct((rows, width), jnp.bfloat16),
        cost_estimate=pl.CostEstimate(
            flops=flops,
            transcendentals=rows * padded_tokens * per_kv * kv_count,
            bytes_accessed=moved,
        ),
    )(rows_in, keys, values)


def local(
    hidden_in,
    q_weight,
    q_gain,
    key_cache,
    value_cache,
    out_weight,
    req_image,
    image_count,
    image_home,
):
    req_count = lax.axis_size("req")
    local_rows = hidden_in.shape[0]
    q_cols = q_weight.shape[1]
    head_dim = q_gain.shape[0]
    group_size = HQ // KVH
    heads_here = q_cols // head_dim
    sub_count = lax.axis_size("sub")
    sub_index = lax.axis_index("sub")
    block_width = hidden_in.shape[1] // req_count
    part_width = block_width // sub_count
    by_block = hidden_in.reshape(local_rows, req_count, sub_count, part_width)
    my_part = lax.dynamic_index_in_dim(by_block, sub_index, axis=2, keepdims=False)
    spread_part = lax.all_to_all(my_part, "req", split_axis=1, concat_axis=0, tiled=True)
    spread_part = spread_part.reshape(req_count * local_rows, part_width)
    spread_cols = jnp.zeros((req_count * local_rows, block_width), spread_part.dtype)
    spread_cols = lax.dynamic_update_slice_in_dim(
        spread_cols, spread_part, sub_index * part_width, 1
    )
    for shift in range(1, sub_count):
        other_part = lax.ppermute(
            spread_part, "sub", [(i, (i + shift) % sub_count) for i in range(sub_count)]
        )
        spread_cols = lax.dynamic_update_slice_in_dim(
            spread_cols, other_part, ((sub_index - shift) % sub_count) * part_width, 1
        )
    query_sum = lax.psum_scatter(
        jnp.dot(spread_cols, q_weight, preferred_element_type=jnp.float32).astype(jnp.bfloat16),
        "req",
        scatter_dimension=0,
        tiled=True,
    )
    queries = lax.optimization_barrier(query_sum)
    normalized = normalize_heads(queries, q_gain, head_dim)
    capacity = 2 * local_rows // req_count
    slot_total = req_count * capacity
    table_ids = lax.broadcasted_iota(jnp.int32, (local_rows, image_home.shape[0]), 1)
    home_rows = jnp.sum(jnp.where(req_image[:, None] == table_ids, image_home[None, :], 0), axis=1)
    wanted = image_count == 1
    dest_ids = lax.broadcasted_iota(jnp.int32, (local_rows, req_count), 1)
    to_dest = ((home_rows[:, None] == dest_ids) & wanted[:, None]).astype(jnp.int32)
    earlier = jnp.cumsum(to_dest, axis=0) - to_dest
    position = home_rows * capacity + jnp.sum(earlier * to_dest, axis=1)
    slot_ids = lax.broadcasted_iota(jnp.int32, (slot_total, local_rows), 0)
    dispatch = ((slot_ids == position[None, :]) & wanted[None, :]).astype(jnp.bfloat16)
    outgoing = jnp.dot(dispatch, normalized, preferred_element_type=jnp.float32).astype(
        jnp.bfloat16
    )
    outgoing = outgoing.reshape(req_count, capacity, q_cols)
    kv_count = max(1, heads_here // group_size)
    per_kv = heads_here // kv_count
    kv_first = sub_index * heads_here // group_size
    token_count = key_cache.shape[1]
    padded_tokens = -(-token_count // 128) * 128
    keys_here = jnp.pad(
        lax.dynamic_slice_in_dim(key_cache[0], kv_first * head_dim, kv_count * head_dim, 1),
        ((0, padded_tokens - token_count), (0, 0)),
    )
    values_here = jnp.pad(
        lax.dynamic_slice_in_dim(value_cache[0], kv_first * head_dim, kv_count * head_dim, 1),
        ((0, padded_tokens - token_count), (0, 0)),
    )
    arrived = lax.all_to_all(outgoing, "req", split_axis=0, concat_axis=0, tiled=True)
    sources = arrived.shape[0]
    slot_count = arrived.shape[1]
    flat_rows = arrived.reshape(sources * slot_count, q_cols)
    mixed_heads = attend(flat_rows, keys_here.T, values_here, kv_count, per_kv, head_dim, token_count)
    replies = mixed_heads.reshape(sources, slot_count, q_cols)
    returned = lax.all_to_all(replies, "req", split_axis=0, concat_axis=0, tiled=True)
    attended = lax.dot_general(
        dispatch,
        returned.reshape(slot_total, q_cols),
        (((0,), (0,)), ((), ())),
        preferred_element_type=jnp.float32,
    ).astype(jnp.bfloat16)
    partial_cols = jnp.dot(
        lax.all_gather(attended, "req", axis=0, tiled=True),
        out_weight,
        preferred_element_type=jnp.float32,
    ).astype(jnp.bfloat16)
    hs_count = lax.axis_size("head") * sub_count
    hs_index = lax.axis_index("head") * sub_count + sub_index
    req_index = lax.axis_index("req")
    head_count = lax.axis_size("head")
    by_group = partial_cols.reshape(sub_count, -1, partial_cols.shape[1])
    owner_sums = exchange_sum(by_group, "sub", sub_count, sub_index)
    owner_sums = owner_sums.reshape(head_count, -1, partial_cols.shape[1])
    owner_sums = exchange_sum(owner_sums, "head", head_count, lax.axis_index("head"))
    per_hs = req_count // hs_count
    out_block = partial_cols.shape[1]
    owner_sums = owner_sums.reshape(per_hs, local_rows, out_block)
    arrived_blocks = []
    for step in range(per_hs):
        chunk = lax.dynamic_index_in_dim(
            owner_sums, (req_index + step) % per_hs, axis=0, keepdims=False
        )
        pairs = []
        for c in range(req_count):
            for h in range(head_count):
                for u in range(sub_count):
                    j = u * head_count + h
                    k = j * per_hs + (c + step) % per_hs
                    src = c * hs_count + h * sub_count + u
                    pairs.append((src, k * hs_count + c // per_hs))
        arrived_blocks.append(lax.ppermute(chunk, ("req", "head", "sub"), pairs))
    stacked = jnp.stack(arrived_blocks)
    order = (req_index % per_hs - jnp.arange(per_hs)) % per_hs
    head_total = jnp.take(stacked, order, axis=0)
    head_total = jnp.transpose(head_total, (1, 0, 2)).reshape(local_rows, per_hs * out_block)
    head_total = head_total.astype(jnp.float32)
    out_width = head_total.shape[1]
    residual = lax.dynamic_slice_in_dim(hidden_in, hs_index * out_width, out_width, 1)
    return (residual.astype(jnp.float32) + head_total).astype(jnp.bfloat16)


def solution(mesh):
    in_specs = (
        P(("groups", "req"), None),
        P("req", ("head", "sub")),
        P(),
        P(("groups", "req"), None, "head"),
        P(("groups", "req"), None, "head"),
        P(("head", "sub"), "req"),
        P(("groups", "req")),
        P(("groups", "req")),
        P("groups"),
    )
    out_specs = P(("groups", "req"), ("head", "sub"))
    return jax.shard_map(local, mesh=mesh, in_specs=in_specs, out_specs=out_specs, check_vma=False)
```

```python
import functools

import jax
import jax.numpy as jnp
from jax import lax
from jax.sharding import PartitionSpec as P
from jax.experimental import pallas as pl

HQ = 64
KVH = 8


def normalize_heads(queries, q_gain, head_dim):
    row_count = queries.shape[0]
    per_head = queries.astype(jnp.float32).reshape(row_count, -1, head_dim)
    inv_rms = lax.rsqrt(jnp.mean(per_head * per_head, axis=2, keepdims=True) + 1e-05)
    return (per_head * inv_rms * q_gain).reshape(row_count, -1).astype(jnp.bfloat16)


def shift_exchange(blocks, axis, count):
    arrived = [blocks[0]]
    for shift in range(1, count):
        arrived.append(
            lax.ppermute(blocks[shift], axis, [(i, (i + shift) % count) for i in range(count)])
        )
    return jnp.stack(arrived)


def exchange_sum(parts, axis, count, index):
    total = lax.dynamic_index_in_dim(parts, index, axis=0, keepdims=False).astype(jnp.float32)
    for shift in range(1, count):
        outgoing = lax.dynamic_index_in_dim(parts, (index + shift) % count, axis=0, keepdims=False)
        incoming = lax.ppermute(outgoing, axis, [(i, (i + shift) % count) for i in range(count)])
        total = total + incoming.astype(jnp.float32)
    return total.astype(jnp.bfloat16)


def attend_kernel(q_ref, k_ref, v_ref, o_ref, *, per_kv, head_dim, token_count):
    padded_tokens = k_ref.shape[0]
    split = (token_count // 128) * 128
    keys = k_ref[...]
    rows = q_ref.shape[0]
    score_scale = head_dim ** (-0.5)
    for g in range(per_kv):
        query = q_ref[:, g * head_dim:(g + 1) * head_dim]
        scores = lax.dot_general(
            query, keys, (((1,), (1,)), ((), ())), preferred_element_type=jnp.float32
        ) * score_scale
        pieces = [scores[:, :split]] if split else []
        if split < padded_tokens:
            tail = scores[:, split:]
            valid = lax.broadcasted_iota(jnp.int32, tail.shape, 1) < token_count - split
            pieces.append(jnp.where(valid, tail, -jnp.inf))
        peak = jnp.max(pieces[0], axis=1, keepdims=True)
        for piece in pieces[1:]:
            peak = jnp.maximum(peak, jnp.max(piece, axis=1, keepdims=True))
        weights = [jnp.exp(piece - peak) for piece in pieces]
        total = sum(jnp.sum(w, axis=1, keepdims=True) for w in weights)
        inverse = 1.0 / total
        mixed = None
        start = 0
        for w in weights:
            width = w.shape[1]
            probs = (w * inverse).astype(jnp.bfloat16)
            term = jnp.dot(
                probs, v_ref[start:start + width, :], preferred_element_type=jnp.float32
            )
            mixed = term if mixed is None else mixed + term
            start += width
        o_ref[:, g * head_dim:(g + 1) * head_dim] = mixed.astype(o_ref.dtype)


def attend(rows_in, keys, values, kv_count, per_kv, head_dim, token_count):
    rows, width = rows_in.shape
    padded_tokens = keys.shape[0]
    group_width = per_kv * head_dim
    kernel = functools.partial(
        attend_kernel, per_kv=per_kv, head_dim=head_dim, token_count=token_count
    )
    flops = 4 * rows * padded_tokens * head_dim * per_kv * kv_count
    moved = 2 * (2 * rows * width + 2 * padded_tokens * head_dim * kv_count)
    return pl.pallas_call(
        kernel,
        grid=(kv_count,),
        in_specs=[
            pl.BlockSpec((rows, group_width), lambda k: (0, k)),
            pl.BlockSpec((padded_tokens, head_dim), lambda k: (0, k)),
            pl.BlockSpec((padded_tokens, head_dim), lambda k: (0, k)),
        ],
        out_specs=pl.BlockSpec((rows, group_width), lambda k: (0, k)),
        out_shape=jax.ShapeDtypeStruct((rows, width), jnp.bfloat16),
        cost_estimate=pl.CostEstimate(
            flops=flops,
            transcendentals=rows * padded_tokens * per_kv * kv_count,
            bytes_accessed=moved,
        ),
    )(rows_in, keys, values)


def local(
    hidden_in,
    q_weight,
    q_gain,
    key_cache,
    value_cache,
    out_weight,
    req_image,
    image_count,
    image_home,
):
    req_count = lax.axis_size("req")
    local_rows = hidden_in.shape[0]
    q_cols = q_weight.shape[1]
    head_dim = q_gain.shape[0]
    group_size = HQ // KVH
    heads_here = q_cols // head_dim
    sub_count = lax.axis_size("sub")
    sub_index = lax.axis_index("sub")
    block_width = hidden_in.shape[1] // req_count
    part_width = block_width // sub_count
    by_block = hidden_in.reshape(local_rows, req_count, sub_count, part_width)
    req_index = lax.axis_index("req")
    my_part = lax.dynamic_index_in_dim(by_block, sub_index, axis=2, keepdims=False)
    shift_order = (req_index + jnp.arange(req_count)) % req_count
    outgoing_parts = jnp.take(jnp.swapaxes(my_part, 0, 1), shift_order, axis=0)
    arrived_parts = shift_exchange(outgoing_parts, "req", req_count)
    source_order = (req_index - jnp.arange(req_count)) % req_count
    spread_part = jnp.take(arrived_parts, source_order, axis=0)
    spread_part = spread_part.reshape(req_count * local_rows, part_width)
    spread_cols = jnp.zeros((req_count * local_rows, block_width), spread_part.dtype)
    spread_cols = lax.dynamic_update_slice_in_dim(
        spread_cols, spread_part, sub_index * part_width, 1
    )
    for shift in range(1, sub_count):
        other_part = lax.ppermute(
            spread_part, "sub", [(i, (i + shift) % sub_count) for i in range(sub_count)]
        )
        spread_cols = lax.dynamic_update_slice_in_dim(
            spread_cols, other_part, ((sub_index - shift) % sub_count) * part_width, 1
        )
    query_sum = lax.psum_scatter(
        jnp.dot(spread_cols, q_weight, preferred_element_type=jnp.float32).astype(jnp.bfloat16),
        "req",
        scatter_dimension=0,
        tiled=True,
    )
    queries = lax.optimization_barrier(query_sum)
    normalized = normalize_heads(queries, q_gain, head_dim)
    capacity = 2 * local_rows // req_count
    slot_total = req_count * capacity
    table_ids = lax.broadcasted_iota(jnp.int32, (local_rows, image_home.shape[0]), 1)
    home_rows = jnp.sum(jnp.where(req_image[:, None] == table_ids, image_home[None, :], 0), axis=1)
    wanted = image_count == 1
    dest_ids = lax.broadcasted_iota(jnp.int32, (local_rows, req_count), 1)
    to_dest = ((home_rows[:, None] == dest_ids) & wanted[:, None]).astype(jnp.int32)
    earlier = jnp.cumsum(to_dest, axis=0) - to_dest
    position = ((home_rows - req_index) % req_count) * capacity + jnp.sum(
        earlier * to_dest, axis=1
    )
    slot_ids = lax.broadcasted_iota(jnp.int32, (slot_total, local_rows), 0)
    dispatch = ((slot_ids == position[None, :]) & wanted[None, :]).astype(jnp.bfloat16)
    outgoing = jnp.dot(dispatch, normalized, preferred_element_type=jnp.float32).astype(
        jnp.bfloat16
    )
    outgoing = outgoing.reshape(req_count, capacity, q_cols)
    kv_count = max(1, heads_here // group_size)
    per_kv = heads_here // kv_count
    kv_first = sub_index * heads_here // group_size
    token_count = key_cache.shape[1]
    padded_tokens = -(-token_count // 128) * 128
    keys_here = jnp.pad(
        lax.dynamic_slice_in_dim(key_cache[0], kv_first * head_dim, kv_count * head_dim, 1),
        ((0, padded_tokens - token_count), (0, 0)),
    )
    values_here = jnp.pad(
        lax.dynamic_slice_in_dim(value_cache[0], kv_first * head_dim, kv_count * head_dim, 1),
        ((0, padded_tokens - token_count), (0, 0)),
    )
    arrived = shift_exchange(outgoing, "req", req_count)
    sources = arrived.shape[0]
    slot_count = arrived.shape[1]
    flat_rows = arrived.reshape(sources * slot_count, q_cols)
    mixed_heads = attend(flat_rows, keys_here, values_here, kv_count, per_kv, head_dim, token_count)
    replies = mixed_heads.reshape(sources, slot_count, q_cols)
    returned = shift_exchange(
        jnp.concatenate([replies[:1], replies[1:][::-1]]), "req", req_count
    )
    returned = jnp.concatenate([returned[:1], returned[1:][::-1]])
    attended = lax.dot_general(
        dispatch,
        returned.reshape(slot_total, q_cols),
        (((0,), (0,)), ((), ())),
        preferred_element_type=jnp.float32,
    ).astype(jnp.bfloat16)
    partial_cols = jnp.dot(
        lax.all_gather(attended, "req", axis=0, tiled=True),
        out_weight,
        preferred_element_type=jnp.float32,
    ).astype(jnp.bfloat16)
    hs_count = lax.axis_size("head") * sub_count
    hs_index = lax.axis_index("head") * sub_count + sub_index
    head_count = lax.axis_size("head")
    by_group = partial_cols.reshape(sub_count, -1, partial_cols.shape[1])
    owner_sums = exchange_sum(by_group, "sub", sub_count, sub_index)
    owner_sums = owner_sums.reshape(head_count, -1, partial_cols.shape[1])
    owner_sums = exchange_sum(owner_sums, "head", head_count, lax.axis_index("head"))
    per_hs = req_count // hs_count
    out_block = partial_cols.shape[1]
    owner_sums = owner_sums.reshape(per_hs, local_rows, out_block)
    arrived_blocks = []
    for step in range(per_hs):
        chunk = lax.dynamic_index_in_dim(
            owner_sums, (req_index + step) % per_hs, axis=0, keepdims=False
        )
        pairs = []
        for c in range(req_count):
            for h in range(head_count):
                for u in range(sub_count):
                    j = u * head_count + h
                    k = j * per_hs + (c + step) % per_hs
                    src = c * hs_count + h * sub_count + u
                    pairs.append((src, k * hs_count + c // per_hs))
        arrived_blocks.append(lax.ppermute(chunk, ("req", "head", "sub"), pairs))
    stacked = jnp.stack(arrived_blocks)
    order = (req_index % per_hs - jnp.arange(per_hs)) % per_hs
    head_total = jnp.take(stacked, order, axis=0)
    head_total = jnp.transpose(head_total, (1, 0, 2)).reshape(local_rows, per_hs * out_block)
    head_total = head_total.astype(jnp.float32)
    out_width = head_total.shape[1]
    residual = lax.dynamic_slice_in_dim(hidden_in, hs_index * out_width, out_width, 1)
    return (residual.astype(jnp.float32) + head_total).astype(jnp.bfloat16)


def solution(mesh):
    in_specs = (
        P(("groups", "req"), None),
        P("req", ("head", "sub")),
        P(),
        P(("groups", "req"), None, "head"),
        P(("groups", "req"), None, "head"),
        P(("head", "sub"), "req"),
        P(("groups", "req")),
        P(("groups", "req")),
        P("groups"),
    )
    out_specs = P(("groups", "req"), ("head", "sub"))
    return jax.shard_map(local, mesh=mesh, in_specs=in_specs, out_specs=out_specs, check_vma=False)
```

```python
import functools

import jax
import jax.numpy as jnp
from jax import lax
from jax.sharding import PartitionSpec as P
from jax.experimental import pallas as pl

HQ = 64
KVH = 8


def normalize_heads(queries, q_gain, head_dim):
    row_count = queries.shape[0]
    per_head = queries.astype(jnp.float32).reshape(row_count, -1, head_dim)
    inv_rms = lax.rsqrt(jnp.mean(per_head * per_head, axis=2, keepdims=True) + 1e-05)
    return (per_head * inv_rms * q_gain).reshape(row_count, -1).astype(jnp.bfloat16)


def shift_exchange(blocks, axis, count):
    arrived = [blocks[0]]
    for shift in range(1, count):
        arrived.append(
            lax.ppermute(blocks[shift], axis, [(i, (i + shift) % count) for i in range(count)])
        )
    return jnp.stack(arrived)


def line_reduce_scatter(chunk_of, axis, count, index):
    right = None
    left = None
    for step in range(1, count):
        dest_r = jnp.minimum(count - step + index, count - 1)
        send_r = chunk_of(dest_r) if right is None else chunk_of(dest_r) + right
        right = lax.ppermute(
            send_r.astype(jnp.bfloat16), axis, [(i, i + 1) for i in range(step)]
        ).astype(jnp.float32)
        dest_l = jnp.maximum(index - (count - step), 0)
        send_l = chunk_of(dest_l) if left is None else chunk_of(dest_l) + left
        left = lax.ppermute(
            send_l.astype(jnp.bfloat16), axis, [(i, i - 1) for i in range(count - step, count)]
        ).astype(jnp.float32)
    total = chunk_of(index)
    if right is not None:
        total = total + right + left
    return total


def line_gather_apply(block, apply, axis, count, index):
    own = apply(block)
    from_left = [own]
    from_right = [own]
    carry_r = block
    carry_l = block
    for step in range(1, count):
        carry_r = lax.ppermute(carry_r, axis, [(i, i + 1) for i in range(step - 1, count - 1)])
        carry_l = lax.ppermute(carry_l, axis, [(i, i - 1) for i in range(1, count - step + 1)])
        from_left.append(apply(carry_r))
        from_right.append(apply(carry_l))
    origins = jnp.arange(count)
    lower = jnp.take(jnp.stack(from_left), jnp.clip(index - origins, 0, count - 1), axis=0)
    upper = jnp.take(jnp.stack(from_right), jnp.clip(origins - index, 0, count - 1), axis=0)
    pick = (origins <= index).reshape((count,) + (1,) * own.ndim)
    return jnp.where(pick, lower, upper)


def exchange_sum(parts, axis, count, index):
    total = lax.dynamic_index_in_dim(parts, index, axis=0, keepdims=False).astype(jnp.float32)
    for shift in range(1, count):
        outgoing = lax.dynamic_index_in_dim(parts, (index + shift) % count, axis=0, keepdims=False)
        incoming = lax.ppermute(outgoing, axis, [(i, (i + shift) % count) for i in range(count)])
        total = total + incoming.astype(jnp.float32)
    return total.astype(jnp.bfloat16)


def attend_kernel(q_ref, k_ref, v_ref, o_ref, *, per_kv, head_dim, token_count):
    padded_tokens = k_ref.shape[0]
    split = (token_count // 128) * 128
    keys = k_ref[...]
    rows = q_ref.shape[0]
    score_scale = head_dim ** (-0.5)
    for g in range(per_kv):
        query = q_ref[:, g * head_dim:(g + 1) * head_dim]
        scores = lax.dot_general(
            query, keys, (((1,), (1,)), ((), ())), preferred_element_type=jnp.float32
        ) * score_scale
        pieces = [scores[:, :split]] if split else []
        if split < padded_tokens:
            tail = scores[:, split:]
            valid = lax.broadcasted_iota(jnp.int32, tail.shape, 1) < token_count - split
            pieces.append(jnp.where(valid, tail, -jnp.inf))
        peak = jnp.max(pieces[0], axis=1, keepdims=True)
        for piece in pieces[1:]:
            peak = jnp.maximum(peak, jnp.max(piece, axis=1, keepdims=True))
        weights = [jnp.exp(piece - peak) for piece in pieces]
        total = sum(jnp.sum(w, axis=1, keepdims=True) for w in weights)
        inverse = 1.0 / total
        mixed = None
        start = 0
        for w in weights:
            width = w.shape[1]
            probs = (w * inverse).astype(jnp.bfloat16)
            term = jnp.dot(
                probs, v_ref[start:start + width, :], preferred_element_type=jnp.float32
            )
            mixed = term if mixed is None else mixed + term
            start += width
        o_ref[:, g * head_dim:(g + 1) * head_dim] = mixed.astype(o_ref.dtype)


def attend(rows_in, keys, values, kv_count, per_kv, head_dim, token_count):
    rows, width = rows_in.shape
    padded_tokens = keys.shape[0]
    group_width = per_kv * head_dim
    kernel = functools.partial(
        attend_kernel, per_kv=per_kv, head_dim=head_dim, token_count=token_count
    )
    flops = 4 * rows * padded_tokens * head_dim * per_kv * kv_count
    moved = 2 * (2 * rows * width + 2 * padded_tokens * head_dim * kv_count)
    return pl.pallas_call(
        kernel,
        grid=(kv_count,),
        in_specs=[
            pl.BlockSpec((rows, group_width), lambda k: (0, k)),
            pl.BlockSpec((padded_tokens, head_dim), lambda k: (0, k)),
            pl.BlockSpec((padded_tokens, head_dim), lambda k: (0, k)),
        ],
        out_specs=pl.BlockSpec((rows, group_width), lambda k: (0, k)),
        out_shape=jax.ShapeDtypeStruct((rows, width), jnp.bfloat16),
        cost_estimate=pl.CostEstimate(
            flops=flops,
            transcendentals=rows * padded_tokens * per_kv * kv_count,
            bytes_accessed=moved,
        ),
    )(rows_in, keys, values)


def local(
    hidden_in,
    q_weight,
    q_gain,
    key_cache,
    value_cache,
    out_weight,
    req_image,
    image_count,
    image_home,
):
    req_count = lax.axis_size("req")
    local_rows = hidden_in.shape[0]
    q_cols = q_weight.shape[1]
    head_dim = q_gain.shape[0]
    group_size = HQ // KVH
    heads_here = q_cols // head_dim
    sub_count = lax.axis_size("sub")
    sub_index = lax.axis_index("sub")
    block_width = hidden_in.shape[1] // req_count
    part_width = block_width // sub_count
    by_block = hidden_in.reshape(local_rows, req_count, sub_count, part_width)
    req_index = lax.axis_index("req")
    my_part = lax.dynamic_index_in_dim(by_block, sub_index, axis=2, keepdims=False)
    shift_order = (req_index + jnp.arange(req_count)) % req_count
    outgoing_parts = jnp.take(jnp.swapaxes(my_part, 0, 1), shift_order, axis=0)
    arrived_parts = shift_exchange(outgoing_parts, "req", req_count)
    source_order = (req_index - jnp.arange(req_count)) % req_count
    spread_part = jnp.take(arrived_parts, source_order, axis=0)
    spread_part = spread_part.reshape(req_count * local_rows, part_width)
    spread_cols = jnp.zeros((req_count * local_rows, block_width), spread_part.dtype)
    spread_cols = lax.dynamic_update_slice_in_dim(
        spread_cols, spread_part, sub_index * part_width, 1
    )
    for shift in range(1, sub_count):
        other_part = lax.ppermute(
            spread_part, "sub", [(i, (i + shift) % sub_count) for i in range(sub_count)]
        )
        spread_cols = lax.dynamic_update_slice_in_dim(
            spread_cols, other_part, ((sub_index - shift) % sub_count) * part_width, 1
        )
    def query_chunk(owner):
        rows = lax.dynamic_slice_in_dim(spread_cols, owner * local_rows, local_rows, 0)
        product = jnp.dot(rows, q_weight, preferred_element_type=jnp.float32)
        return product.astype(jnp.bfloat16).astype(jnp.float32)

    query_sum = line_reduce_scatter(query_chunk, "req", req_count, req_index)
    queries = lax.optimization_barrier(query_sum.astype(jnp.bfloat16))
    normalized = normalize_heads(queries, q_gain, head_dim)
    capacity = 2 * local_rows // req_count
    slot_total = req_count * capacity
    table_ids = lax.broadcasted_iota(jnp.int32, (local_rows, image_home.shape[0]), 1)
    home_rows = jnp.sum(jnp.where(req_image[:, None] == table_ids, image_home[None, :], 0), axis=1)
    wanted = image_count == 1
    dest_ids = lax.broadcasted_iota(jnp.int32, (local_rows, req_count), 1)
    to_dest = ((home_rows[:, None] == dest_ids) & wanted[:, None]).astype(jnp.int32)
    earlier = jnp.cumsum(to_dest, axis=0) - to_dest
    position = ((home_rows - req_index) % req_count) * capacity + jnp.sum(
        earlier * to_dest, axis=1
    )
    slot_ids = lax.broadcasted_iota(jnp.int32, (slot_total, local_rows), 0)
    dispatch = ((slot_ids == position[None, :]) & wanted[None, :]).astype(jnp.bfloat16)
    outgoing = jnp.dot(dispatch, normalized, preferred_element_type=jnp.float32).astype(
        jnp.bfloat16
    )
    outgoing = outgoing.reshape(req_count, capacity, q_cols)
    kv_count = max(1, heads_here // group_size)
    per_kv = heads_here // kv_count
    kv_first = sub_index * heads_here // group_size
    token_count = key_cache.shape[1]
    padded_tokens = -(-token_count // 128) * 128
    keys_here = jnp.pad(
        lax.dynamic_slice_in_dim(key_cache[0], kv_first * head_dim, kv_count * head_dim, 1),
        ((0, padded_tokens - token_count), (0, 0)),
    )
    values_here = jnp.pad(
        lax.dynamic_slice_in_dim(value_cache[0], kv_first * head_dim, kv_count * head_dim, 1),
        ((0, padded_tokens - token_count), (0, 0)),
    )
    arrived = shift_exchange(outgoing, "req", req_count)
    sources = arrived.shape[0]
    slot_count = arrived.shape[1]
    flat_rows = arrived.reshape(sources * slot_count, q_cols)
    mixed_heads = attend(flat_rows, keys_here, values_here, kv_count, per_kv, head_dim, token_count)
    replies = mixed_heads.reshape(sources, slot_count, q_cols)
    returned = shift_exchange(
        jnp.concatenate([replies[:1], replies[1:][::-1]]), "req", req_count
    )
    returned = jnp.concatenate([returned[:1], returned[1:][::-1]])
    attended = lax.dot_general(
        dispatch,
        returned.reshape(slot_total, q_cols),
        (((0,), (0,)), ((), ())),
        preferred_element_type=jnp.float32,
    ).astype(jnp.bfloat16)
    def out_part(rows):
        product = jnp.dot(rows, out_weight, preferred_element_type=jnp.float32)
        return product.astype(jnp.bfloat16)

    partial_cols = line_gather_apply(attended, out_part, "req", req_count, req_index)
    partial_cols = partial_cols.reshape(req_count * local_rows, out_weight.shape[1])
    hs_count = lax.axis_size("head") * sub_count
    hs_index = lax.axis_index("head") * sub_count + sub_index
    head_count = lax.axis_size("head")
    by_group = partial_cols.reshape(sub_count, -1, partial_cols.shape[1])
    owner_sums = exchange_sum(by_group, "sub", sub_count, sub_index)
    owner_sums = owner_sums.reshape(head_count, -1, partial_cols.shape[1])
    owner_sums = exchange_sum(owner_sums, "head", head_count, lax.axis_index("head"))
    per_hs = req_count // hs_count
    out_block = partial_cols.shape[1]
    owner_sums = owner_sums.reshape(per_hs, local_rows, out_block)
    arrived_blocks = []
    for step in range(per_hs):
        chunk = lax.dynamic_index_in_dim(
            owner_sums, (req_index + step) % per_hs, axis=0, keepdims=False
        )
        pairs = []
        for c in range(req_count):
            for h in range(head_count):
                for u in range(sub_count):
                    j = u * head_count + h
                    k = j * per_hs + (c + step) % per_hs
                    src = c * hs_count + h * sub_count + u
                    pairs.append((src, k * hs_count + c // per_hs))
        arrived_blocks.append(lax.ppermute(chunk, ("req", "head", "sub"), pairs))
    stacked = jnp.stack(arrived_blocks)
    order = (req_index % per_hs - jnp.arange(per_hs)) % per_hs
    head_total = jnp.take(stacked, order, axis=0)
    head_total = jnp.transpose(head_total, (1, 0, 2)).reshape(local_rows, per_hs * out_block)
    head_total = head_total.astype(jnp.float32)
    out_width = head_total.shape[1]
    residual = lax.dynamic_slice_in_dim(hidden_in, hs_index * out_width, out_width, 1)
    return (residual.astype(jnp.float32) + head_total).astype(jnp.bfloat16)


def solution(mesh):
    in_specs = (
        P(("groups", "req"), None),
        P("req", ("head", "sub")),
        P(),
        P(("groups", "req"), None, "head"),
        P(("groups", "req"), None, "head"),
        P(("head", "sub"), "req"),
        P(("groups", "req")),
        P(("groups", "req")),
        P("groups"),
    )
    out_specs = P(("groups", "req"), ("head", "sub"))
    return jax.shard_map(local, mesh=mesh, in_specs=in_specs, out_specs=out_specs, check_vma=False)
```

```python
import functools

import jax
import jax.numpy as jnp
from jax import lax
from jax.sharding import PartitionSpec as P
from jax.experimental import pallas as pl

HQ = 64
KVH = 8


def normalize_heads(queries, q_gain, head_dim):
    row_count = queries.shape[0]
    per_head = queries.astype(jnp.float32).reshape(row_count, -1, head_dim)
    inv_rms = lax.rsqrt(jnp.mean(per_head * per_head, axis=2, keepdims=True) + 1e-05)
    return (per_head * inv_rms * q_gain).reshape(row_count, -1).astype(jnp.bfloat16)


def shift_exchange(blocks, axis, count):
    arrived = [blocks[0]]
    for shift in range(1, count):
        arrived.append(
            lax.ppermute(blocks[shift], axis, [(i, (i + shift) % count) for i in range(count)])
        )
    return jnp.stack(arrived)


def line_reduce_scatter(chunk_of, axis, count, index):
    right = None
    left = None
    for step in range(1, count):
        dest_r = jnp.minimum(count - step + index, count - 1)
        send_r = chunk_of(dest_r) if right is None else chunk_of(dest_r) + right
        right = lax.ppermute(
            send_r.astype(jnp.bfloat16), axis, [(i, i + 1) for i in range(step)]
        ).astype(jnp.float32)
        dest_l = jnp.maximum(index - (count - step), 0)
        send_l = chunk_of(dest_l) if left is None else chunk_of(dest_l) + left
        left = lax.ppermute(
            send_l.astype(jnp.bfloat16), axis, [(i, i - 1) for i in range(count - step, count)]
        ).astype(jnp.float32)
    total = chunk_of(index)
    if right is not None:
        total = total + right + left
    return total


def line_gather_apply(block, apply, axis, count, index):
    own = apply(block)
    from_left = [own]
    from_right = [own]
    carry_r = block
    carry_l = block
    for step in range(1, count):
        carry_r = lax.ppermute(carry_r, axis, [(i, i + 1) for i in range(step - 1, count - 1)])
        carry_l = lax.ppermute(carry_l, axis, [(i, i - 1) for i in range(1, count - step + 1)])
        from_left.append(apply(carry_r))
        from_right.append(apply(carry_l))
    placed = jnp.zeros((count,) + own.shape, own.dtype)
    for step in range(count - 1, 0, -1):
        placed = lax.dynamic_update_index_in_dim(placed, from_left[step], index - step, 0)
    for step in range(count - 1, 0, -1):
        placed = lax.dynamic_update_index_in_dim(placed, from_right[step], index + step, 0)
    return lax.dynamic_update_index_in_dim(placed, own, index, 0)


def exchange_sum(parts, axis, count, index):
    total = lax.dynamic_index_in_dim(parts, index, axis=0, keepdims=False).astype(jnp.float32)
    for shift in range(1, count):
        outgoing = lax.dynamic_index_in_dim(parts, (index + shift) % count, axis=0, keepdims=False)
        incoming = lax.ppermute(outgoing, axis, [(i, (i + shift) % count) for i in range(count)])
        total = total + incoming.astype(jnp.float32)
    return total.astype(jnp.bfloat16)


def attend_kernel(q_ref, k_ref, v_ref, o_ref, *, per_kv, head_dim, token_count):
    padded_tokens = k_ref.shape[0]
    split = (token_count // 128) * 128
    keys = k_ref[...]
    rows = q_ref.shape[0]
    score_scale = head_dim ** (-0.5)
    for g in range(per_kv):
        query = q_ref[:, g * head_dim:(g + 1) * head_dim]
        scores = lax.dot_general(
            query, keys, (((1,), (1,)), ((), ())), preferred_element_type=jnp.float32
        ) * score_scale
        pieces = [scores[:, :split]] if split else []
        if split < padded_tokens:
            tail = scores[:, split:]
            valid = lax.broadcasted_iota(jnp.int32, tail.shape, 1) < token_count - split
            pieces.append(jnp.where(valid, tail, -jnp.inf))
        peak = jnp.max(pieces[0], axis=1, keepdims=True)
        for piece in pieces[1:]:
            peak = jnp.maximum(peak, jnp.max(piece, axis=1, keepdims=True))
        weights = [jnp.exp(piece - peak) for piece in pieces]
        total = sum(jnp.sum(w, axis=1, keepdims=True) for w in weights)
        inverse = 1.0 / total
        mixed = None
        start = 0
        for w in weights:
            width = w.shape[1]
            probs = (w * inverse).astype(jnp.bfloat16)
            term = jnp.dot(
                probs, v_ref[start:start + width, :], preferred_element_type=jnp.float32
            )
            mixed = term if mixed is None else mixed + term
            start += width
        o_ref[:, g * head_dim:(g + 1) * head_dim] = mixed.astype(o_ref.dtype)


def attend(rows_in, keys, values, kv_count, per_kv, head_dim, token_count):
    rows, width = rows_in.shape
    padded_tokens = keys.shape[0]
    group_width = per_kv * head_dim
    kernel = functools.partial(
        attend_kernel, per_kv=per_kv, head_dim=head_dim, token_count=token_count
    )
    flops = 4 * rows * padded_tokens * head_dim * per_kv * kv_count
    moved = 2 * (2 * rows * width + 2 * padded_tokens * head_dim * kv_count)
    return pl.pallas_call(
        kernel,
        grid=(kv_count,),
        in_specs=[
            pl.BlockSpec((rows, group_width), lambda k: (0, k)),
            pl.BlockSpec((padded_tokens, head_dim), lambda k: (0, k)),
            pl.BlockSpec((padded_tokens, head_dim), lambda k: (0, k)),
        ],
        out_specs=pl.BlockSpec((rows, group_width), lambda k: (0, k)),
        out_shape=jax.ShapeDtypeStruct((rows, width), jnp.bfloat16),
        cost_estimate=pl.CostEstimate(
            flops=flops,
            transcendentals=rows * padded_tokens * per_kv * kv_count,
            bytes_accessed=moved,
        ),
    )(rows_in, keys, values)


def local(
    hidden_in,
    q_weight,
    q_gain,
    key_cache,
    value_cache,
    out_weight,
    req_image,
    image_count,
    image_home,
):
    req_count = lax.axis_size("req")
    local_rows = hidden_in.shape[0]
    q_cols = q_weight.shape[1]
    head_dim = q_gain.shape[0]
    group_size = HQ // KVH
    heads_here = q_cols // head_dim
    sub_count = lax.axis_size("sub")
    sub_index = lax.axis_index("sub")
    block_width = hidden_in.shape[1] // req_count
    part_width = block_width // sub_count
    by_block = hidden_in.reshape(local_rows, req_count, sub_count, part_width)
    req_index = lax.axis_index("req")
    my_part = lax.dynamic_index_in_dim(by_block, sub_index, axis=2, keepdims=False)
    spread_part = jnp.zeros((req_count, local_rows, part_width), my_part.dtype)
    spread_part = lax.dynamic_update_index_in_dim(
        spread_part, lax.dynamic_index_in_dim(my_part, req_index, 1, keepdims=False), req_index, 0
    )
    for shift in range(1, req_count):
        outgoing_part = lax.dynamic_index_in_dim(
            my_part, (req_index + shift) % req_count, 1, keepdims=False
        )
        arrived_part = lax.ppermute(
            outgoing_part, "req", [(i, (i + shift) % req_count) for i in range(req_count)]
        )
        spread_part = lax.dynamic_update_index_in_dim(
            spread_part, arrived_part, (req_index - shift) % req_count, 0
        )
    spread_part = spread_part.reshape(req_count * local_rows, part_width)
    spread_cols = jnp.zeros((req_count * local_rows, block_width), spread_part.dtype)
    spread_cols = lax.dynamic_update_slice_in_dim(
        spread_cols, spread_part, sub_index * part_width, 1
    )
    for shift in range(1, sub_count):
        other_part = lax.ppermute(
            spread_part, "sub", [(i, (i + shift) % sub_count) for i in range(sub_count)]
        )
        spread_cols = lax.dynamic_update_slice_in_dim(
            spread_cols, other_part, ((sub_index - shift) % sub_count) * part_width, 1
        )
    def query_chunk(owner):
        rows = lax.dynamic_slice_in_dim(spread_cols, owner * local_rows, local_rows, 0)
        product = jnp.dot(rows, q_weight, preferred_element_type=jnp.float32)
        return product.astype(jnp.bfloat16).astype(jnp.float32)

    query_sum = line_reduce_scatter(query_chunk, "req", req_count, req_index)
    queries = lax.optimization_barrier(query_sum.astype(jnp.bfloat16))
    normalized = normalize_heads(queries, q_gain, head_dim)
    capacity = 2 * local_rows // req_count
    slot_total = req_count * capacity
    table_ids = lax.broadcasted_iota(jnp.int32, (local_rows, image_home.shape[0]), 1)
    home_rows = jnp.sum(jnp.where(req_image[:, None] == table_ids, image_home[None, :], 0), axis=1)
    wanted = image_count == 1
    dest_ids = lax.broadcasted_iota(jnp.int32, (local_rows, req_count), 1)
    to_dest = ((home_rows[:, None] == dest_ids) & wanted[:, None]).astype(jnp.int32)
    earlier = jnp.cumsum(to_dest, axis=0) - to_dest
    position = ((home_rows - req_index) % req_count) * capacity + jnp.sum(
        earlier * to_dest, axis=1
    )
    slot_ids = lax.broadcasted_iota(jnp.int32, (slot_total, local_rows), 0)
    dispatch = ((slot_ids == position[None, :]) & wanted[None, :]).astype(jnp.bfloat16)
    outgoing = jnp.dot(dispatch, normalized, preferred_element_type=jnp.float32).astype(
        jnp.bfloat16
    )
    outgoing = outgoing.reshape(req_count, capacity, q_cols)
    kv_count = max(1, heads_here // group_size)
    per_kv = heads_here // kv_count
    kv_first = sub_index * heads_here // group_size
    token_count = key_cache.shape[1]
    padded_tokens = -(-token_count // 128) * 128
    keys_here = jnp.pad(
        lax.dynamic_slice_in_dim(key_cache[0], kv_first * head_dim, kv_count * head_dim, 1),
        ((0, padded_tokens - token_count), (0, 0)),
    )
    values_here = jnp.pad(
        lax.dynamic_slice_in_dim(value_cache[0], kv_first * head_dim, kv_count * head_dim, 1),
        ((0, padded_tokens - token_count), (0, 0)),
    )
    arrived = shift_exchange(outgoing, "req", req_count)
    sources = arrived.shape[0]
    slot_count = arrived.shape[1]
    flat_rows = arrived.reshape(sources * slot_count, q_cols)
    mixed_heads = attend(flat_rows, keys_here, values_here, kv_count, per_kv, head_dim, token_count)
    replies = mixed_heads.reshape(sources, slot_count, q_cols)
    returned = shift_exchange(
        jnp.concatenate([replies[:1], replies[1:][::-1]]), "req", req_count
    )
    returned = jnp.concatenate([returned[:1], returned[1:][::-1]])
    attended = lax.dot_general(
        dispatch,
        returned.reshape(slot_total, q_cols),
        (((0,), (0,)), ((), ())),
        preferred_element_type=jnp.float32,
    ).astype(jnp.bfloat16)
    def out_part(rows):
        product = jnp.dot(rows, out_weight, preferred_element_type=jnp.float32)
        return product.astype(jnp.bfloat16)

    partial_cols = line_gather_apply(attended, out_part, "req", req_count, req_index)
    partial_cols = partial_cols.reshape(req_count * local_rows, out_weight.shape[1])
    hs_count = lax.axis_size("head") * sub_count
    hs_index = lax.axis_index("head") * sub_count + sub_index
    head_count = lax.axis_size("head")
    by_group = partial_cols.reshape(sub_count, -1, partial_cols.shape[1])
    owner_sums = exchange_sum(by_group, "sub", sub_count, sub_index)
    owner_sums = owner_sums.reshape(head_count, -1, partial_cols.shape[1])
    owner_sums = exchange_sum(owner_sums, "head", head_count, lax.axis_index("head"))
    per_hs = req_count // hs_count
    out_block = partial_cols.shape[1]
    owner_sums = owner_sums.reshape(per_hs, local_rows, out_block)
    arrived_blocks = []
    for step in range(per_hs):
        chunk = lax.dynamic_index_in_dim(
            owner_sums, (req_index + step) % per_hs, axis=0, keepdims=False
        )
        pairs = []
        for c in range(req_count):
            for h in range(head_count):
                for u in range(sub_count):
                    j = u * head_count + h
                    k = j * per_hs + (c + step) % per_hs
                    src = c * hs_count + h * sub_count + u
                    pairs.append((src, k * hs_count + c // per_hs))
        arrived_blocks.append(lax.ppermute(chunk, ("req", "head", "sub"), pairs))
    stacked = jnp.stack(arrived_blocks)
    order = (req_index % per_hs - jnp.arange(per_hs)) % per_hs
    head_total = jnp.take(stacked, order, axis=0)
    head_total = jnp.transpose(head_total, (1, 0, 2)).reshape(local_rows, per_hs * out_block)
    head_total = head_total.astype(jnp.float32)
    out_width = head_total.shape[1]
    residual = lax.dynamic_slice_in_dim(hidden_in, hs_index * out_width, out_width, 1)
    return (residual.astype(jnp.float32) + head_total).astype(jnp.bfloat16)


def solution(mesh):
    in_specs = (
        P(("groups", "req"), None),
        P("req", ("head", "sub")),
        P(),
        P(("groups", "req"), None, "head"),
        P(("groups", "req"), None, "head"),
        P(("head", "sub"), "req"),
        P(("groups", "req")),
        P(("groups", "req")),
        P("groups"),
    )
    out_specs = P(("groups", "req"), ("head", "sub"))
    return jax.shard_map(local, mesh=mesh, in_specs=in_specs, out_specs=out_specs, check_vma=False)
```

```python
import functools

import jax
import jax.numpy as jnp
from jax import lax
from jax.sharding import PartitionSpec as P
from jax.experimental import pallas as pl

HQ = 64
KVH = 8


def normalize_heads(queries, q_gain, head_dim):
    row_count = queries.shape[0]
    per_head = queries.astype(jnp.float32).reshape(row_count, -1, head_dim)
    inv_rms = lax.rsqrt(jnp.mean(per_head * per_head, axis=2, keepdims=True) + 1e-05)
    return (per_head * inv_rms * q_gain).reshape(row_count, -1).astype(jnp.bfloat16)


def shift_exchange(blocks, axis, count):
    arrived = [blocks[0]]
    for shift in range(1, count):
        arrived.append(
            lax.ppermute(blocks[shift], axis, [(i, (i + shift) % count) for i in range(count)])
        )
    return jnp.stack(arrived)


def line_reduce_scatter(chunk_of, axis, count, index):
    right = None
    left = None
    for step in range(1, count):
        dest_r = jnp.minimum(count - step + index, count - 1)
        send_r = chunk_of(dest_r) if right is None else chunk_of(dest_r) + right
        right = lax.ppermute(
            send_r.astype(jnp.bfloat16), axis, [(i, i + 1) for i in range(step)]
        ).astype(jnp.float32)
        dest_l = jnp.maximum(index - (count - step), 0)
        send_l = chunk_of(dest_l) if left is None else chunk_of(dest_l) + left
        left = lax.ppermute(
            send_l.astype(jnp.bfloat16), axis, [(i, i - 1) for i in range(count - step, count)]
        ).astype(jnp.float32)
    total = chunk_of(index)
    if right is not None:
        total = total + right + left
    return total


def line_gather_apply(block, apply, axis, count, index):
    own = apply(block)
    from_left = [own]
    from_right = [own]
    carry_r = block
    carry_l = block
    for step in range(1, count):
        carry_r = lax.ppermute(carry_r, axis, [(i, i + 1) for i in range(step - 1, count - 1)])
        carry_l = lax.ppermute(carry_l, axis, [(i, i - 1) for i in range(1, count - step + 1)])
        from_left.append(apply(carry_r))
        from_right.append(apply(carry_l))
    placed = jnp.zeros((count,) + own.shape, own.dtype)
    for step in range(count - 1, 0, -1):
        placed = lax.dynamic_update_index_in_dim(placed, from_left[step], index - step, 0)
    for step in range(count - 1, 0, -1):
        placed = lax.dynamic_update_index_in_dim(placed, from_right[step], index + step, 0)
    return lax.dynamic_update_index_in_dim(placed, own, index, 0)


def exchange_sum(parts, axis, count, index):
    total = lax.dynamic_index_in_dim(parts, index, axis=0, keepdims=False).astype(jnp.float32)
    for shift in range(1, count):
        outgoing = lax.dynamic_index_in_dim(parts, (index + shift) % count, axis=0, keepdims=False)
        incoming = lax.ppermute(outgoing, axis, [(i, (i + shift) % count) for i in range(count)])
        total = total + incoming.astype(jnp.float32)
    return total.astype(jnp.bfloat16)


def attend_kernel(q_ref, k_ref, v_ref, o_ref, *, per_kv, head_dim, token_count):
    padded_tokens = k_ref.shape[0]
    split = (token_count // 128) * 128
    keys = k_ref[...]
    rows = q_ref.shape[0]
    score_scale = head_dim ** (-0.5)
    for g in range(per_kv):
        query = q_ref[:, g * head_dim:(g + 1) * head_dim]
        scores = lax.dot_general(
            query, keys, (((1,), (1,)), ((), ())), preferred_element_type=jnp.float32
        ) * score_scale
        pieces = [scores[:, :split]] if split else []
        if split < padded_tokens:
            tail = scores[:, split:]
            valid = lax.broadcasted_iota(jnp.int32, tail.shape, 1) < token_count - split
            pieces.append(jnp.where(valid, tail, -jnp.inf))
        peak = jnp.max(pieces[0], axis=1, keepdims=True)
        for piece in pieces[1:]:
            peak = jnp.maximum(peak, jnp.max(piece, axis=1, keepdims=True))
        weights = [jnp.exp(piece - peak) for piece in pieces]
        total = sum(jnp.sum(w, axis=1, keepdims=True) for w in weights)
        inverse = 1.0 / total
        mixed = None
        start = 0
        for w in weights:
            width = w.shape[1]
            probs = (w * inverse).astype(jnp.bfloat16)
            term = jnp.dot(
                probs, v_ref[start:start + width, :], preferred_element_type=jnp.float32
            )
            mixed = term if mixed is None else mixed + term
            start += width
        o_ref[:, g * head_dim:(g + 1) * head_dim] = mixed.astype(o_ref.dtype)


def attend(rows_in, keys, values, kv_count, per_kv, head_dim, token_count):
    rows, width = rows_in.shape
    padded_tokens = keys.shape[0]
    group_width = per_kv * head_dim
    kernel = functools.partial(
        attend_kernel, per_kv=per_kv, head_dim=head_dim, token_count=token_count
    )
    flops = 4 * rows * padded_tokens * head_dim * per_kv * kv_count
    moved = 2 * (2 * rows * width + 2 * padded_tokens * head_dim * kv_count)
    return pl.pallas_call(
        kernel,
        grid=(kv_count,),
        in_specs=[
            pl.BlockSpec((rows, group_width), lambda k: (0, k)),
            pl.BlockSpec((padded_tokens, head_dim), lambda k: (0, k)),
            pl.BlockSpec((padded_tokens, head_dim), lambda k: (0, k)),
        ],
        out_specs=pl.BlockSpec((rows, group_width), lambda k: (0, k)),
        out_shape=jax.ShapeDtypeStruct((rows, width), jnp.bfloat16),
        cost_estimate=pl.CostEstimate(
            flops=flops,
            transcendentals=rows * padded_tokens * per_kv * kv_count,
            bytes_accessed=moved,
        ),
    )(rows_in, keys, values)


def local(
    hidden_in,
    q_weight,
    q_gain,
    key_cache,
    value_cache,
    out_weight,
    req_image,
    image_count,
    image_home,
):
    req_count = lax.axis_size("req")
    local_rows = hidden_in.shape[0]
    q_cols = q_weight.shape[1]
    head_dim = q_gain.shape[0]
    group_size = HQ // KVH
    heads_here = q_cols // head_dim
    sub_count = lax.axis_size("sub")
    sub_index = lax.axis_index("sub")
    block_width = hidden_in.shape[1] // req_count
    part_width = block_width // sub_count
    by_block = hidden_in.reshape(local_rows, req_count, sub_count, part_width)
    req_index = lax.axis_index("req")
    my_part = lax.dynamic_index_in_dim(by_block, sub_index, axis=2, keepdims=False)
    spread_part = jnp.zeros((req_count, local_rows, part_width), my_part.dtype)
    spread_part = lax.dynamic_update_index_in_dim(
        spread_part, lax.dynamic_index_in_dim(my_part, req_index, 1, keepdims=False), req_index, 0
    )
    for shift in range(1, req_count):
        outgoing_part = lax.dynamic_index_in_dim(
            my_part, (req_index + shift) % req_count, 1, keepdims=False
        )
        arrived_part = lax.ppermute(
            outgoing_part, "req", [(i, (i + shift) % req_count) for i in range(req_count)]
        )
        spread_part = lax.dynamic_update_index_in_dim(
            spread_part, arrived_part, (req_index - shift) % req_count, 0
        )
    spread_part = spread_part.reshape(req_count * local_rows, part_width)
    spread_cols = jnp.zeros((req_count * local_rows, block_width), spread_part.dtype)
    spread_cols = lax.dynamic_update_slice_in_dim(
        spread_cols, spread_part, sub_index * part_width, 1
    )
    for shift in range(1, sub_count):
        other_part = lax.ppermute(
            spread_part, "sub", [(i, (i + shift) % sub_count) for i in range(sub_count)]
        )
        spread_cols = lax.dynamic_update_slice_in_dim(
            spread_cols, other_part, ((sub_index - shift) % sub_count) * part_width, 1
        )
    def query_chunk(owner):
        rows = lax.dynamic_slice_in_dim(spread_cols, owner * local_rows, local_rows, 0)
        product = jnp.dot(rows, q_weight, preferred_element_type=jnp.float32)
        return product.astype(jnp.bfloat16).astype(jnp.float32)

    query_sum = line_reduce_scatter(query_chunk, "req", req_count, req_index)
    queries = lax.optimization_barrier(query_sum.astype(jnp.bfloat16))
    normalized = normalize_heads(queries, q_gain, head_dim)
    capacity = 2 * local_rows // req_count
    slot_total = req_count * capacity
    table_ids = lax.broadcasted_iota(jnp.int32, (local_rows, image_home.shape[0]), 1)
    home_rows = jnp.sum(jnp.where(req_image[:, None] == table_ids, image_home[None, :], 0), axis=1)
    wanted = image_count == 1
    dest_ids = lax.broadcasted_iota(jnp.int32, (local_rows, req_count), 1)
    to_dest = ((home_rows[:, None] == dest_ids) & wanted[:, None]).astype(jnp.int32)
    earlier = jnp.cumsum(to_dest, axis=0) - to_dest
    position = ((home_rows - req_index) % req_count) * capacity + jnp.sum(
        earlier * to_dest, axis=1
    )
    slot_ids = lax.broadcasted_iota(jnp.int32, (slot_total, local_rows), 0)
    dispatch = ((slot_ids == position[None, :]) & wanted[None, :]).astype(jnp.bfloat16)
    outgoing = jnp.dot(dispatch, normalized, preferred_element_type=jnp.float32).astype(
        jnp.bfloat16
    )
    outgoing = outgoing.reshape(req_count, capacity, q_cols)
    kv_count = max(1, heads_here // group_size)
    per_kv = heads_here // kv_count
    kv_first = sub_index * heads_here // group_size
    token_count = key_cache.shape[1]
    padded_tokens = -(-token_count // 128) * 128
    keys_here = jnp.pad(
        lax.dynamic_slice_in_dim(key_cache[0], kv_first * head_dim, kv_count * head_dim, 1),
        ((0, padded_tokens - token_count), (0, 0)),
    )
    values_here = jnp.pad(
        lax.dynamic_slice_in_dim(value_cache[0], kv_first * head_dim, kv_count * head_dim, 1),
        ((0, padded_tokens - token_count), (0, 0)),
    )
    arrived = shift_exchange(outgoing, "req", req_count)
    sources = arrived.shape[0]
    slot_count = arrived.shape[1]
    flat_rows = arrived.reshape(sources * slot_count, q_cols)
    mixed_heads = attend(flat_rows, keys_here, values_here, kv_count, per_kv, head_dim, token_count)
    replies = mixed_heads.reshape(sources, slot_count, q_cols)
    returned = shift_exchange(
        jnp.concatenate([replies[:1], replies[1:][::-1]]), "req", req_count
    )
    returned = jnp.concatenate([returned[:1], returned[1:][::-1]])
    attended = lax.dot_general(
        dispatch,
        returned.reshape(slot_total, q_cols),
        (((0,), (0,)), ((), ())),
        preferred_element_type=jnp.float32,
    ).astype(jnp.bfloat16)
    def out_part(rows):
        product = jnp.dot(rows, out_weight, preferred_element_type=jnp.float32)
        return product.astype(jnp.bfloat16)

    partial_cols = line_gather_apply(attended, out_part, "req", req_count, req_index)
    partial_cols = partial_cols.reshape(req_count * local_rows, out_weight.shape[1])
    hs_count = lax.axis_size("head") * sub_count
    hs_index = lax.axis_index("head") * sub_count + sub_index
    head_count = lax.axis_size("head")
    by_group = partial_cols.reshape(sub_count, -1, partial_cols.shape[1])
    sub_sums = exchange_sum(by_group, "sub", sub_count, sub_index)
    per_hs = req_count // hs_count
    out_block = partial_cols.shape[1]
    sub_sums = sub_sums.reshape(head_count, per_hs, local_rows, out_block)
    head_index = lax.axis_index("head")
    head_total = jnp.zeros((local_rows, per_hs * out_block), jnp.float32)
    for step in range(per_hs):
        gathered = None
        for turn in range(head_count):
            group = (head_index + turn) % head_count
            chunk = lax.dynamic_index_in_dim(sub_sums, group, 0, keepdims=False)
            chunk = lax.dynamic_index_in_dim(
                chunk, (req_index + step) % per_hs, 0, keepdims=False
            )
            pairs = []
            for c in range(req_count):
                for h in range(head_count):
                    for u in range(sub_count):
                        g = (h + turn) % head_count
                        k = (u * head_count + g) * per_hs + (c + step) % per_hs
                        src = c * hs_count + h * sub_count + u
                        pairs.append((src, k * hs_count + c // per_hs))
            got = lax.ppermute(chunk, ("req", "head", "sub"), pairs).astype(jnp.float32)
            gathered = got if gathered is None else gathered + got
        head_total = lax.dynamic_update_slice_in_dim(
            head_total, gathered, ((req_index % per_hs - step) % per_hs) * out_block, 1
        )
    head_total = head_total.astype(jnp.float32)
    out_width = head_total.shape[1]
    residual = lax.dynamic_slice_in_dim(hidden_in, hs_index * out_width, out_width, 1)
    return (residual.astype(jnp.float32) + head_total).astype(jnp.bfloat16)


def solution(mesh):
    in_specs = (
        P(("groups", "req"), None),
        P("req", ("head", "sub")),
        P(),
        P(("groups", "req"), None, "head"),
        P(("groups", "req"), None, "head"),
        P(("head", "sub"), "req"),
        P(("groups", "req")),
        P(("groups", "req")),
        P("groups"),
    )
    out_specs = P(("groups", "req"), ("head", "sub"))
    return jax.shard_map(local, mesh=mesh, in_specs=in_specs, out_specs=out_specs, check_vma=False)
```

```python
import functools

import jax
import jax.numpy as jnp
from jax import lax
from jax.sharding import PartitionSpec as P
from jax.experimental import pallas as pl

HQ = 64
KVH = 8


def normalize_heads(queries, q_gain, head_dim):
    row_count = queries.shape[0]
    per_head = queries.astype(jnp.float32).reshape(row_count, -1, head_dim)
    inv_rms = lax.rsqrt(jnp.mean(per_head * per_head, axis=2, keepdims=True) + 1e-05)
    return (per_head * inv_rms * q_gain).reshape(row_count, -1).astype(jnp.bfloat16)


def shift_exchange(blocks, axis, count):
    arrived = [blocks[0]]
    for shift in range(1, count):
        arrived.append(
            lax.ppermute(blocks[shift], axis, [(i, (i + shift) % count) for i in range(count)])
        )
    return jnp.stack(arrived)


def direct_reduce_scatter(chunk_of, axis, count, index):
    total = None
    for shift in range(1, count):
        outgoing = chunk_of((index + shift) % count).astype(jnp.bfloat16)
        incoming = lax.ppermute(outgoing, axis, [(i, (i + shift) % count) for i in range(count)])
        incoming = incoming.astype(jnp.float32)
        total = incoming if total is None else total + incoming
    own = chunk_of(index)
    return own if total is None else own + total


def direct_gather_apply(block, apply, axis, count, index):
    own = apply(block)
    placed = jnp.zeros((count,) + own.shape, own.dtype)
    placed = lax.dynamic_update_index_in_dim(placed, own, index, 0)
    for shift in range(1, count):
        incoming = lax.ppermute(block, axis, [(i, (i + shift) % count) for i in range(count)])
        placed = lax.dynamic_update_index_in_dim(
            placed, apply(incoming), (index - shift) % count, 0
        )
    return placed


def exchange_sum(parts, axis, count, index):
    total = lax.dynamic_index_in_dim(parts, index, axis=0, keepdims=False).astype(jnp.float32)
    for shift in range(1, count):
        outgoing = lax.dynamic_index_in_dim(parts, (index + shift) % count, axis=0, keepdims=False)
        incoming = lax.ppermute(outgoing, axis, [(i, (i + shift) % count) for i in range(count)])
        total = total + incoming.astype(jnp.float32)
    return total.astype(jnp.bfloat16)


def attend_kernel(q_ref, k_ref, v_ref, o_ref, *, per_kv, head_dim, token_count):
    padded_tokens = k_ref.shape[0]
    split = (token_count // 128) * 128
    keys = k_ref[...]
    rows = q_ref.shape[0]
    score_scale = head_dim ** (-0.5)
    for g in range(per_kv):
        query = q_ref[:, g * head_dim:(g + 1) * head_dim]
        scores = lax.dot_general(
            query, keys, (((1,), (1,)), ((), ())), preferred_element_type=jnp.float32
        ) * score_scale
        pieces = [scores[:, :split]] if split else []
        if split < padded_tokens:
            tail = scores[:, split:]
            valid = lax.broadcasted_iota(jnp.int32, tail.shape, 1) < token_count - split
            pieces.append(jnp.where(valid, tail, -jnp.inf))
        peak = jnp.max(pieces[0], axis=1, keepdims=True)
        for piece in pieces[1:]:
            peak = jnp.maximum(peak, jnp.max(piece, axis=1, keepdims=True))
        weights = [jnp.exp(piece - peak) for piece in pieces]
        total = sum(jnp.sum(w, axis=1, keepdims=True) for w in weights)
        inverse = 1.0 / total
        mixed = None
        start = 0
        for w in weights:
            width = w.shape[1]
            probs = (w * inverse).astype(jnp.bfloat16)
            term = jnp.dot(
                probs, v_ref[start:start + width, :], preferred_element_type=jnp.float32
            )
            mixed = term if mixed is None else mixed + term
            start += width
        o_ref[:, g * head_dim:(g + 1) * head_dim] = mixed.astype(o_ref.dtype)


def attend(rows_in, keys, values, kv_count, per_kv, head_dim, token_count):
    rows, width = rows_in.shape
    padded_tokens = keys.shape[0]
    group_width = per_kv * head_dim
    kernel = functools.partial(
        attend_kernel, per_kv=per_kv, head_dim=head_dim, token_count=token_count
    )
    flops = 4 * rows * padded_tokens * head_dim * per_kv * kv_count
    moved = 2 * (2 * rows * width + 2 * padded_tokens * head_dim * kv_count)
    return pl.pallas_call(
        kernel,
        grid=(kv_count,),
        in_specs=[
            pl.BlockSpec((rows, group_width), lambda k: (0, k)),
            pl.BlockSpec((padded_tokens, head_dim), lambda k: (0, k)),
            pl.BlockSpec((padded_tokens, head_dim), lambda k: (0, k)),
        ],
        out_specs=pl.BlockSpec((rows, group_width), lambda k: (0, k)),
        out_shape=jax.ShapeDtypeStruct((rows, width), jnp.bfloat16),
        cost_estimate=pl.CostEstimate(
            flops=flops,
            transcendentals=rows * padded_tokens * per_kv * kv_count,
            bytes_accessed=moved,
        ),
    )(rows_in, keys, values)


def local(
    hidden_in,
    q_weight,
    q_gain,
    key_cache,
    value_cache,
    out_weight,
    req_image,
    image_count,
    image_home,
):
    req_count = lax.axis_size("req")
    local_rows = hidden_in.shape[0]
    q_cols = q_weight.shape[1]
    head_dim = q_gain.shape[0]
    group_size = HQ // KVH
    heads_here = q_cols // head_dim
    sub_count = lax.axis_size("sub")
    sub_index = lax.axis_index("sub")
    block_width = hidden_in.shape[1] // req_count
    part_width = block_width // sub_count
    by_block = hidden_in.reshape(local_rows, req_count, sub_count, part_width)
    req_index = lax.axis_index("req")
    my_part = lax.dynamic_index_in_dim(by_block, sub_index, axis=2, keepdims=False)
    spread_part = jnp.zeros((req_count, local_rows, part_width), my_part.dtype)
    spread_part = lax.dynamic_update_index_in_dim(
        spread_part, lax.dynamic_index_in_dim(my_part, req_index, 1, keepdims=False), req_index, 0
    )
    for shift in range(1, req_count):
        outgoing_part = lax.dynamic_index_in_dim(
            my_part, (req_index + shift) % req_count, 1, keepdims=False
        )
        arrived_part = lax.ppermute(
            outgoing_part, "req", [(i, (i + shift) % req_count) for i in range(req_count)]
        )
        spread_part = lax.dynamic_update_index_in_dim(
            spread_part, arrived_part, (req_index - shift) % req_count, 0
        )
    spread_part = spread_part.reshape(req_count * local_rows, part_width)
    spread_cols = jnp.zeros((req_count * local_rows, block_width), spread_part.dtype)
    spread_cols = lax.dynamic_update_slice_in_dim(
        spread_cols, spread_part, sub_index * part_width, 1
    )
    for shift in range(1, sub_count):
        other_part = lax.ppermute(
            spread_part, "sub", [(i, (i + shift) % sub_count) for i in range(sub_count)]
        )
        spread_cols = lax.dynamic_update_slice_in_dim(
            spread_cols, other_part, ((sub_index - shift) % sub_count) * part_width, 1
        )
    def query_chunk(owner):
        rows = lax.dynamic_slice_in_dim(spread_cols, owner * local_rows, local_rows, 0)
        product = jnp.dot(rows, q_weight, preferred_element_type=jnp.float32)
        return product.astype(jnp.bfloat16).astype(jnp.float32)

    query_sum = direct_reduce_scatter(query_chunk, "req", req_count, req_index)
    queries = lax.optimization_barrier(query_sum.astype(jnp.bfloat16))
    normalized = normalize_heads(queries, q_gain, head_dim)
    capacity = 2 * local_rows // req_count
    slot_total = req_count * capacity
    table_ids = lax.broadcasted_iota(jnp.int32, (local_rows, image_home.shape[0]), 1)
    home_rows = jnp.sum(jnp.where(req_image[:, None] == table_ids, image_home[None, :], 0), axis=1)
    wanted = image_count == 1
    dest_ids = lax.broadcasted_iota(jnp.int32, (local_rows, req_count), 1)
    to_dest = ((home_rows[:, None] == dest_ids) & wanted[:, None]).astype(jnp.int32)
    earlier = jnp.cumsum(to_dest, axis=0) - to_dest
    position = ((home_rows - req_index) % req_count) * capacity + jnp.sum(
        earlier * to_dest, axis=1
    )
    slot_ids = lax.broadcasted_iota(jnp.int32, (slot_total, local_rows), 0)
    dispatch = ((slot_ids == position[None, :]) & wanted[None, :]).astype(jnp.bfloat16)
    outgoing = jnp.dot(dispatch, normalized, preferred_element_type=jnp.float32).astype(
        jnp.bfloat16
    )
    outgoing = outgoing.reshape(req_count, capacity, q_cols)
    kv_count = max(1, heads_here // group_size)
    per_kv = heads_here // kv_count
    kv_first = sub_index * heads_here // group_size
    token_count = key_cache.shape[1]
    padded_tokens = -(-token_count // 128) * 128
    keys_here = jnp.pad(
        lax.dynamic_slice_in_dim(key_cache[0], kv_first * head_dim, kv_count * head_dim, 1),
        ((0, padded_tokens - token_count), (0, 0)),
    )
    values_here = jnp.pad(
        lax.dynamic_slice_in_dim(value_cache[0], kv_first * head_dim, kv_count * head_dim, 1),
        ((0, padded_tokens - token_count), (0, 0)),
    )
    arrived = shift_exchange(outgoing, "req", req_count)
    sources = arrived.shape[0]
    slot_count = arrived.shape[1]
    flat_rows = arrived.reshape(sources * slot_count, q_cols)
    mixed_heads = attend(flat_rows, keys_here, values_here, kv_count, per_kv, head_dim, token_count)
    replies = mixed_heads.reshape(sources, slot_count, q_cols)
    returned = shift_exchange(
        jnp.concatenate([replies[:1], replies[1:][::-1]]), "req", req_count
    )
    returned = jnp.concatenate([returned[:1], returned[1:][::-1]])
    attended = lax.dot_general(
        dispatch,
        returned.reshape(slot_total, q_cols),
        (((0,), (0,)), ((), ())),
        preferred_element_type=jnp.float32,
    ).astype(jnp.bfloat16)
    def out_part(rows):
        product = jnp.dot(rows, out_weight, preferred_element_type=jnp.float32)
        return product.astype(jnp.bfloat16)

    partial_cols = direct_gather_apply(attended, out_part, "req", req_count, req_index)
    partial_cols = partial_cols.reshape(req_count * local_rows, out_weight.shape[1])
    hs_count = lax.axis_size("head") * sub_count
    hs_index = lax.axis_index("head") * sub_count + sub_index
    head_count = lax.axis_size("head")
    by_group = partial_cols.reshape(sub_count, -1, partial_cols.shape[1])
    sub_sums = exchange_sum(by_group, "sub", sub_count, sub_index)
    per_hs = req_count // hs_count
    out_block = partial_cols.shape[1]
    sub_sums = sub_sums.reshape(head_count, per_hs, local_rows, out_block)
    head_index = lax.axis_index("head")
    head_total = jnp.zeros((local_rows, per_hs * out_block), jnp.float32)
    for step in range(per_hs):
        gathered = None
        for turn in range(head_count):
            group = (head_index + turn) % head_count
            chunk = lax.dynamic_index_in_dim(sub_sums, group, 0, keepdims=False)
            chunk = lax.dynamic_index_in_dim(
                chunk, (req_index + step) % per_hs, 0, keepdims=False
            )
            pairs = []
            for c in range(req_count):
                for h in range(head_count):
                    for u in range(sub_count):
                        g = (h + turn) % head_count
                        k = (u * head_count + g) * per_hs + (c + step) % per_hs
                        src = c * hs_count + h * sub_count + u
                        pairs.append((src, k * hs_count + c // per_hs))
            got = lax.ppermute(chunk, ("req", "head", "sub"), pairs).astype(jnp.float32)
            gathered = got if gathered is None else gathered + got
        head_total = lax.dynamic_update_slice_in_dim(
            head_total, gathered, ((req_index % per_hs - step) % per_hs) * out_block, 1
        )
    head_total = head_total.astype(jnp.float32)
    out_width = head_total.shape[1]
    residual = lax.dynamic_slice_in_dim(hidden_in, hs_index * out_width, out_width, 1)
    return (residual.astype(jnp.float32) + head_total).astype(jnp.bfloat16)


def solution(mesh):
    in_specs = (
        P(("groups", "req"), None),
        P("req", ("head", "sub")),
        P(),
        P(("groups", "req"), None, "head"),
        P(("groups", "req"), None, "head"),
        P(("head", "sub"), "req"),
        P(("groups", "req")),
        P(("groups", "req")),
        P("groups"),
    )
    out_specs = P(("groups", "req"), ("head", "sub"))
    return jax.shard_map(local, mesh=mesh, in_specs=in_specs, out_specs=out_specs, check_vma=False)
```

```python
import functools

import jax
import jax.numpy as jnp
from jax import lax
from jax.sharding import PartitionSpec as P
from jax.experimental import pallas as pl

HQ = 64
KVH = 8


def normalize_heads(queries, q_gain, head_dim):
    row_count = queries.shape[0]
    per_head = queries.astype(jnp.float32).reshape(row_count, -1, head_dim)
    inv_rms = lax.rsqrt(jnp.mean(per_head * per_head, axis=2, keepdims=True) + 1e-05)
    return (per_head * inv_rms * q_gain).reshape(row_count, -1).astype(jnp.bfloat16)


def direct_reduce_scatter(chunk_of, axis, count, index):
    total = None
    for shift in range(1, count):
        outgoing = chunk_of((index + shift) % count).astype(jnp.bfloat16)
        incoming = lax.ppermute(outgoing, axis, [(i, (i + shift) % count) for i in range(count)])
        incoming = incoming.astype(jnp.float32)
        total = incoming if total is None else total + incoming
    own = chunk_of(index)
    return own if total is None else own + total


def direct_gather_apply(block, apply, axis, count, index):
    own = apply(block)
    placed = jnp.zeros((count,) + own.shape, own.dtype)
    placed = lax.dynamic_update_index_in_dim(placed, own, index, 0)
    for shift in range(1, count):
        incoming = lax.ppermute(block, axis, [(i, (i + shift) % count) for i in range(count)])
        placed = lax.dynamic_update_index_in_dim(
            placed, apply(incoming), (index - shift) % count, 0
        )
    return placed


def exchange_sum(parts, axis, count, index):
    total = lax.dynamic_index_in_dim(parts, index, axis=0, keepdims=False).astype(jnp.float32)
    for shift in range(1, count):
        outgoing = lax.dynamic_index_in_dim(parts, (index + shift) % count, axis=0, keepdims=False)
        incoming = lax.ppermute(outgoing, axis, [(i, (i + shift) % count) for i in range(count)])
        total = total + incoming.astype(jnp.float32)
    return total.astype(jnp.bfloat16)


def attend_kernel(q_ref, k_ref, v_ref, o_ref, *, per_kv, head_dim, token_count):
    padded_tokens = k_ref.shape[0]
    split = (token_count // 128) * 128
    keys = k_ref[...]
    rows = q_ref.shape[0]
    score_scale = head_dim ** (-0.5)
    for g in range(per_kv):
        query = q_ref[:, g * head_dim:(g + 1) * head_dim]
        scores = lax.dot_general(
            query, keys, (((1,), (1,)), ((), ())), preferred_element_type=jnp.float32
        ) * score_scale
        pieces = [scores[:, :split]] if split else []
        if split < padded_tokens:
            tail = scores[:, split:]
            valid = lax.broadcasted_iota(jnp.int32, tail.shape, 1) < token_count - split
            pieces.append(jnp.where(valid, tail, -jnp.inf))
        peak = jnp.max(pieces[0], axis=1, keepdims=True)
        for piece in pieces[1:]:
            peak = jnp.maximum(peak, jnp.max(piece, axis=1, keepdims=True))
        weights = [jnp.exp(piece - peak) for piece in pieces]
        total = sum(jnp.sum(w, axis=1, keepdims=True) for w in weights)
        inverse = 1.0 / total
        mixed = None
        start = 0
        for w in weights:
            width = w.shape[1]
            probs = (w * inverse).astype(jnp.bfloat16)
            term = jnp.dot(
                probs, v_ref[start:start + width, :], preferred_element_type=jnp.float32
            )
            mixed = term if mixed is None else mixed + term
            start += width
        o_ref[:, g * head_dim:(g + 1) * head_dim] = mixed.astype(o_ref.dtype)


def attend(rows_in, keys, values, kv_count, per_kv, head_dim, token_count):
    rows, width = rows_in.shape
    padded_tokens = keys.shape[0]
    group_width = per_kv * head_dim
    kernel = functools.partial(
        attend_kernel, per_kv=per_kv, head_dim=head_dim, token_count=token_count
    )
    flops = 4 * rows * padded_tokens * head_dim * per_kv * kv_count
    moved = 2 * (2 * rows * width + 2 * padded_tokens * head_dim * kv_count)
    return pl.pallas_call(
        kernel,
        grid=(kv_count,),
        in_specs=[
            pl.BlockSpec((rows, group_width), lambda k: (0, k)),
            pl.BlockSpec((padded_tokens, head_dim), lambda k: (0, k)),
            pl.BlockSpec((padded_tokens, head_dim), lambda k: (0, k)),
        ],
        out_specs=pl.BlockSpec((rows, group_width), lambda k: (0, k)),
        out_shape=jax.ShapeDtypeStruct((rows, width), jnp.bfloat16),
        cost_estimate=pl.CostEstimate(
            flops=flops,
            transcendentals=rows * padded_tokens * per_kv * kv_count,
            bytes_accessed=moved,
        ),
    )(rows_in, keys, values)


def local(
    hidden_in,
    q_weight,
    q_gain,
    key_cache,
    value_cache,
    out_weight,
    req_image,
    image_count,
    image_home,
):
    req_count = lax.axis_size("req")
    local_rows = hidden_in.shape[0]
    q_cols = q_weight.shape[1]
    head_dim = q_gain.shape[0]
    group_size = HQ // KVH
    heads_here = q_cols // head_dim
    sub_count = lax.axis_size("sub")
    sub_index = lax.axis_index("sub")
    block_width = hidden_in.shape[1] // req_count
    part_width = block_width // sub_count
    by_block = hidden_in.reshape(local_rows, req_count, sub_count, part_width)
    req_index = lax.axis_index("req")
    my_part = lax.dynamic_index_in_dim(by_block, sub_index, axis=2, keepdims=False)
    spread_part = jnp.zeros((req_count, local_rows, part_width), my_part.dtype)
    spread_part = lax.dynamic_update_index_in_dim(
        spread_part, lax.dynamic_index_in_dim(my_part, req_index, 1, keepdims=False), req_index, 0
    )
    for shift in range(1, req_count):
        outgoing_part = lax.dynamic_index_in_dim(
            my_part, (req_index + shift) % req_count, 1, keepdims=False
        )
        arrived_part = lax.ppermute(
            outgoing_part, "req", [(i, (i + shift) % req_count) for i in range(req_count)]
        )
        spread_part = lax.dynamic_update_index_in_dim(
            spread_part, arrived_part, (req_index - shift) % req_count, 0
        )
    spread_part = spread_part.reshape(req_count * local_rows, part_width)
    spread_cols = jnp.zeros((req_count * local_rows, block_width), spread_part.dtype)
    spread_cols = lax.dynamic_update_slice_in_dim(
        spread_cols, spread_part, sub_index * part_width, 1
    )
    for shift in range(1, sub_count):
        other_part = lax.ppermute(
            spread_part, "sub", [(i, (i + shift) % sub_count) for i in range(sub_count)]
        )
        spread_cols = lax.dynamic_update_slice_in_dim(
            spread_cols, other_part, ((sub_index - shift) % sub_count) * part_width, 1
        )
    def query_chunk(owner):
        rows = lax.dynamic_slice_in_dim(spread_cols, owner * local_rows, local_rows, 0)
        product = jnp.dot(rows, q_weight, preferred_element_type=jnp.float32)
        return product.astype(jnp.bfloat16).astype(jnp.float32)

    query_sum = direct_reduce_scatter(query_chunk, "req", req_count, req_index)
    queries = lax.optimization_barrier(query_sum.astype(jnp.bfloat16))
    normalized = normalize_heads(queries, q_gain, head_dim)
    capacity = 2 * local_rows // req_count
    slot_total = req_count * capacity
    table_ids = lax.broadcasted_iota(jnp.int32, (local_rows, image_home.shape[0]), 1)
    home_rows = jnp.sum(jnp.where(req_image[:, None] == table_ids, image_home[None, :], 0), axis=1)
    wanted = image_count == 1
    dest_ids = lax.broadcasted_iota(jnp.int32, (local_rows, req_count), 1)
    to_dest = ((home_rows[:, None] == dest_ids) & wanted[:, None]).astype(jnp.int32)
    earlier = jnp.cumsum(to_dest, axis=0) - to_dest
    position = ((home_rows - req_index) % req_count) * capacity + jnp.sum(
        earlier * to_dest, axis=1
    )
    slot_ids = lax.broadcasted_iota(jnp.int32, (slot_total, local_rows), 0)
    dispatch = ((slot_ids == position[None, :]) & wanted[None, :]).astype(jnp.bfloat16)
    outgoing = jnp.dot(dispatch, normalized, preferred_element_type=jnp.float32).astype(
        jnp.bfloat16
    )
    outgoing = outgoing.reshape(req_count, capacity, q_cols)
    kv_count = max(1, heads_here // group_size)
    per_kv = heads_here // kv_count
    kv_first = sub_index * heads_here // group_size
    token_count = key_cache.shape[1]
    padded_tokens = -(-token_count // 128) * 128
    keys_here = jnp.pad(
        lax.dynamic_slice_in_dim(key_cache[0], kv_first * head_dim, kv_count * head_dim, 1),
        ((0, padded_tokens - token_count), (0, 0)),
    )
    values_here = jnp.pad(
        lax.dynamic_slice_in_dim(value_cache[0], kv_first * head_dim, kv_count * head_dim, 1),
        ((0, padded_tokens - token_count), (0, 0)),
    )
    returned_blocks = []
    for shift in range(req_count):
        if shift == 0:
            arrived_block = outgoing[0]
        else:
            arrived_block = lax.ppermute(
                outgoing[shift], "req", [(i, (i + shift) % req_count) for i in range(req_count)]
            )
        mixed_block = attend(
            arrived_block, keys_here, values_here, kv_count, per_kv, head_dim, token_count
        )
        if shift:
            mixed_block = lax.ppermute(
                mixed_block, "req", [(i, (i - shift) % req_count) for i in range(req_count)]
            )
        returned_blocks.append(mixed_block)
    returned = jnp.stack(returned_blocks)
    attended = lax.dot_general(
        dispatch,
        returned.reshape(slot_total, q_cols),
        (((0,), (0,)), ((), ())),
        preferred_element_type=jnp.float32,
    ).astype(jnp.bfloat16)
    def out_part(rows):
        product = jnp.dot(rows, out_weight, preferred_element_type=jnp.float32)
        return product.astype(jnp.bfloat16)

    partial_cols = direct_gather_apply(attended, out_part, "req", req_count, req_index)
    partial_cols = partial_cols.reshape(req_count * local_rows, out_weight.shape[1])
    hs_count = lax.axis_size("head") * sub_count
    hs_index = lax.axis_index("head") * sub_count + sub_index
    head_count = lax.axis_size("head")
    by_group = partial_cols.reshape(sub_count, -1, partial_cols.shape[1])
    sub_sums = exchange_sum(by_group, "sub", sub_count, sub_index)
    per_hs = req_count // hs_count
    out_block = partial_cols.shape[1]
    sub_sums = sub_sums.reshape(head_count, per_hs, local_rows, out_block)
    head_index = lax.axis_index("head")
    head_total = jnp.zeros((local_rows, per_hs * out_block), jnp.float32)
    for step in range(per_hs):
        gathered = None
        for turn in range(head_count):
            group = (head_index + turn) % head_count
            chunk = lax.dynamic_index_in_dim(sub_sums, group, 0, keepdims=False)
            chunk = lax.dynamic_index_in_dim(
                chunk, (req_index + step) % per_hs, 0, keepdims=False
            )
            pairs = []
            for c in range(req_count):
                for h in range(head_count):
                    for u in range(sub_count):
                        g = (h + turn) % head_count
                        k = (u * head_count + g) * per_hs + (c + step) % per_hs
                        src = c * hs_count + h * sub_count + u
                        pairs.append((src, k * hs_count + c // per_hs))
            got = lax.ppermute(chunk, ("req", "head", "sub"), pairs).astype(jnp.float32)
            gathered = got if gathered is None else gathered + got
        head_total = lax.dynamic_update_slice_in_dim(
            head_total, gathered, ((req_index % per_hs - step) % per_hs) * out_block, 1
        )
    head_total = head_total.astype(jnp.float32)
    out_width = head_total.shape[1]
    residual = lax.dynamic_slice_in_dim(hidden_in, hs_index * out_width, out_width, 1)
    return (residual.astype(jnp.float32) + head_total).astype(jnp.bfloat16)


def solution(mesh):
    in_specs = (
        P(("groups", "req"), None),
        P("req", ("head", "sub")),
        P(),
        P(("groups", "req"), None, "head"),
        P(("groups", "req"), None, "head"),
        P(("head", "sub"), "req"),
        P(("groups", "req")),
        P(("groups", "req")),
        P("groups"),
    )
    out_specs = P(("groups", "req"), ("head", "sub"))
    return jax.shard_map(local, mesh=mesh, in_specs=in_specs, out_specs=out_specs, check_vma=False)
```

```python
import functools

import jax
import jax.numpy as jnp
from jax import lax
from jax.sharding import PartitionSpec as P
from jax.experimental import pallas as pl

HQ = 64
KVH = 8


def normalize_heads(queries, q_gain, head_dim):
    row_count = queries.shape[0]
    per_head = queries.astype(jnp.float32).reshape(row_count, -1, head_dim)
    inv_rms = lax.rsqrt(jnp.mean(per_head * per_head, axis=2, keepdims=True) + 1e-05)
    return (per_head * inv_rms * q_gain).reshape(row_count, -1).astype(jnp.bfloat16)


def direct_reduce_scatter(chunk_of, axis, count, index):
    total = None
    for shift in range(1, count):
        outgoing = chunk_of((index + shift) % count).astype(jnp.bfloat16)
        incoming = lax.ppermute(outgoing, axis, [(i, (i + shift) % count) for i in range(count)])
        incoming = incoming.astype(jnp.float32)
        total = incoming if total is None else total + incoming
    own = chunk_of(index)
    return own if total is None else own + total


def direct_gather_apply(block, apply, axis, count, index):
    own = apply(block)
    placed = jnp.zeros((count,) + own.shape, own.dtype)
    placed = lax.dynamic_update_index_in_dim(placed, own, index, 0)
    for shift in range(1, count):
        incoming = lax.ppermute(block, axis, [(i, (i + shift) % count) for i in range(count)])
        placed = lax.dynamic_update_index_in_dim(
            placed, apply(incoming), (index - shift) % count, 0
        )
    return placed


def exchange_sum(parts, axis, count, index):
    total = lax.dynamic_index_in_dim(parts, index, axis=0, keepdims=False).astype(jnp.float32)
    for shift in range(1, count):
        outgoing = lax.dynamic_index_in_dim(parts, (index + shift) % count, axis=0, keepdims=False)
        incoming = lax.ppermute(outgoing, axis, [(i, (i + shift) % count) for i in range(count)])
        total = total + incoming.astype(jnp.float32)
    return total.astype(jnp.bfloat16)


def attend_kernel(q_ref, k_ref, v_ref, o_ref, *, head_dim, token_count):
    padded_tokens = k_ref.shape[0]
    split = (token_count // 128) * 128
    scores = lax.dot_general(
        q_ref[0], k_ref[...], (((1,), (1,)), ((), ())), preferred_element_type=jnp.float32
    ) * (head_dim ** (-0.5))
    pieces = [scores[:, :split]] if split else []
    if split < padded_tokens:
        tail = scores[:, split:]
        valid = lax.broadcasted_iota(jnp.int32, tail.shape, 1) < token_count - split
        pieces.append(jnp.where(valid, tail, -jnp.inf))
    peak = jnp.max(pieces[0], axis=1, keepdims=True)
    for piece in pieces[1:]:
        peak = jnp.maximum(peak, jnp.max(piece, axis=1, keepdims=True))
    weights = [jnp.exp(piece - peak) for piece in pieces]
    total = sum(jnp.sum(w, axis=1, keepdims=True) for w in weights)
    inverse = 1.0 / total
    mixed = None
    start = 0
    for w in weights:
        width = w.shape[1]
        probs = (w * inverse).astype(jnp.bfloat16)
        term = jnp.dot(probs, v_ref[start:start + width, :], preferred_element_type=jnp.float32)
        mixed = term if mixed is None else mixed + term
        start += width
    o_ref[0] = mixed.astype(o_ref.dtype)


def attend(rows_in, keys, values, kv_count, per_kv, head_dim, token_count):
    rows, width = rows_in.shape
    padded_tokens = keys.shape[0]
    stacked = rows_in.reshape(rows, kv_count, per_kv, head_dim).transpose(1, 2, 0, 3)
    stacked = stacked.reshape(kv_count, per_kv * rows, head_dim)
    kernel = functools.partial(attend_kernel, head_dim=head_dim, token_count=token_count)
    flops = 4 * rows * padded_tokens * head_dim * per_kv * kv_count
    moved = 2 * (2 * rows * width + 2 * padded_tokens * head_dim * kv_count)
    mixed = pl.pallas_call(
        kernel,
        grid=(kv_count,),
        in_specs=[
            pl.BlockSpec((1, per_kv * rows, head_dim), lambda k: (k, 0, 0)),
            pl.BlockSpec((padded_tokens, head_dim), lambda k: (0, k)),
            pl.BlockSpec((padded_tokens, head_dim), lambda k: (0, k)),
        ],
        out_specs=pl.BlockSpec((1, per_kv * rows, head_dim), lambda k: (k, 0, 0)),
        out_shape=jax.ShapeDtypeStruct((kv_count, per_kv * rows, head_dim), jnp.bfloat16),
        cost_estimate=pl.CostEstimate(
            flops=flops,
            transcendentals=rows * padded_tokens * per_kv * kv_count,
            bytes_accessed=moved,
        ),
    )(stacked, keys, values)
    mixed = mixed.reshape(kv_count, per_kv, rows, head_dim).transpose(2, 0, 1, 3)
    return mixed.reshape(rows, width)


def direct_reduce_scatter(chunk_of, axis, count, index):
    total = None
    for shift in range(1, count):
        outgoing = chunk_of((index + shift) % count).astype(jnp.bfloat16)
        incoming = lax.ppermute(outgoing, axis, [(i, (i + shift) % count) for i in range(count)])
        incoming = incoming.astype(jnp.float32)
        total = incoming if total is None else total + incoming
    own = chunk_of(index)
    return own if total is None else own + total


def direct_gather_apply(block, apply, axis, count, index):
    own = apply(block)
    placed = jnp.zeros((count,) + own.shape, own.dtype)
    placed = lax.dynamic_update_index_in_dim(placed, own, index, 0)
    for shift in range(1, count):
        incoming = lax.ppermute(block, axis, [(i, (i + shift) % count) for i in range(count)])
        placed = lax.dynamic_update_index_in_dim(
            placed, apply(incoming), (index - shift) % count, 0
        )
    return placed


def exchange_sum(parts, axis, count, index):
    total = lax.dynamic_index_in_dim(parts, index, axis=0, keepdims=False).astype(jnp.float32)
    for shift in range(1, count):
        outgoing = lax.dynamic_index_in_dim(parts, (index + shift) % count, axis=0, keepdims=False)
        incoming = lax.ppermute(outgoing, axis, [(i, (i + shift) % count) for i in range(count)])
        total = total + incoming.astype(jnp.float32)
    return total.astype(jnp.bfloat16)


def attend_kernel(q_ref, k_ref, v_ref, o_ref, *, per_kv, head_dim, token_count):
    padded_tokens = k_ref.shape[0]
    split = (token_count // 128) * 128
    keys = k_ref[...]
    rows = q_ref.shape[0]
    score_scale = head_dim ** (-0.5)
    for g in range(per_kv):
        query = q_ref[:, g * head_dim:(g + 1) * head_dim]
        scores = lax.dot_general(
            query, keys, (((1,), (1,)), ((), ())), preferred_element_type=jnp.float32
        ) * score_scale
        pieces = [scores[:, :split]] if split else []
        if split < padded_tokens:
            tail = scores[:, split:]
            valid = lax.broadcasted_iota(jnp.int32, tail.shape, 1) < token_count - split
            pieces.append(jnp.where(valid, tail, -jnp.inf))
        peak = jnp.max(pieces[0], axis=1, keepdims=True)
        for piece in pieces[1:]:
            peak = jnp.maximum(peak, jnp.max(piece, axis=1, keepdims=True))
        weights = [jnp.exp(piece - peak) for piece in pieces]
        total = sum(jnp.sum(w, axis=1, keepdims=True) for w in weights)
        inverse = 1.0 / total
        mixed = None
        start = 0
        for w in weights:
            width = w.shape[1]
            probs = (w * inverse).astype(jnp.bfloat16)
            term = jnp.dot(
                probs, v_ref[start:start + width, :], preferred_element_type=jnp.float32
            )
            mixed = term if mixed is None else mixed + term
            start += width
        o_ref[:, g * head_dim:(g + 1) * head_dim] = mixed.astype(o_ref.dtype)


def attend(rows_in, keys, values, kv_count, per_kv, head_dim, token_count):
    rows, width = rows_in.shape
    padded_tokens = keys.shape[0]
    group_width = per_kv * head_dim
    kernel = functools.partial(
        attend_kernel, per_kv=per_kv, head_dim=head_dim, token_count=token_count
    )
    flops = 4 * rows * padded_tokens * head_dim * per_kv * kv_count
    moved = 2 * (2 * rows * width + 2 * padded_tokens * head_dim * kv_count)
    return pl.pallas_call(
        kernel,
        grid=(kv_count,),
        in_specs=[
            pl.BlockSpec((rows, group_width), lambda k: (0, k)),
            pl.BlockSpec((padded_tokens, head_dim), lambda k: (0, k)),
            pl.BlockSpec((padded_tokens, head_dim), lambda k: (0, k)),
        ],
        out_specs=pl.BlockSpec((rows, group_width), lambda k: (0, k)),
        out_shape=jax.ShapeDtypeStruct((rows, width), jnp.bfloat16),
        cost_estimate=pl.CostEstimate(
            flops=flops,
            transcendentals=rows * padded_tokens * per_kv * kv_count,
            bytes_accessed=moved,
        ),
    )(rows_in, keys, values)


def local(
    hidden_in,
    q_weight,
    q_gain,
    key_cache,
    value_cache,
    out_weight,
    req_image,
    image_count,
    image_home,
):
    req_count = lax.axis_size("req")
    local_rows = hidden_in.shape[0]
    q_cols = q_weight.shape[1]
    head_dim = q_gain.shape[0]
    group_size = HQ // KVH
    heads_here = q_cols // head_dim
    sub_count = lax.axis_size("sub")
    sub_index = lax.axis_index("sub")
    block_width = hidden_in.shape[1] // req_count
    part_width = block_width // sub_count
    by_block = hidden_in.reshape(local_rows, req_count, sub_count, part_width)
    req_index = lax.axis_index("req")
    my_part = lax.dynamic_index_in_dim(by_block, sub_index, axis=2, keepdims=False)
    spread_part = jnp.zeros((req_count, local_rows, part_width), my_part.dtype)
    spread_part = lax.dynamic_update_index_in_dim(
        spread_part, lax.dynamic_index_in_dim(my_part, req_index, 1, keepdims=False), req_index, 0
    )
    for shift in range(1, req_count):
        outgoing_part = lax.dynamic_index_in_dim(
            my_part, (req_index + shift) % req_count, 1, keepdims=False
        )
        arrived_part = lax.ppermute(
            outgoing_part, "req", [(i, (i + shift) % req_count) for i in range(req_count)]
        )
        spread_part = lax.dynamic_update_index_in_dim(
            spread_part, arrived_part, (req_index - shift) % req_count, 0
        )
    spread_part = spread_part.reshape(req_count * local_rows, part_width)
    spread_cols = jnp.zeros((req_count * local_rows, block_width), spread_part.dtype)
    spread_cols = lax.dynamic_update_slice_in_dim(
        spread_cols, spread_part, sub_index * part_width, 1
    )
    for shift in range(1, sub_count):
        other_part = lax.ppermute(
            spread_part, "sub", [(i, (i + shift) % sub_count) for i in range(sub_count)]
        )
        spread_cols = lax.dynamic_update_slice_in_dim(
            spread_cols, other_part, ((sub_index - shift) % sub_count) * part_width, 1
        )
    def query_chunk(owner):
        rows = lax.dynamic_slice_in_dim(spread_cols, owner * local_rows, local_rows, 0)
        product = jnp.dot(rows, q_weight, preferred_element_type=jnp.float32)
        return product.astype(jnp.bfloat16).astype(jnp.float32)

    query_sum = direct_reduce_scatter(query_chunk, "req", req_count, req_index)
    queries = lax.optimization_barrier(query_sum.astype(jnp.bfloat16))
    normalized = normalize_heads(queries, q_gain, head_dim)
    capacity = 2 * local_rows // req_count
    slot_total = req_count * capacity
    table_ids = lax.broadcasted_iota(jnp.int32, (local_rows, image_home.shape[0]), 1)
    home_rows = jnp.sum(jnp.where(req_image[:, None] == table_ids, image_home[None, :], 0), axis=1)
    wanted = image_count == 1
    dest_ids = lax.broadcasted_iota(jnp.int32, (local_rows, req_count), 1)
    to_dest = ((home_rows[:, None] == dest_ids) & wanted[:, None]).astype(jnp.int32)
    earlier = jnp.cumsum(to_dest, axis=0) - to_dest
    position = ((home_rows - req_index) % req_count) * capacity + jnp.sum(
        earlier * to_dest, axis=1
    )
    slot_ids = lax.broadcasted_iota(jnp.int32, (slot_total, local_rows), 0)
    dispatch = ((slot_ids == position[None, :]) & wanted[None, :]).astype(jnp.bfloat16)
    outgoing = jnp.dot(dispatch, normalized, preferred_element_type=jnp.float32).astype(
        jnp.bfloat16
    )
    outgoing = outgoing.reshape(req_count, capacity, q_cols)
    kv_count = max(1, heads_here // group_size)
    per_kv = heads_here // kv_count
    kv_first = sub_index * heads_here // group_size
    token_count = key_cache.shape[1]
    padded_tokens = -(-token_count // 128) * 128
    keys_here = jnp.pad(
        lax.dynamic_slice_in_dim(key_cache[0], kv_first * head_dim, kv_count * head_dim, 1),
        ((0, padded_tokens - token_count), (0, 0)),
    )
    values_here = jnp.pad(
        lax.dynamic_slice_in_dim(value_cache[0], kv_first * head_dim, kv_count * head_dim, 1),
        ((0, padded_tokens - token_count), (0, 0)),
    )
    returned_blocks = []
    for shift in range(req_count):
        if shift == 0:
            arrived_block = outgoing[0]
        else:
            arrived_block = lax.ppermute(
                outgoing[shift], "req", [(i, (i + shift) % req_count) for i in range(req_count)]
            )
        mixed_block = attend(
            arrived_block, keys_here, values_here, kv_count, per_kv, head_dim, token_count
        )
        if shift:
            mixed_block = lax.ppermute(
                mixed_block, "req", [(i, (i - shift) % req_count) for i in range(req_count)]
            )
        returned_blocks.append(mixed_block)
    returned = jnp.stack(returned_blocks)
    attended = lax.dot_general(
        dispatch,
        returned.reshape(slot_total, q_cols),
        (((0,), (0,)), ((), ())),
        preferred_element_type=jnp.float32,
    ).astype(jnp.bfloat16)
    def out_part(rows):
        product = jnp.dot(rows, out_weight, preferred_element_type=jnp.float32)
        return product.astype(jnp.bfloat16)

    partial_cols = direct_gather_apply(attended, out_part, "req", req_count, req_index)
    partial_cols = partial_cols.reshape(req_count * local_rows, out_weight.shape[1])
    hs_count = lax.axis_size("head") * sub_count
    hs_index = lax.axis_index("head") * sub_count + sub_index
    head_count = lax.axis_size("head")
    by_group = partial_cols.reshape(sub_count, -1, partial_cols.shape[1])
    sub_sums = exchange_sum(by_group, "sub", sub_count, sub_index)
    per_hs = req_count // hs_count
    out_block = partial_cols.shape[1]
    sub_sums = sub_sums.reshape(head_count, per_hs, local_rows, out_block)
    head_index = lax.axis_index("head")
    head_total = jnp.zeros((local_rows, per_hs * out_block), jnp.float32)
    for step in range(per_hs):
        gathered = None
        for turn in range(head_count):
            group = (head_index + turn) % head_count
            chunk = lax.dynamic_index_in_dim(sub_sums, group, 0, keepdims=False)
            chunk = lax.dynamic_index_in_dim(
                chunk, (req_index + step) % per_hs, 0, keepdims=False
            )
            pairs = []
            for c in range(req_count):
                for h in range(head_count):
                    for u in range(sub_count):
                        g = (h + turn) % head_count
                        k = (u * head_count + g) * per_hs + (c + step) % per_hs
                        src = c * hs_count + h * sub_count + u
                        pairs.append((src, k * hs_count + c // per_hs))
            got = lax.ppermute(chunk, ("req", "head", "sub"), pairs).astype(jnp.float32)
            gathered = got if gathered is None else gathered + got
        head_total = lax.dynamic_update_slice_in_dim(
            head_total, gathered, ((req_index % per_hs - step) % per_hs) * out_block, 1
        )
    head_total = head_total.astype(jnp.float32)
    out_width = head_total.shape[1]
    residual = lax.dynamic_slice_in_dim(hidden_in, hs_index * out_width, out_width, 1)
    return (residual.astype(jnp.float32) + head_total).astype(jnp.bfloat16)


def solution(mesh):
    in_specs = (
        P(("groups", "req"), None),
        P("req", ("head", "sub")),
        P(),
        P(("groups", "req"), None, "head"),
        P(("groups", "req"), None, "head"),
        P(("head", "sub"), "req"),
        P(("groups", "req")),
        P(("groups", "req")),
        P("groups"),
    )
    out_specs = P(("groups", "req"), ("head", "sub"))
    return jax.shard_map(local, mesh=mesh, in_specs=in_specs, out_specs=out_specs, check_vma=False)
```

```python
import functools

import jax
import jax.numpy as jnp
from jax import lax
from jax.sharding import PartitionSpec as P
from jax.experimental import pallas as pl

HQ = 64
KVH = 8


def normalize_heads(queries, q_gain, head_dim):
    row_count = queries.shape[0]
    per_head = queries.astype(jnp.float32).reshape(row_count, -1, head_dim)
    inv_rms = lax.rsqrt(jnp.mean(per_head * per_head, axis=2, keepdims=True) + 1e-05)
    return (per_head * inv_rms * q_gain).reshape(row_count, -1).astype(jnp.bfloat16)


def direct_reduce_scatter(chunk_of, axis, count, index):
    total = None
    for shift in range(1, count):
        outgoing = chunk_of((index + shift) % count).astype(jnp.bfloat16)
        incoming = lax.ppermute(outgoing, axis, [(i, (i + shift) % count) for i in range(count)])
        incoming = incoming.astype(jnp.float32)
        total = incoming if total is None else total + incoming
    own = chunk_of(index)
    return own if total is None else own + total


def direct_gather_apply(block, apply, axis, count, index):
    own = apply(block)
    placed = jnp.zeros((count,) + own.shape, own.dtype)
    placed = lax.dynamic_update_index_in_dim(placed, own, index, 0)
    for shift in range(1, count):
        incoming = lax.ppermute(block, axis, [(i, (i + shift) % count) for i in range(count)])
        placed = lax.dynamic_update_index_in_dim(
            placed, apply(incoming), (index - shift) % count, 0
        )
    return placed


def exchange_sum(parts, axis, count, index):
    total = lax.dynamic_index_in_dim(parts, index, axis=0, keepdims=False).astype(jnp.float32)
    for shift in range(1, count):
        outgoing = lax.dynamic_index_in_dim(parts, (index + shift) % count, axis=0, keepdims=False)
        incoming = lax.ppermute(outgoing, axis, [(i, (i + shift) % count) for i in range(count)])
        total = total + incoming.astype(jnp.float32)
    return total.astype(jnp.bfloat16)


def attend_kernel(q_ref, k_ref, v_ref, o_ref, *, head_dim, token_count):
    padded_tokens = k_ref.shape[1]
    split = (token_count // 128) * 128
    scores = lax.dot_general(
        q_ref[0], k_ref[0], (((1,), (1,)), ((), ())), preferred_element_type=jnp.float32
    ) * (head_dim ** (-0.5))
    pieces = [scores[:, :split]] if split else []
    if split < padded_tokens:
        tail = scores[:, split:]
        valid = lax.broadcasted_iota(jnp.int32, tail.shape, 1) < token_count - split
        pieces.append(jnp.where(valid, tail, -jnp.inf))
    peak = jnp.max(pieces[0], axis=1, keepdims=True)
    for piece in pieces[1:]:
        peak = jnp.maximum(peak, jnp.max(piece, axis=1, keepdims=True))
    weights = [jnp.exp(piece - peak) for piece in pieces]
    total = sum(jnp.sum(w, axis=1, keepdims=True) for w in weights)
    inverse = 1.0 / total
    mixed = None
    start = 0
    for w in weights:
        width = w.shape[1]
        probs = (w * inverse).astype(jnp.bfloat16)
        term = jnp.dot(probs, v_ref[0, start:start + width, :], preferred_element_type=jnp.float32)
        mixed = term if mixed is None else mixed + term
        start += width
    o_ref[0] = mixed.astype(o_ref.dtype)


def attend(rows_in, keys, values, kv_count, per_kv, head_dim, token_count):
    rows, width = rows_in.shape
    padded_tokens = keys.shape[1]
    stacked = rows_in.reshape(rows, kv_count, per_kv, head_dim).transpose(1, 2, 0, 3)
    stacked = stacked.reshape(kv_count, per_kv * rows, head_dim)
    kernel = functools.partial(attend_kernel, head_dim=head_dim, token_count=token_count)
    flops = 4 * rows * padded_tokens * head_dim * per_kv * kv_count
    moved = 2 * (2 * rows * width + 2 * padded_tokens * head_dim * kv_count)
    mixed = pl.pallas_call(
        kernel,
        grid=(kv_count,),
        in_specs=[
            pl.BlockSpec((1, per_kv * rows, head_dim), lambda k: (k, 0, 0)),
            pl.BlockSpec((1, padded_tokens, head_dim), lambda k: (k, 0, 0)),
            pl.BlockSpec((1, padded_tokens, head_dim), lambda k: (k, 0, 0)),
        ],
        out_specs=pl.BlockSpec((1, per_kv * rows, head_dim), lambda k: (k, 0, 0)),
        out_shape=jax.ShapeDtypeStruct((kv_count, per_kv * rows, head_dim), jnp.bfloat16),
        cost_estimate=pl.CostEstimate(
            flops=flops,
            transcendentals=rows * padded_tokens * per_kv * kv_count,
            bytes_accessed=moved,
        ),
    )(stacked, keys, values)
    mixed = mixed.reshape(kv_count, per_kv, rows, head_dim).transpose(2, 0, 1, 3)
    return mixed.reshape(rows, width)


def local(
    hidden_in,
    q_weight,
    q_gain,
    key_cache,
    value_cache,
    out_weight,
    req_image,
    image_count,
    image_home,
):
    req_count = lax.axis_size("req")
    local_rows = hidden_in.shape[0]
    q_cols = q_weight.shape[1]
    head_dim = q_gain.shape[0]
    group_size = HQ // KVH
    heads_here = q_cols // head_dim
    sub_count = lax.axis_size("sub")
    sub_index = lax.axis_index("sub")
    block_width = hidden_in.shape[1] // req_count
    part_width = block_width // sub_count
    by_block = hidden_in.reshape(local_rows, req_count, sub_count, part_width)
    req_index = lax.axis_index("req")
    my_part = lax.dynamic_index_in_dim(by_block, sub_index, axis=2, keepdims=False)
    spread_part = jnp.zeros((req_count, local_rows, part_width), my_part.dtype)
    spread_part = lax.dynamic_update_index_in_dim(
        spread_part, lax.dynamic_index_in_dim(my_part, req_index, 1, keepdims=False), req_index, 0
    )
    for shift in range(1, req_count):
        outgoing_part = lax.dynamic_index_in_dim(
            my_part, (req_index + shift) % req_count, 1, keepdims=False
        )
        arrived_part = lax.ppermute(
            outgoing_part, "req", [(i, (i + shift) % req_count) for i in range(req_count)]
        )
        spread_part = lax.dynamic_update_index_in_dim(
            spread_part, arrived_part, (req_index - shift) % req_count, 0
        )
    spread_part = spread_part.reshape(req_count * local_rows, part_width)
    spread_cols = jnp.zeros((req_count * local_rows, block_width), spread_part.dtype)
    spread_cols = lax.dynamic_update_slice_in_dim(
        spread_cols, spread_part, sub_index * part_width, 1
    )
    for shift in range(1, sub_count):
        other_part = lax.ppermute(
            spread_part, "sub", [(i, (i + shift) % sub_count) for i in range(sub_count)]
        )
        spread_cols = lax.dynamic_update_slice_in_dim(
            spread_cols, other_part, ((sub_index - shift) % sub_count) * part_width, 1
        )
    def query_chunk(owner):
        rows = lax.dynamic_slice_in_dim(spread_cols, owner * local_rows, local_rows, 0)
        product = jnp.dot(rows, q_weight, preferred_element_type=jnp.float32)
        return product.astype(jnp.bfloat16).astype(jnp.float32)

    query_sum = direct_reduce_scatter(query_chunk, "req", req_count, req_index)
    queries = lax.optimization_barrier(query_sum.astype(jnp.bfloat16))
    normalized = normalize_heads(queries, q_gain, head_dim)
    capacity = 2 * local_rows // req_count
    slot_total = req_count * capacity
    table_ids = lax.broadcasted_iota(jnp.int32, (local_rows, image_home.shape[0]), 1)
    home_rows = jnp.sum(jnp.where(req_image[:, None] == table_ids, image_home[None, :], 0), axis=1)
    wanted = image_count == 1
    dest_ids = lax.broadcasted_iota(jnp.int32, (local_rows, req_count), 1)
    to_dest = ((home_rows[:, None] == dest_ids) & wanted[:, None]).astype(jnp.int32)
    earlier = jnp.cumsum(to_dest, axis=0) - to_dest
    position = ((home_rows - req_index) % req_count) * capacity + jnp.sum(
        earlier * to_dest, axis=1
    )
    slot_ids = lax.broadcasted_iota(jnp.int32, (slot_total, local_rows), 0)
    dispatch = ((slot_ids == position[None, :]) & wanted[None, :]).astype(jnp.bfloat16)
    outgoing = jnp.dot(dispatch, normalized, preferred_element_type=jnp.float32).astype(
        jnp.bfloat16
    )
    outgoing = outgoing.reshape(req_count, capacity, q_cols)
    kv_count = max(1, heads_here // group_size)
    per_kv = heads_here // kv_count
    kv_first = sub_index * heads_here // group_size
    token_count = key_cache.shape[1]
    padded_tokens = -(-token_count // 128) * 128
    def group_major(cache):
        picked = lax.dynamic_slice_in_dim(cache[0], kv_first * head_dim, kv_count * head_dim, 1)
        picked = jnp.pad(picked, ((0, padded_tokens - token_count), (0, 0)))
        return picked.reshape(padded_tokens, kv_count, head_dim).transpose(1, 0, 2)

    keys_here = group_major(key_cache)
    values_here = group_major(value_cache)
    returned_blocks = []
    for shift in range(req_count):
        if shift == 0:
            arrived_block = outgoing[0]
        else:
            arrived_block = lax.ppermute(
                outgoing[shift], "req", [(i, (i + shift) % req_count) for i in range(req_count)]
            )
        mixed_block = attend(
            arrived_block, keys_here, values_here, kv_count, per_kv, head_dim, token_count
        )
        if shift:
            mixed_block = lax.ppermute(
                mixed_block, "req", [(i, (i - shift) % req_count) for i in range(req_count)]
            )
        returned_blocks.append(mixed_block)
    returned = jnp.stack(returned_blocks)
    attended = lax.dot_general(
        dispatch,
        returned.reshape(slot_total, q_cols),
        (((0,), (0,)), ((), ())),
        preferred_element_type=jnp.float32,
    ).astype(jnp.bfloat16)
    def out_part(rows):
        product = jnp.dot(rows, out_weight, preferred_element_type=jnp.float32)
        return product.astype(jnp.bfloat16)

    partial_cols = direct_gather_apply(attended, out_part, "req", req_count, req_index)
    partial_cols = partial_cols.reshape(req_count * local_rows, out_weight.shape[1])
    hs_count = lax.axis_size("head") * sub_count
    hs_index = lax.axis_index("head") * sub_count + sub_index
    head_count = lax.axis_size("head")
    by_group = partial_cols.reshape(sub_count, -1, partial_cols.shape[1])
    sub_sums = exchange_sum(by_group, "sub", sub_count, sub_index)
    per_hs = req_count // hs_count
    out_block = partial_cols.shape[1]
    sub_sums = sub_sums.reshape(head_count, per_hs, local_rows, out_block)
    head_index = lax.axis_index("head")
    head_total = jnp.zeros((local_rows, per_hs * out_block), jnp.float32)
    for step in range(per_hs):
        gathered = None
        for turn in range(head_count):
            group = (head_index + turn) % head_count
            chunk = lax.dynamic_index_in_dim(sub_sums, group, 0, keepdims=False)
            chunk = lax.dynamic_index_in_dim(
                chunk, (req_index + step) % per_hs, 0, keepdims=False
            )
            pairs = []
            for c in range(req_count):
                for h in range(head_count):
                    for u in range(sub_count):
                        g = (h + turn) % head_count
                        k = (u * head_count + g) * per_hs + (c + step) % per_hs
                        src = c * hs_count + h * sub_count + u
                        pairs.append((src, k * hs_count + c // per_hs))
            got = lax.ppermute(chunk, ("req", "head", "sub"), pairs).astype(jnp.float32)
            gathered = got if gathered is None else gathered + got
        head_total = lax.dynamic_update_slice_in_dim(
            head_total, gathered, ((req_index % per_hs - step) % per_hs) * out_block, 1
        )
    head_total = head_total.astype(jnp.float32)
    out_width = head_total.shape[1]
    residual = lax.dynamic_slice_in_dim(hidden_in, hs_index * out_width, out_width, 1)
    return (residual.astype(jnp.float32) + head_total).astype(jnp.bfloat16)


def solution(mesh):
    in_specs = (
        P(("groups", "req"), None),
        P("req", ("head", "sub")),
        P(),
        P(("groups", "req"), None, "head"),
        P(("groups", "req"), None, "head"),
        P(("head", "sub"), "req"),
        P(("groups", "req")),
        P(("groups", "req")),
        P("groups"),
    )
    out_specs = P(("groups", "req"), ("head", "sub"))
    return jax.shard_map(local, mesh=mesh, in_specs=in_specs, out_specs=out_specs, check_vma=False)
```

```python
import functools

import jax
import jax.numpy as jnp
from jax import lax
from jax.sharding import PartitionSpec as P
from jax.experimental import pallas as pl

HQ = 64
KVH = 8


def normalize_heads(queries, q_gain, head_dim):
    row_count = queries.shape[0]
    per_head = queries.astype(jnp.float32).reshape(row_count, -1, head_dim)
    inv_rms = lax.rsqrt(jnp.mean(per_head * per_head, axis=2, keepdims=True) + 1e-05)
    return (per_head * inv_rms * q_gain).reshape(row_count, -1).astype(jnp.bfloat16)


def direct_reduce_scatter(chunk_of, axis, count, index):
    total = None
    for shift in range(1, count):
        outgoing = chunk_of((index + shift) % count).astype(jnp.bfloat16)
        incoming = lax.ppermute(outgoing, axis, [(i, (i + shift) % count) for i in range(count)])
        incoming = incoming.astype(jnp.float32)
        total = incoming if total is None else total + incoming
    own = chunk_of(index)
    return own if total is None else own + total


def direct_gather_apply(block, apply, axis, count, index):
    own = apply(block)
    placed = jnp.zeros((count,) + own.shape, own.dtype)
    placed = lax.dynamic_update_index_in_dim(placed, own, index, 0)
    for shift in range(1, count):
        incoming = lax.ppermute(block, axis, [(i, (i + shift) % count) for i in range(count)])
        placed = lax.dynamic_update_index_in_dim(
            placed, apply(incoming), (index - shift) % count, 0
        )
    return placed


def exchange_sum(parts, axis, count, index):
    total = lax.dynamic_index_in_dim(parts, index, axis=0, keepdims=False).astype(jnp.float32)
    for shift in range(1, count):
        outgoing = lax.dynamic_index_in_dim(parts, (index + shift) % count, axis=0, keepdims=False)
        incoming = lax.ppermute(outgoing, axis, [(i, (i + shift) % count) for i in range(count)])
        total = total + incoming.astype(jnp.float32)
    return total.astype(jnp.bfloat16)


def attend_kernel(q_ref, k_ref, v_ref, o_ref, *, per_kv, head_dim, token_count):
    padded_tokens = k_ref.shape[1]
    split = (token_count // 128) * 128
    keys = k_ref[0]
    score_scale = head_dim ** (-0.5)
    for g in range(per_kv):
        query = q_ref[:, g * head_dim:(g + 1) * head_dim]
        scores = lax.dot_general(
            query, keys, (((1,), (1,)), ((), ())), preferred_element_type=jnp.float32
        ) * score_scale
        pieces = [scores[:, :split]] if split else []
        if split < padded_tokens:
            tail = scores[:, split:]
            valid = lax.broadcasted_iota(jnp.int32, tail.shape, 1) < token_count - split
            pieces.append(jnp.where(valid, tail, -jnp.inf))
        peak = jnp.max(pieces[0], axis=1, keepdims=True)
        for piece in pieces[1:]:
            peak = jnp.maximum(peak, jnp.max(piece, axis=1, keepdims=True))
        weights = [jnp.exp(piece - peak) for piece in pieces]
        total = sum(jnp.sum(w, axis=1, keepdims=True) for w in weights)
        inverse = 1.0 / total
        mixed = None
        start = 0
        for w in weights:
            width = w.shape[1]
            probs = (w * inverse).astype(jnp.bfloat16)
            term = jnp.dot(
                probs, v_ref[0, start:start + width, :], preferred_element_type=jnp.float32
            )
            mixed = term if mixed is None else mixed + term
            start += width
        o_ref[:, g * head_dim:(g + 1) * head_dim] = mixed.astype(o_ref.dtype)


def attend(rows_in, keys, values, kv_count, per_kv, head_dim, token_count):
    rows, width = rows_in.shape
    padded_tokens = keys.shape[1]
    group_width = per_kv * head_dim
    kernel = functools.partial(
        attend_kernel, per_kv=per_kv, head_dim=head_dim, token_count=token_count
    )
    flops = 4 * rows * padded_tokens * head_dim * per_kv * kv_count
    moved = 2 * (2 * rows * width + 2 * padded_tokens * head_dim * kv_count)
    return pl.pallas_call(
        kernel,
        grid=(kv_count,),
        in_specs=[
            pl.BlockSpec((rows, group_width), lambda k: (0, k)),
            pl.BlockSpec((1, padded_tokens, head_dim), lambda k: (k, 0, 0)),
            pl.BlockSpec((1, padded_tokens, head_dim), lambda k: (k, 0, 0)),
        ],
        out_specs=pl.BlockSpec((rows, group_width), lambda k: (0, k)),
        out_shape=jax.ShapeDtypeStruct((rows, width), jnp.bfloat16),
        cost_estimate=pl.CostEstimate(
            flops=flops,
            transcendentals=rows * padded_tokens * per_kv * kv_count,
            bytes_accessed=moved,
        ),
    )(rows_in, keys, values)


def local(
    hidden_in,
    q_weight,
    q_gain,
    key_cache,
    value_cache,
    out_weight,
    req_image,
    image_count,
    image_home,
):
    req_count = lax.axis_size("req")
    local_rows = hidden_in.shape[0]
    q_cols = q_weight.shape[1]
    head_dim = q_gain.shape[0]
    group_size = HQ // KVH
    heads_here = q_cols // head_dim
    sub_count = lax.axis_size("sub")
    sub_index = lax.axis_index("sub")
    block_width = hidden_in.shape[1] // req_count
    part_width = block_width // sub_count
    by_block = hidden_in.reshape(local_rows, req_count, sub_count, part_width)
    req_index = lax.axis_index("req")
    my_part = lax.dynamic_index_in_dim(by_block, sub_index, axis=2, keepdims=False)
    spread_part = jnp.zeros((req_count, local_rows, part_width), my_part.dtype)
    spread_part = lax.dynamic_update_index_in_dim(
        spread_part, lax.dynamic_index_in_dim(my_part, req_index, 1, keepdims=False), req_index, 0
    )
    for shift in range(1, req_count):
        outgoing_part = lax.dynamic_index_in_dim(
            my_part, (req_index + shift) % req_count, 1, keepdims=False
        )
        arrived_part = lax.ppermute(
            outgoing_part, "req", [(i, (i + shift) % req_count) for i in range(req_count)]
        )
        spread_part = lax.dynamic_update_index_in_dim(
            spread_part, arrived_part, (req_index - shift) % req_count, 0
        )
    spread_part = spread_part.reshape(req_count * local_rows, part_width)
    spread_cols = jnp.zeros((req_count * local_rows, block_width), spread_part.dtype)
    spread_cols = lax.dynamic_update_slice_in_dim(
        spread_cols, spread_part, sub_index * part_width, 1
    )
    for shift in range(1, sub_count):
        other_part = lax.ppermute(
            spread_part, "sub", [(i, (i + shift) % sub_count) for i in range(sub_count)]
        )
        spread_cols = lax.dynamic_update_slice_in_dim(
            spread_cols, other_part, ((sub_index - shift) % sub_count) * part_width, 1
        )
    def query_chunk(owner):
        rows = lax.dynamic_slice_in_dim(spread_cols, owner * local_rows, local_rows, 0)
        product = jnp.dot(rows, q_weight, preferred_element_type=jnp.float32)
        return product.astype(jnp.bfloat16).astype(jnp.float32)

    query_sum = direct_reduce_scatter(query_chunk, "req", req_count, req_index)
    queries = lax.optimization_barrier(query_sum.astype(jnp.bfloat16))
    normalized = normalize_heads(queries, q_gain, head_dim)
    capacity = 2 * local_rows // req_count
    slot_total = req_count * capacity
    table_ids = lax.broadcasted_iota(jnp.int32, (local_rows, image_home.shape[0]), 1)
    home_rows = jnp.sum(jnp.where(req_image[:, None] == table_ids, image_home[None, :], 0), axis=1)
    wanted = image_count == 1
    dest_ids = lax.broadcasted_iota(jnp.int32, (local_rows, req_count), 1)
    to_dest = ((home_rows[:, None] == dest_ids) & wanted[:, None]).astype(jnp.int32)
    earlier = jnp.cumsum(to_dest, axis=0) - to_dest
    position = ((home_rows - req_index) % req_count) * capacity + jnp.sum(
        earlier * to_dest, axis=1
    )
    slot_ids = lax.broadcasted_iota(jnp.int32, (slot_total, local_rows), 0)
    dispatch = ((slot_ids == position[None, :]) & wanted[None, :]).astype(jnp.bfloat16)
    outgoing = jnp.dot(dispatch, normalized, preferred_element_type=jnp.float32).astype(
        jnp.bfloat16
    )
    outgoing = outgoing.reshape(req_count, capacity, q_cols)
    kv_count = max(1, heads_here // group_size)
    per_kv = heads_here // kv_count
    kv_first = sub_index * heads_here // group_size
    token_count = key_cache.shape[1]
    padded_tokens = -(-token_count // 128) * 128
    def group_major(cache):
        picked = lax.dynamic_slice_in_dim(cache[0], kv_first * head_dim, kv_count * head_dim, 1)
        picked = jnp.pad(picked, ((0, padded_tokens - token_count), (0, 0)))
        return picked.reshape(padded_tokens, kv_count, head_dim).transpose(1, 0, 2)

    keys_here = group_major(key_cache)
    values_here = group_major(value_cache)
    returned_blocks = []
    for shift in range(req_count):
        if shift == 0:
            arrived_block = outgoing[0]
        else:
            arrived_block = lax.ppermute(
                outgoing[shift], "req", [(i, (i + shift) % req_count) for i in range(req_count)]
            )
        mixed_block = attend(
            arrived_block, keys_here, values_here, kv_count, per_kv, head_dim, token_count
        )
        if shift:
            mixed_block = lax.ppermute(
                mixed_block, "req", [(i, (i - shift) % req_count) for i in range(req_count)]
            )
        returned_blocks.append(mixed_block)
    returned = jnp.stack(returned_blocks)
    attended = lax.dot_general(
        dispatch,
        returned.reshape(slot_total, q_cols),
        (((0,), (0,)), ((), ())),
        preferred_element_type=jnp.float32,
    ).astype(jnp.bfloat16)
    def out_part(rows):
        product = jnp.dot(rows, out_weight, preferred_element_type=jnp.float32)
        return product.astype(jnp.bfloat16)

    partial_cols = direct_gather_apply(attended, out_part, "req", req_count, req_index)
    partial_cols = partial_cols.reshape(req_count * local_rows, out_weight.shape[1])
    hs_count = lax.axis_size("head") * sub_count
    hs_index = lax.axis_index("head") * sub_count + sub_index
    head_count = lax.axis_size("head")
    by_group = partial_cols.reshape(sub_count, -1, partial_cols.shape[1])
    sub_sums = exchange_sum(by_group, "sub", sub_count, sub_index)
    per_hs = req_count // hs_count
    out_block = partial_cols.shape[1]
    sub_sums = sub_sums.reshape(head_count, per_hs, local_rows, out_block)
    head_index = lax.axis_index("head")
    head_total = jnp.zeros((local_rows, per_hs * out_block), jnp.float32)
    for step in range(per_hs):
        gathered = None
        for turn in range(head_count):
            group = (head_index + turn) % head_count
            chunk = lax.dynamic_index_in_dim(sub_sums, group, 0, keepdims=False)
            chunk = lax.dynamic_index_in_dim(
                chunk, (req_index + step) % per_hs, 0, keepdims=False
            )
            pairs = []
            for c in range(req_count):
                for h in range(head_count):
                    for u in range(sub_count):
                        g = (h + turn) % head_count
                        k = (u * head_count + g) * per_hs + (c + step) % per_hs
                        src = c * hs_count + h * sub_count + u
                        pairs.append((src, k * hs_count + c // per_hs))
            got = lax.ppermute(chunk, ("req", "head", "sub"), pairs).astype(jnp.float32)
            gathered = got if gathered is None else gathered + got
        head_total = lax.dynamic_update_slice_in_dim(
            head_total, gathered, ((req_index % per_hs - step) % per_hs) * out_block, 1
        )
    head_total = head_total.astype(jnp.float32)
    out_width = head_total.shape[1]
    residual = lax.dynamic_slice_in_dim(hidden_in, hs_index * out_width, out_width, 1)
    return (residual.astype(jnp.float32) + head_total).astype(jnp.bfloat16)


def solution(mesh):
    in_specs = (
        P(("groups", "req"), None),
        P("req", ("head", "sub")),
        P(),
        P(("groups", "req"), None, "head"),
        P(("groups", "req"), None, "head"),
        P(("head", "sub"), "req"),
        P(("groups", "req")),
        P(("groups", "req")),
        P("groups"),
    )
    out_specs = P(("groups", "req"), ("head", "sub"))
    return jax.shard_map(local, mesh=mesh, in_specs=in_specs, out_specs=out_specs, check_vma=False)
```

```python
import functools

import jax
import jax.numpy as jnp
from jax import lax
from jax.sharding import PartitionSpec as P
from jax.experimental import pallas as pl

HQ = 64
KVH = 8


def normalize_heads(queries, q_gain, head_dim):
    row_count = queries.shape[0]
    per_head = queries.astype(jnp.float32).reshape(row_count, -1, head_dim)
    inv_rms = lax.rsqrt(jnp.mean(per_head * per_head, axis=2, keepdims=True) + 1e-05)
    return (per_head * inv_rms * q_gain).reshape(row_count, -1).astype(jnp.bfloat16)


def direct_reduce_scatter(chunk_of, axis, count, index):
    total = None
    for shift in range(1, count):
        outgoing = chunk_of((index + shift) % count).astype(jnp.bfloat16)
        incoming = lax.ppermute(outgoing, axis, [(i, (i + shift) % count) for i in range(count)])
        incoming = incoming.astype(jnp.float32)
        total = incoming if total is None else total + incoming
    own = chunk_of(index)
    return own if total is None else own + total


def direct_gather_apply(block, apply, axis, count, index):
    own = apply(block)
    placed = jnp.zeros((count,) + own.shape, own.dtype)
    placed = lax.dynamic_update_index_in_dim(placed, own, index, 0)
    for shift in range(1, count):
        incoming = lax.ppermute(block, axis, [(i, (i + shift) % count) for i in range(count)])
        placed = lax.dynamic_update_index_in_dim(
            placed, apply(incoming), (index - shift) % count, 0
        )
    return placed


def exchange_sum(parts, axis, count, index):
    total = lax.dynamic_index_in_dim(parts, index, axis=0, keepdims=False).astype(jnp.float32)
    for shift in range(1, count):
        outgoing = lax.dynamic_index_in_dim(parts, (index + shift) % count, axis=0, keepdims=False)
        incoming = lax.ppermute(outgoing, axis, [(i, (i + shift) % count) for i in range(count)])
        total = total + incoming.astype(jnp.float32)
    return total.astype(jnp.bfloat16)


def attend_kernel(q_ref, k_ref, v_ref, o_ref, *, head_dim, token_count):
    padded_tokens = k_ref.shape[2]
    split = (token_count // 128) * 128
    scores = jnp.dot(q_ref[0], k_ref[0], preferred_element_type=jnp.float32) * (
        head_dim ** (-0.5)
    )
    pieces = [scores[:, :split]] if split else []
    if split < padded_tokens:
        tail = scores[:, split:]
        valid = lax.broadcasted_iota(jnp.int32, tail.shape, 1) < token_count - split
        pieces.append(jnp.where(valid, tail, -jnp.inf))
    peak = jnp.max(pieces[0], axis=1, keepdims=True)
    for piece in pieces[1:]:
        peak = jnp.maximum(peak, jnp.max(piece, axis=1, keepdims=True))
    weights = [jnp.exp(piece - peak) for piece in pieces]
    total = sum(jnp.sum(w, axis=1, keepdims=True) for w in weights)
    inverse = 1.0 / total
    mixed = None
    start = 0
    for w in weights:
        width = w.shape[1]
        probs = (w * inverse).astype(jnp.bfloat16)
        term = jnp.dot(probs, v_ref[0, start:start + width, :], preferred_element_type=jnp.float32)
        mixed = term if mixed is None else mixed + term
        start += width
    o_ref[0] = mixed.astype(o_ref.dtype)


def attend(stacked, keys_t, values, token_count):
    kv_count, stacked_rows, head_dim = stacked.shape
    padded_tokens = keys_t.shape[2]
    kernel = functools.partial(attend_kernel, head_dim=head_dim, token_count=token_count)
    flops = 4 * stacked_rows * padded_tokens * head_dim * kv_count
    moved = 2 * (2 * stacked_rows * head_dim * kv_count + 2 * padded_tokens * head_dim * kv_count)
    return pl.pallas_call(
        kernel,
        grid=(kv_count,),
        in_specs=[
            pl.BlockSpec((1, stacked_rows, head_dim), lambda k: (k, 0, 0)),
            pl.BlockSpec((1, head_dim, padded_tokens), lambda k: (k, 0, 0)),
            pl.BlockSpec((1, padded_tokens, head_dim), lambda k: (k, 0, 0)),
        ],
        out_specs=pl.BlockSpec((1, stacked_rows, head_dim), lambda k: (k, 0, 0)),
        out_shape=jax.ShapeDtypeStruct((kv_count, stacked_rows, head_dim), jnp.bfloat16),
        cost_estimate=pl.CostEstimate(
            flops=flops,
            transcendentals=stacked_rows * padded_tokens * kv_count,
            bytes_accessed=moved,
        ),
    )(stacked, keys_t, values)


def local(
    hidden_in,
    q_weight,
    q_gain,
    key_cache,
    value_cache,
    out_weight,
    req_image,
    image_count,
    image_home,
):
    req_count = lax.axis_size("req")
    local_rows = hidden_in.shape[0]
    q_cols = q_weight.shape[1]
    head_dim = q_gain.shape[0]
    group_size = HQ // KVH
    heads_here = q_cols // head_dim
    sub_count = lax.axis_size("sub")
    sub_index = lax.axis_index("sub")
    block_width = hidden_in.shape[1] // req_count
    part_width = block_width // sub_count
    by_block = hidden_in.reshape(local_rows, req_count, sub_count, part_width)
    req_index = lax.axis_index("req")
    my_part = lax.dynamic_index_in_dim(by_block, sub_index, axis=2, keepdims=False)
    spread_part = jnp.zeros((req_count, local_rows, part_width), my_part.dtype)
    spread_part = lax.dynamic_update_index_in_dim(
        spread_part, lax.dynamic_index_in_dim(my_part, req_index, 1, keepdims=False), req_index, 0
    )
    for shift in range(1, req_count):
        outgoing_part = lax.dynamic_index_in_dim(
            my_part, (req_index + shift) % req_count, 1, keepdims=False
        )
        arrived_part = lax.ppermute(
            outgoing_part, "req", [(i, (i + shift) % req_count) for i in range(req_count)]
        )
        spread_part = lax.dynamic_update_index_in_dim(
            spread_part, arrived_part, (req_index - shift) % req_count, 0
        )
    spread_part = spread_part.reshape(req_count * local_rows, part_width)
    spread_cols = jnp.zeros((req_count * local_rows, block_width), spread_part.dtype)
    spread_cols = lax.dynamic_update_slice_in_dim(
        spread_cols, spread_part, sub_index * part_width, 1
    )
    for shift in range(1, sub_count):
        other_part = lax.ppermute(
            spread_part, "sub", [(i, (i + shift) % sub_count) for i in range(sub_count)]
        )
        spread_cols = lax.dynamic_update_slice_in_dim(
            spread_cols, other_part, ((sub_index - shift) % sub_count) * part_width, 1
        )
    def query_chunk(owner):
        rows = lax.dynamic_slice_in_dim(spread_cols, owner * local_rows, local_rows, 0)
        product = jnp.dot(rows, q_weight, preferred_element_type=jnp.float32)
        return product.astype(jnp.bfloat16).astype(jnp.float32)

    query_sum = direct_reduce_scatter(query_chunk, "req", req_count, req_index)
    queries = lax.optimization_barrier(query_sum.astype(jnp.bfloat16))
    normalized = normalize_heads(queries, q_gain, head_dim)
    capacity = 2 * local_rows // req_count
    slot_total = req_count * capacity
    table_ids = lax.broadcasted_iota(jnp.int32, (local_rows, image_home.shape[0]), 1)
    home_rows = jnp.sum(jnp.where(req_image[:, None] == table_ids, image_home[None, :], 0), axis=1)
    wanted = image_count == 1
    dest_ids = lax.broadcasted_iota(jnp.int32, (local_rows, req_count), 1)
    to_dest = ((home_rows[:, None] == dest_ids) & wanted[:, None]).astype(jnp.int32)
    earlier = jnp.cumsum(to_dest, axis=0) - to_dest
    position = ((home_rows - req_index) % req_count) * capacity + jnp.sum(
        earlier * to_dest, axis=1
    )
    slot_ids = lax.broadcasted_iota(jnp.int32, (slot_total, local_rows), 0)
    dispatch = ((slot_ids == position[None, :]) & wanted[None, :]).astype(jnp.bfloat16)
    outgoing = jnp.dot(dispatch, normalized, preferred_element_type=jnp.float32).astype(
        jnp.bfloat16
    )
    kv_count = max(1, heads_here // group_size)
    per_kv = heads_here // kv_count
    outgoing = outgoing.reshape(req_count, capacity, kv_count, per_kv, head_dim)
    outgoing = outgoing.transpose(0, 2, 3, 1, 4).reshape(
        req_count, kv_count, per_kv * capacity, head_dim
    )
    kv_first = sub_index * heads_here // group_size
    token_count = key_cache.shape[1]
    padded_tokens = -(-token_count // 128) * 128
    def group_major(cache):
        picked = lax.dynamic_slice_in_dim(cache[0], kv_first * head_dim, kv_count * head_dim, 1)
        picked = jnp.pad(picked, ((0, padded_tokens - token_count), (0, 0)))
        return picked.reshape(padded_tokens, kv_count, head_dim).transpose(1, 0, 2)

    keys_here = group_major(key_cache).transpose(0, 2, 1)
    values_here = group_major(value_cache)
    returned_blocks = []
    for shift in range(req_count):
        if shift == 0:
            arrived_block = outgoing[0]
        else:
            arrived_block = lax.ppermute(
                outgoing[shift], "req", [(i, (i + shift) % req_count) for i in range(req_count)]
            )
        mixed_block = attend(arrived_block, keys_here, values_here, token_count)
        if shift:
            mixed_block = lax.ppermute(
                mixed_block, "req", [(i, (i - shift) % req_count) for i in range(req_count)]
            )
        returned_blocks.append(mixed_block)
    returned = jnp.stack(returned_blocks).reshape(
        req_count, kv_count, per_kv, capacity, head_dim
    )
    returned = returned.transpose(0, 3, 1, 2, 4)
    attended = lax.dot_general(
        dispatch,
        returned.reshape(slot_total, q_cols),
        (((0,), (0,)), ((), ())),
        preferred_element_type=jnp.float32,
    ).astype(jnp.bfloat16)
    def out_part(rows):
        product = jnp.dot(rows, out_weight, preferred_element_type=jnp.float32)
        return product.astype(jnp.bfloat16)

    partial_cols = direct_gather_apply(attended, out_part, "req", req_count, req_index)
    partial_cols = partial_cols.reshape(req_count * local_rows, out_weight.shape[1])
    hs_count = lax.axis_size("head") * sub_count
    hs_index = lax.axis_index("head") * sub_count + sub_index
    head_count = lax.axis_size("head")
    by_group = partial_cols.reshape(sub_count, -1, partial_cols.shape[1])
    sub_sums = exchange_sum(by_group, "sub", sub_count, sub_index)
    per_hs = req_count // hs_count
    out_block = partial_cols.shape[1]
    sub_sums = sub_sums.reshape(head_count, per_hs, local_rows, out_block)
    head_index = lax.axis_index("head")
    head_total = jnp.zeros((local_rows, per_hs * out_block), jnp.float32)
    for step in range(per_hs):
        gathered = None
        for turn in range(head_count):
            group = (head_index + turn) % head_count
            chunk = lax.dynamic_index_in_dim(sub_sums, group, 0, keepdims=False)
            chunk = lax.dynamic_index_in_dim(
                chunk, (req_index + step) % per_hs, 0, keepdims=False
            )
            pairs = []
            for c in range(req_count):
                for h in range(head_count):
                    for u in range(sub_count):
                        g = (h + turn) % head_count
                        k = (u * head_count + g) * per_hs + (c + step) % per_hs
                        src = c * hs_count + h * sub_count + u
                        pairs.append((src, k * hs_count + c // per_hs))
            got = lax.ppermute(chunk, ("req", "head", "sub"), pairs).astype(jnp.float32)
            gathered = got if gathered is None else gathered + got
        head_total = lax.dynamic_update_slice_in_dim(
            head_total, gathered, ((req_index % per_hs - step) % per_hs) * out_block, 1
        )
    head_total = head_total.astype(jnp.float32)
    out_width = head_total.shape[1]
    residual = lax.dynamic_slice_in_dim(hidden_in, hs_index * out_width, out_width, 1)
    return (residual.astype(jnp.float32) + head_total).astype(jnp.bfloat16)


def solution(mesh):
    in_specs = (
        P(("groups", "req"), None),
        P("req", ("head", "sub")),
        P(),
        P(("groups", "req"), None, "head"),
        P(("groups", "req"), None, "head"),
        P(("head", "sub"), "req"),
        P(("groups", "req")),
        P(("groups", "req")),
        P("groups"),
    )
    out_specs = P(("groups", "req"), ("head", "sub"))
    return jax.shard_map(local, mesh=mesh, in_specs=in_specs, out_specs=out_specs, check_vma=False)
```

```python
import functools

import jax
import jax.numpy as jnp
from jax import lax
from jax.sharding import PartitionSpec as P
from jax.experimental import pallas as pl

HQ = 64
KVH = 8


def normalize_heads(queries, q_gain, head_dim):
    row_count = queries.shape[0]
    per_head = queries.astype(jnp.float32).reshape(row_count, -1, head_dim)
    inv_rms = lax.rsqrt(jnp.mean(per_head * per_head, axis=2, keepdims=True) + 1e-05)
    return (per_head * inv_rms * q_gain).reshape(row_count, -1).astype(jnp.bfloat16)


def direct_reduce_scatter(chunk_of, axis, count, index):
    total = None
    for shift in range(1, count):
        outgoing = chunk_of((index + shift) % count).astype(jnp.bfloat16)
        incoming = lax.ppermute(outgoing, axis, [(i, (i + shift) % count) for i in range(count)])
        incoming = incoming.astype(jnp.float32)
        total = incoming if total is None else total + incoming
    own = chunk_of(index)
    return own if total is None else own + total


def direct_gather_apply(block, apply, axis, count, index):
    own = apply(block)
    placed = jnp.zeros((count,) + own.shape, own.dtype)
    placed = lax.dynamic_update_index_in_dim(placed, own, index, 0)
    for shift in range(1, count):
        incoming = lax.ppermute(block, axis, [(i, (i + shift) % count) for i in range(count)])
        placed = lax.dynamic_update_index_in_dim(
            placed, apply(incoming), (index - shift) % count, 0
        )
    return placed


def exchange_sum(parts, axis, count, index):
    total = lax.dynamic_index_in_dim(parts, index, axis=0, keepdims=False).astype(jnp.float32)
    for shift in range(1, count):
        outgoing = lax.dynamic_index_in_dim(parts, (index + shift) % count, axis=0, keepdims=False)
        incoming = lax.ppermute(outgoing, axis, [(i, (i + shift) % count) for i in range(count)])
        total = total + incoming.astype(jnp.float32)
    return total.astype(jnp.bfloat16)


def attend_kernel(q_ref, k_ref, v_ref, o_ref, *, head_dim, token_count):
    padded_tokens = k_ref.shape[1]
    split = (token_count // 128) * 128
    scores = lax.dot_general(
        q_ref[0], k_ref[0], (((1,), (1,)), ((), ())), preferred_element_type=jnp.float32
    ) * (head_dim ** (-0.5))
    pieces = [scores[:, :split]] if split else []
    if split < padded_tokens:
        tail = scores[:, split:]
        valid = lax.broadcasted_iota(jnp.int32, tail.shape, 1) < token_count - split
        pieces.append(jnp.where(valid, tail, -jnp.inf))
    peak = jnp.max(pieces[0], axis=1, keepdims=True)
    for piece in pieces[1:]:
        peak = jnp.maximum(peak, jnp.max(piece, axis=1, keepdims=True))
    weights = [jnp.exp(piece - peak) for piece in pieces]
    total = sum(jnp.sum(w, axis=1, keepdims=True) for w in weights)
    inverse = 1.0 / total
    mixed = None
    start = 0
    for w in weights:
        width = w.shape[1]
        probs = (w * inverse).astype(jnp.bfloat16)
        term = jnp.dot(probs, v_ref[0, start:start + width, :], preferred_element_type=jnp.float32)
        mixed = term if mixed is None else mixed + term
        start += width
    o_ref[0] = mixed.astype(o_ref.dtype)


def attend(rows_in, keys, values, kv_count, per_kv, head_dim, token_count):
    rows, width = rows_in.shape
    padded_tokens = keys.shape[1]
    stacked = rows_in.reshape(rows, kv_count, per_kv, head_dim).transpose(1, 2, 0, 3)
    stacked = stacked.reshape(kv_count, per_kv * rows, head_dim)
    kernel = functools.partial(attend_kernel, head_dim=head_dim, token_count=token_count)
    flops = 4 * rows * padded_tokens * head_dim * per_kv * kv_count
    moved = 2 * (2 * rows * width + 2 * padded_tokens * head_dim * kv_count)
    mixed = pl.pallas_call(
        kernel,
        grid=(kv_count,),
        in_specs=[
            pl.BlockSpec((1, per_kv * rows, head_dim), lambda k: (k, 0, 0)),
            pl.BlockSpec((1, padded_tokens, head_dim), lambda k: (k, 0, 0)),
            pl.BlockSpec((1, padded_tokens, head_dim), lambda k: (k, 0, 0)),
        ],
        out_specs=pl.BlockSpec((1, per_kv * rows, head_dim), lambda k: (k, 0, 0)),
        out_shape=jax.ShapeDtypeStruct((kv_count, per_kv * rows, head_dim), jnp.bfloat16),
        cost_estimate=pl.CostEstimate(
            flops=flops,
            transcendentals=rows * padded_tokens * per_kv * kv_count,
            bytes_accessed=moved,
        ),
    )(stacked, keys, values)
    mixed = mixed.reshape(kv_count, per_kv, rows, head_dim).transpose(2, 0, 1, 3)
    return mixed.reshape(rows, width)


def local(
    hidden_in,
    q_weight,
    q_gain,
    key_cache,
    value_cache,
    out_weight,
    req_image,
    image_count,
    image_home,
):
    req_count = lax.axis_size("req")
    local_rows = hidden_in.shape[0]
    q_cols = q_weight.shape[1]
    head_dim = q_gain.shape[0]
    group_size = HQ // KVH
    heads_here = q_cols // head_dim
    sub_count = lax.axis_size("sub")
    sub_index = lax.axis_index("sub")
    block_width = hidden_in.shape[1] // req_count
    part_width = block_width // sub_count
    by_block = hidden_in.reshape(local_rows, req_count, sub_count, part_width)
    req_index = lax.axis_index("req")
    my_part = lax.dynamic_index_in_dim(by_block, sub_index, axis=2, keepdims=False)
    spread_part = jnp.zeros((req_count, local_rows, part_width), my_part.dtype)
    spread_part = lax.dynamic_update_index_in_dim(
        spread_part, lax.dynamic_index_in_dim(my_part, req_index, 1, keepdims=False), req_index, 0
    )
    for shift in range(1, req_count):
        outgoing_part = lax.dynamic_index_in_dim(
            my_part, (req_index + shift) % req_count, 1, keepdims=False
        )
        arrived_part = lax.ppermute(
            outgoing_part, "req", [(i, (i + shift) % req_count) for i in range(req_count)]
        )
        spread_part = lax.dynamic_update_index_in_dim(
            spread_part, arrived_part, (req_index - shift) % req_count, 0
        )
    spread_part = spread_part.reshape(req_count * local_rows, part_width)
    spread_cols = jnp.zeros((req_count * local_rows, block_width), spread_part.dtype)
    spread_cols = lax.dynamic_update_slice_in_dim(
        spread_cols, spread_part, sub_index * part_width, 1
    )
    for shift in range(1, sub_count):
        other_part = lax.ppermute(
            spread_part, "sub", [(i, (i + shift) % sub_count) for i in range(sub_count)]
        )
        spread_cols = lax.dynamic_update_slice_in_dim(
            spread_cols, other_part, ((sub_index - shift) % sub_count) * part_width, 1
        )
    def query_chunk(owner):
        rows = lax.dynamic_slice_in_dim(spread_cols, owner * local_rows, local_rows, 0)
        product = jnp.dot(rows, q_weight, preferred_element_type=jnp.float32)
        return product.astype(jnp.bfloat16).astype(jnp.float32)

    query_sum = direct_reduce_scatter(query_chunk, "req", req_count, req_index)
    queries = lax.optimization_barrier(query_sum.astype(jnp.bfloat16))
    normalized = normalize_heads(queries, q_gain, head_dim)
    capacity = 2 * local_rows // req_count
    slot_total = req_count * capacity
    table_ids = lax.broadcasted_iota(jnp.int32, (local_rows, image_home.shape[0]), 1)
    home_rows = jnp.sum(jnp.where(req_image[:, None] == table_ids, image_home[None, :], 0), axis=1)
    wanted = image_count == 1
    dest_ids = lax.broadcasted_iota(jnp.int32, (local_rows, req_count), 1)
    to_dest = ((home_rows[:, None] == dest_ids) & wanted[:, None]).astype(jnp.int32)
    earlier = jnp.cumsum(to_dest, axis=0) - to_dest
    position = ((home_rows - req_index) % req_count) * capacity + jnp.sum(
        earlier * to_dest, axis=1
    )
    slot_ids = lax.broadcasted_iota(jnp.int32, (slot_total, local_rows), 0)
    dispatch = ((slot_ids == position[None, :]) & wanted[None, :]).astype(jnp.bfloat16)
    outgoing = jnp.dot(dispatch, normalized, preferred_element_type=jnp.float32).astype(
        jnp.bfloat16
    )
    outgoing = outgoing.reshape(req_count, capacity, q_cols)
    kv_count = max(1, heads_here // group_size)
    per_kv = heads_here // kv_count
    kv_first = sub_index * heads_here // group_size
    token_count = key_cache.shape[1]
    padded_tokens = -(-token_count // 128) * 128
    def group_major(cache):
        picked = lax.dynamic_slice_in_dim(cache[0], kv_first * head_dim, kv_count * head_dim, 1)
        picked = jnp.pad(picked, ((0, padded_tokens - token_count), (0, 0)))
        return picked.reshape(padded_tokens, kv_count, head_dim).transpose(1, 0, 2)

    keys_here = group_major(key_cache)
    values_here = group_major(value_cache)
    arrived_blocks = [outgoing[0]] + [
        lax.ppermute(
            outgoing[shift], "req", [(i, (i + shift) % req_count) for i in range(req_count)]
        )
        for shift in range(1, req_count)
    ]
    returned_blocks = [
        attend(outgoing[0], keys_here, values_here, kv_count, per_kv, head_dim, token_count)
    ]
    if req_count > 1:
        returned_blocks[0], arrived_blocks[1] = lax.optimization_barrier(
            (returned_blocks[0], arrived_blocks[1])
        )
    for shift in range(1, req_count):
        mixed_block = attend(
            arrived_blocks[shift], keys_here, values_here, kv_count, per_kv, head_dim, token_count
        )
        mixed_block = lax.ppermute(
            mixed_block, "req", [(i, (i - shift) % req_count) for i in range(req_count)]
        )
        returned_blocks.append(mixed_block)
    returned = jnp.stack(returned_blocks)
    attended = lax.dot_general(
        dispatch,
        returned.reshape(slot_total, q_cols),
        (((0,), (0,)), ((), ())),
        preferred_element_type=jnp.float32,
    ).astype(jnp.bfloat16)
    def out_part(rows):
        product = jnp.dot(rows, out_weight, preferred_element_type=jnp.float32)
        return product.astype(jnp.bfloat16)

    partial_cols = direct_gather_apply(attended, out_part, "req", req_count, req_index)
    partial_cols = partial_cols.reshape(req_count * local_rows, out_weight.shape[1])
    hs_count = lax.axis_size("head") * sub_count
    hs_index = lax.axis_index("head") * sub_count + sub_index
    head_count = lax.axis_size("head")
    by_group = partial_cols.reshape(sub_count, -1, partial_cols.shape[1])
    sub_sums = exchange_sum(by_group, "sub", sub_count, sub_index)
    per_hs = req_count // hs_count
    out_block = partial_cols.shape[1]
    sub_sums = sub_sums.reshape(head_count, per_hs, local_rows, out_block)
    head_index = lax.axis_index("head")
    head_total = jnp.zeros((local_rows, per_hs * out_block), jnp.float32)
    for step in range(per_hs):
        gathered = None
        for turn in range(head_count):
            group = (head_index + turn) % head_count
            chunk = lax.dynamic_index_in_dim(sub_sums, group, 0, keepdims=False)
            chunk = lax.dynamic_index_in_dim(
                chunk, (req_index + step) % per_hs, 0, keepdims=False
            )
            pairs = []
            for c in range(req_count):
                for h in range(head_count):
                    for u in range(sub_count):
                        g = (h + turn) % head_count
                        k = (u * head_count + g) * per_hs + (c + step) % per_hs
                        src = c * hs_count + h * sub_count + u
                        pairs.append((src, k * hs_count + c // per_hs))
            got = lax.ppermute(chunk, ("req", "head", "sub"), pairs).astype(jnp.float32)
            gathered = got if gathered is None else gathered + got
        head_total = lax.dynamic_update_slice_in_dim(
            head_total, gathered, ((req_index % per_hs - step) % per_hs) * out_block, 1
        )
    head_total = head_total.astype(jnp.float32)
    out_width = head_total.shape[1]
    residual = lax.dynamic_slice_in_dim(hidden_in, hs_index * out_width, out_width, 1)
    return (residual.astype(jnp.float32) + head_total).astype(jnp.bfloat16)


def solution(mesh):
    in_specs = (
        P(("groups", "req"), None),
        P("req", ("head", "sub")),
        P(),
        P(("groups", "req"), None, "head"),
        P(("groups", "req"), None, "head"),
        P(("head", "sub"), "req"),
        P(("groups", "req")),
        P(("groups", "req")),
        P("groups"),
    )
    out_specs = P(("groups", "req"), ("head", "sub"))
    return jax.shard_map(local, mesh=mesh, in_specs=in_specs, out_specs=out_specs, check_vma=False)
```

```python
import functools

import jax
import jax.numpy as jnp
from jax import lax
from jax.sharding import PartitionSpec as P
from jax.experimental import pallas as pl

HQ = 64
KVH = 8


def normalize_heads(queries, q_gain, head_dim):
    row_count = queries.shape[0]
    per_head = queries.astype(jnp.float32).reshape(row_count, -1, head_dim)
    inv_rms = lax.rsqrt(jnp.mean(per_head * per_head, axis=2, keepdims=True) + 1e-05)
    return (per_head * inv_rms * q_gain).reshape(row_count, -1).astype(jnp.bfloat16)


def direct_reduce_scatter(chunk_of, axis, count, index):
    total = None
    for shift in range(1, count):
        outgoing = chunk_of((index + shift) % count).astype(jnp.bfloat16)
        incoming = lax.ppermute(outgoing, axis, [(i, (i + shift) % count) for i in range(count)])
        incoming = incoming.astype(jnp.float32)
        total = incoming if total is None else total + incoming
    own = chunk_of(index)
    return own if total is None else own + total


def direct_gather_apply(block, apply, axis, count, index):
    own = apply(block)
    placed = jnp.zeros((count,) + own.shape, own.dtype)
    placed = lax.dynamic_update_index_in_dim(placed, own, index, 0)
    for shift in range(1, count):
        incoming = lax.ppermute(block, axis, [(i, (i + shift) % count) for i in range(count)])
        placed = lax.dynamic_update_index_in_dim(
            placed, apply(incoming), (index - shift) % count, 0
        )
    return placed


def exchange_sum(parts, axis, count, index):
    total = lax.dynamic_index_in_dim(parts, index, axis=0, keepdims=False).astype(jnp.float32)
    for shift in range(1, count):
        outgoing = lax.dynamic_index_in_dim(parts, (index + shift) % count, axis=0, keepdims=False)
        incoming = lax.ppermute(outgoing, axis, [(i, (i + shift) % count) for i in range(count)])
        total = total + incoming.astype(jnp.float32)
    return total.astype(jnp.bfloat16)


def attend_kernel(q_ref, k_ref, v_ref, o_ref, *, head_dim, token_count):
    padded_tokens = k_ref.shape[1]
    split = (token_count // 128) * 128
    scores = lax.dot_general(
        q_ref[0], k_ref[0], (((1,), (1,)), ((), ())), preferred_element_type=jnp.float32
    ) * (head_dim ** (-0.5))
    pieces = [scores[:, :split]] if split else []
    if split < padded_tokens:
        tail = scores[:, split:]
        valid = lax.broadcasted_iota(jnp.int32, tail.shape, 1) < token_count - split
        pieces.append(jnp.where(valid, tail, -jnp.inf))
    peak = jnp.max(pieces[0], axis=1, keepdims=True)
    for piece in pieces[1:]:
        peak = jnp.maximum(peak, jnp.max(piece, axis=1, keepdims=True))
    weights = [jnp.exp(piece - peak) for piece in pieces]
    total = sum(jnp.sum(w, axis=1, keepdims=True) for w in weights)
    inverse = 1.0 / total
    mixed = None
    start = 0
    for w in weights:
        width = w.shape[1]
        probs = (w * inverse).astype(jnp.bfloat16)
        term = jnp.dot(probs, v_ref[0, start:start + width, :], preferred_element_type=jnp.float32)
        mixed = term if mixed is None else mixed + term
        start += width
    o_ref[0] = mixed.astype(o_ref.dtype)


def attend(stacked, keys, values, token_count):
    kv_count, stacked_rows, head_dim = stacked.shape
    padded_tokens = keys.shape[1]
    kernel = functools.partial(attend_kernel, head_dim=head_dim, token_count=token_count)
    flops = 4 * stacked_rows * padded_tokens * head_dim * kv_count
    moved = 2 * (2 * stacked_rows * head_dim * kv_count + 2 * padded_tokens * head_dim * kv_count)
    return pl.pallas_call(
        kernel,
        grid=(kv_count,),
        in_specs=[
            pl.BlockSpec((1, stacked_rows, head_dim), lambda k: (k, 0, 0)),
            pl.BlockSpec((1, padded_tokens, head_dim), lambda k: (k, 0, 0)),
            pl.BlockSpec((1, padded_tokens, head_dim), lambda k: (k, 0, 0)),
        ],
        out_specs=pl.BlockSpec((1, stacked_rows, head_dim), lambda k: (k, 0, 0)),
        out_shape=jax.ShapeDtypeStruct((kv_count, stacked_rows, head_dim), jnp.bfloat16),
        cost_estimate=pl.CostEstimate(
            flops=flops,
            transcendentals=stacked_rows * padded_tokens * kv_count,
            bytes_accessed=moved,
        ),
    )(stacked, keys, values)


def local(
    hidden_in,
    q_weight,
    q_gain,
    key_cache,
    value_cache,
    out_weight,
    req_image,
    image_count,
    image_home,
):
    req_count = lax.axis_size("req")
    local_rows = hidden_in.shape[0]
    q_cols = q_weight.shape[1]
    head_dim = q_gain.shape[0]
    group_size = HQ // KVH
    heads_here = q_cols // head_dim
    sub_count = lax.axis_size("sub")
    sub_index = lax.axis_index("sub")
    block_width = hidden_in.shape[1] // req_count
    part_width = block_width // sub_count
    by_block = hidden_in.reshape(local_rows, req_count, sub_count, part_width)
    req_index = lax.axis_index("req")
    my_part = lax.dynamic_index_in_dim(by_block, sub_index, axis=2, keepdims=False)
    spread_part = jnp.zeros((req_count, local_rows, part_width), my_part.dtype)
    spread_part = lax.dynamic_update_index_in_dim(
        spread_part, lax.dynamic_index_in_dim(my_part, req_index, 1, keepdims=False), req_index, 0
    )
    for shift in range(1, req_count):
        outgoing_part = lax.dynamic_index_in_dim(
            my_part, (req_index + shift) % req_count, 1, keepdims=False
        )
        arrived_part = lax.ppermute(
            outgoing_part, "req", [(i, (i + shift) % req_count) for i in range(req_count)]
        )
        spread_part = lax.dynamic_update_index_in_dim(
            spread_part, arrived_part, (req_index - shift) % req_count, 0
        )
    spread_part = spread_part.reshape(req_count * local_rows, part_width)
    spread_cols = jnp.zeros((req_count * local_rows, block_width), spread_part.dtype)
    spread_cols = lax.dynamic_update_slice_in_dim(
        spread_cols, spread_part, sub_index * part_width, 1
    )
    for shift in range(1, sub_count):
        other_part = lax.ppermute(
            spread_part, "sub", [(i, (i + shift) % sub_count) for i in range(sub_count)]
        )
        spread_cols = lax.dynamic_update_slice_in_dim(
            spread_cols, other_part, ((sub_index - shift) % sub_count) * part_width, 1
        )
    def query_chunk(owner):
        rows = lax.dynamic_slice_in_dim(spread_cols, owner * local_rows, local_rows, 0)
        product = jnp.dot(rows, q_weight, preferred_element_type=jnp.float32)
        return product.astype(jnp.bfloat16).astype(jnp.float32)

    query_sum = direct_reduce_scatter(query_chunk, "req", req_count, req_index)
    queries = lax.optimization_barrier(query_sum.astype(jnp.bfloat16))
    normalized = normalize_heads(queries, q_gain, head_dim)
    capacity = 2 * local_rows // req_count
    slot_total = req_count * capacity
    table_ids = lax.broadcasted_iota(jnp.int32, (local_rows, image_home.shape[0]), 1)
    home_rows = jnp.sum(jnp.where(req_image[:, None] == table_ids, image_home[None, :], 0), axis=1)
    wanted = image_count == 1
    dest_ids = lax.broadcasted_iota(jnp.int32, (local_rows, req_count), 1)
    to_dest = ((home_rows[:, None] == dest_ids) & wanted[:, None]).astype(jnp.int32)
    earlier = jnp.cumsum(to_dest, axis=0) - to_dest
    position = ((home_rows - req_index) % req_count) * capacity + jnp.sum(
        earlier * to_dest, axis=1
    )
    slot_ids = lax.broadcasted_iota(jnp.int32, (slot_total, local_rows), 0)
    dispatch = ((slot_ids == position[None, :]) & wanted[None, :]).astype(jnp.bfloat16)
    outgoing = jnp.dot(dispatch, normalized, preferred_element_type=jnp.float32).astype(
        jnp.bfloat16
    )
    kv_count = max(1, heads_here // group_size)
    per_kv = heads_here // kv_count
    outgoing = outgoing.reshape(req_count, capacity, kv_count, per_kv, head_dim)
    outgoing = outgoing.transpose(0, 2, 3, 1, 4).reshape(
        req_count, kv_count, per_kv * capacity, head_dim
    )
    kv_first = sub_index * heads_here // group_size
    token_count = key_cache.shape[1]
    padded_tokens = -(-token_count // 128) * 128
    def group_major(cache):
        picked = lax.dynamic_slice_in_dim(cache[0], kv_first * head_dim, kv_count * head_dim, 1)
        picked = jnp.pad(picked, ((0, padded_tokens - token_count), (0, 0)))
        return picked.reshape(padded_tokens, kv_count, head_dim).transpose(1, 0, 2)

    keys_here = group_major(key_cache)
    values_here = group_major(value_cache)
    arrived_blocks = [outgoing[0]] + [
        lax.ppermute(
            outgoing[shift], "req", [(i, (i + shift) % req_count) for i in range(req_count)]
        )
        for shift in range(1, req_count)
    ]
    returned_blocks = [
        attend(outgoing[0], keys_here, values_here, token_count)
    ]
    if req_count > 1:
        returned_blocks[0], arrived_blocks[1] = lax.optimization_barrier(
            (returned_blocks[0], arrived_blocks[1])
        )
    for shift in range(1, req_count):
        mixed_block = attend(arrived_blocks[shift], keys_here, values_here, token_count)
        mixed_block = lax.ppermute(
            mixed_block, "req", [(i, (i - shift) % req_count) for i in range(req_count)]
        )
        returned_blocks.append(mixed_block)
    returned = jnp.stack(returned_blocks).reshape(
        req_count, kv_count, per_kv, capacity, head_dim
    )
    returned = returned.transpose(0, 3, 1, 2, 4)
    attended = lax.dot_general(
        dispatch,
        returned.reshape(slot_total, q_cols),
        (((0,), (0,)), ((), ())),
        preferred_element_type=jnp.float32,
    ).astype(jnp.bfloat16)
    def out_part(rows):
        product = jnp.dot(rows, out_weight, preferred_element_type=jnp.float32)
        return product.astype(jnp.bfloat16)

    partial_cols = direct_gather_apply(attended, out_part, "req", req_count, req_index)
    partial_cols = partial_cols.reshape(req_count * local_rows, out_weight.shape[1])
    hs_count = lax.axis_size("head") * sub_count
    hs_index = lax.axis_index("head") * sub_count + sub_index
    head_count = lax.axis_size("head")
    by_group = partial_cols.reshape(sub_count, -1, partial_cols.shape[1])
    sub_sums = exchange_sum(by_group, "sub", sub_count, sub_index)
    per_hs = req_count // hs_count
    out_block = partial_cols.shape[1]
    sub_sums = sub_sums.reshape(head_count, per_hs, local_rows, out_block)
    head_index = lax.axis_index("head")
    head_total = jnp.zeros((local_rows, per_hs * out_block), jnp.float32)
    for step in range(per_hs):
        gathered = None
        for turn in range(head_count):
            group = (head_index + turn) % head_count
            chunk = lax.dynamic_index_in_dim(sub_sums, group, 0, keepdims=False)
            chunk = lax.dynamic_index_in_dim(
                chunk, (req_index + step) % per_hs, 0, keepdims=False
            )
            pairs = []
            for c in range(req_count):
                for h in range(head_count):
                    for u in range(sub_count):
                        g = (h + turn) % head_count
                        k = (u * head_count + g) * per_hs + (c + step) % per_hs
                        src = c * hs_count + h * sub_count + u
                        pairs.append((src, k * hs_count + c // per_hs))
            got = lax.ppermute(chunk, ("req", "head", "sub"), pairs).astype(jnp.float32)
            gathered = got if gathered is None else gathered + got
        head_total = lax.dynamic_update_slice_in_dim(
            head_total, gathered, ((req_index % per_hs - step) % per_hs) * out_block, 1
        )
    head_total = head_total.astype(jnp.float32)
    out_width = head_total.shape[1]
    residual = lax.dynamic_slice_in_dim(hidden_in, hs_index * out_width, out_width, 1)
    return (residual.astype(jnp.float32) + head_total).astype(jnp.bfloat16)


def solution(mesh):
    in_specs = (
        P(("groups", "req"), None),
        P("req", ("head", "sub")),
        P(),
        P(("groups", "req"), None, "head"),
        P(("groups", "req"), None, "head"),
        P(("head", "sub"), "req"),
        P(("groups", "req")),
        P(("groups", "req")),
        P("groups"),
    )
    out_specs = P(("groups", "req"), ("head", "sub"))
    return jax.shard_map(local, mesh=mesh, in_specs=in_specs, out_specs=out_specs, check_vma=False)
```

```python
import functools

import jax
import jax.numpy as jnp
from jax import lax
from jax.sharding import PartitionSpec as P
from jax.experimental import pallas as pl

HQ = 64
KVH = 8


def normalize_heads(queries, q_gain, head_dim):
    row_count = queries.shape[0]
    per_head = queries.astype(jnp.float32).reshape(row_count, -1, head_dim)
    inv_rms = lax.rsqrt(jnp.mean(per_head * per_head, axis=2, keepdims=True) + 1e-05)
    return (per_head * inv_rms * q_gain).reshape(row_count, -1).astype(jnp.bfloat16)


def direct_reduce_scatter(chunk_of, axis, count, index):
    total = None
    for shift in range(1, count):
        outgoing = chunk_of((index + shift) % count).astype(jnp.bfloat16)
        incoming = lax.ppermute(outgoing, axis, [(i, (i + shift) % count) for i in range(count)])
        incoming = incoming.astype(jnp.float32)
        total = incoming if total is None else total + incoming
    own = chunk_of(index)
    return own if total is None else own + total


def direct_gather_apply(block, apply, axis, count, index):
    own = apply(block)
    placed = jnp.zeros((count,) + own.shape, own.dtype)
    placed = lax.dynamic_update_index_in_dim(placed, own, index, 0)
    for shift in range(1, count):
        incoming = lax.ppermute(block, axis, [(i, (i + shift) % count) for i in range(count)])
        placed = lax.dynamic_update_index_in_dim(
            placed, apply(incoming), (index - shift) % count, 0
        )
    return placed


def exchange_sum(parts, axis, count, index):
    total = lax.dynamic_index_in_dim(parts, index, axis=0, keepdims=False).astype(jnp.float32)
    for shift in range(1, count):
        outgoing = lax.dynamic_index_in_dim(parts, (index + shift) % count, axis=0, keepdims=False)
        incoming = lax.ppermute(outgoing, axis, [(i, (i + shift) % count) for i in range(count)])
        total = total + incoming.astype(jnp.float32)
    return total.astype(jnp.bfloat16)


def attend_kernel(q_ref, k_ref, v_ref, o_ref, *, head_dim, token_count):
    padded_tokens = k_ref.shape[1]
    split = (token_count // 128) * 128
    scores = lax.dot_general(
        q_ref[0], k_ref[0], (((1,), (1,)), ((), ())), preferred_element_type=jnp.float32
    ) * (head_dim ** (-0.5))
    pieces = [scores[:, :split]] if split else []
    if split < padded_tokens:
        tail = scores[:, split:]
        valid = lax.broadcasted_iota(jnp.int32, tail.shape, 1) < token_count - split
        pieces.append(jnp.where(valid, tail, -jnp.inf))
    peak = jnp.max(pieces[0], axis=1, keepdims=True)
    for piece in pieces[1:]:
        peak = jnp.maximum(peak, jnp.max(piece, axis=1, keepdims=True))
    weights = [jnp.exp(piece - peak) for piece in pieces]
    total = sum(jnp.sum(w, axis=1, keepdims=True) for w in weights)
    inverse = 1.0 / total
    mixed = None
    start = 0
    for w in weights:
        width = w.shape[1]
        probs = (w * inverse).astype(jnp.bfloat16)
        term = jnp.dot(probs, v_ref[0, start:start + width, :], preferred_element_type=jnp.float32)
        mixed = term if mixed is None else mixed + term
        start += width
    o_ref[0] = mixed.astype(o_ref.dtype)


def attend(stacked, keys, values, token_count):
    kv_count, stacked_rows, head_dim = stacked.shape
    padded_tokens = keys.shape[1]
    kernel = functools.partial(attend_kernel, head_dim=head_dim, token_count=token_count)
    flops = 4 * stacked_rows * padded_tokens * head_dim * kv_count
    moved = 2 * (2 * stacked_rows * head_dim * kv_count + 2 * padded_tokens * head_dim * kv_count)
    return pl.pallas_call(
        kernel,
        grid=(kv_count,),
        in_specs=[
            pl.BlockSpec((1, stacked_rows, head_dim), lambda k: (k, 0, 0)),
            pl.BlockSpec((1, padded_tokens, head_dim), lambda k: (k, 0, 0)),
            pl.BlockSpec((1, padded_tokens, head_dim), lambda k: (k, 0, 0)),
        ],
        out_specs=pl.BlockSpec((1, stacked_rows, head_dim), lambda k: (k, 0, 0)),
        out_shape=jax.ShapeDtypeStruct((kv_count, stacked_rows, head_dim), jnp.bfloat16),
        cost_estimate=pl.CostEstimate(
            flops=flops,
            transcendentals=stacked_rows * padded_tokens * kv_count,
            bytes_accessed=moved,
        ),
    )(stacked, keys, values)


def local(
    hidden_in,
    q_weight,
    q_gain,
    key_cache,
    value_cache,
    out_weight,
    req_image,
    image_count,
    image_home,
):
    req_count = lax.axis_size("req")
    local_rows = hidden_in.shape[0]
    q_cols = q_weight.shape[1]
    head_dim = q_gain.shape[0]
    group_size = HQ // KVH
    heads_here = q_cols // head_dim
    sub_count = lax.axis_size("sub")
    sub_index = lax.axis_index("sub")
    block_width = hidden_in.shape[1] // req_count
    half_rows = local_rows // sub_count
    req_index = lax.axis_index("req")
    my_rows = lax.dynamic_slice_in_dim(hidden_in, sub_index * half_rows, half_rows, 0)

    def my_block(dest):
        return lax.dynamic_slice_in_dim(my_rows, dest * block_width, block_width, 1)

    spread_part = jnp.zeros((req_count, half_rows, block_width), hidden_in.dtype)
    spread_part = lax.dynamic_update_index_in_dim(spread_part, my_block(req_index), req_index, 0)
    for shift in range(1, req_count):
        arrived_part = lax.ppermute(
            my_block((req_index + shift) % req_count),
            "req",
            [(i, (i + shift) % req_count) for i in range(req_count)],
        )
        spread_part = lax.dynamic_update_index_in_dim(
            spread_part, arrived_part, (req_index - shift) % req_count, 0
        )
    spread_cols = jnp.zeros((req_count, sub_count, half_rows, block_width), hidden_in.dtype)
    spread_cols = lax.dynamic_update_index_in_dim(spread_cols, spread_part, sub_index, 1)
    for shift in range(1, sub_count):
        other_part = lax.ppermute(
            spread_part, "sub", [(i, (i + shift) % sub_count) for i in range(sub_count)]
        )
        spread_cols = lax.dynamic_update_index_in_dim(
            spread_cols, other_part, (sub_index - shift) % sub_count, 1
        )
    spread_cols = spread_cols.reshape(req_count * local_rows, block_width)
    def query_chunk(owner):
        rows = lax.dynamic_slice_in_dim(spread_cols, owner * local_rows, local_rows, 0)
        product = jnp.dot(rows, q_weight, preferred_element_type=jnp.float32)
        return product.astype(jnp.bfloat16).astype(jnp.float32)

    query_sum = direct_reduce_scatter(query_chunk, "req", req_count, req_index)
    queries = lax.optimization_barrier(query_sum.astype(jnp.bfloat16))
    normalized = normalize_heads(queries, q_gain, head_dim)
    capacity = 2 * local_rows // req_count
    slot_total = req_count * capacity
    table_ids = lax.broadcasted_iota(jnp.int32, (local_rows, image_home.shape[0]), 1)
    home_rows = jnp.sum(jnp.where(req_image[:, None] == table_ids, image_home[None, :], 0), axis=1)
    wanted = image_count == 1
    dest_ids = lax.broadcasted_iota(jnp.int32, (local_rows, req_count), 1)
    to_dest = ((home_rows[:, None] == dest_ids) & wanted[:, None]).astype(jnp.int32)
    earlier = jnp.cumsum(to_dest, axis=0) - to_dest
    position = ((home_rows - req_index) % req_count) * capacity + jnp.sum(
        earlier * to_dest, axis=1
    )
    slot_ids = lax.broadcasted_iota(jnp.int32, (slot_total, local_rows), 0)
    dispatch = ((slot_ids == position[None, :]) & wanted[None, :]).astype(jnp.bfloat16)
    outgoing = jnp.dot(dispatch, normalized, preferred_element_type=jnp.float32).astype(
        jnp.bfloat16
    )
    kv_count = max(1, heads_here // group_size)
    per_kv = heads_here // kv_count
    outgoing = outgoing.reshape(req_count, capacity, kv_count, per_kv, head_dim)
    outgoing = outgoing.transpose(0, 2, 3, 1, 4).reshape(
        req_count, kv_count, per_kv * capacity, head_dim
    )
    kv_first = sub_index * heads_here // group_size
    token_count = key_cache.shape[1]
    padded_tokens = -(-token_count // 128) * 128
    def group_major(cache):
        picked = lax.dynamic_slice_in_dim(cache[0], kv_first * head_dim, kv_count * head_dim, 1)
        picked = jnp.pad(picked, ((0, padded_tokens - token_count), (0, 0)))
        return picked.reshape(padded_tokens, kv_count, head_dim).transpose(1, 0, 2)

    keys_here = group_major(key_cache)
    values_here = group_major(value_cache)
    arrived_blocks = [outgoing[0]] + [
        lax.ppermute(
            outgoing[shift], "req", [(i, (i + shift) % req_count) for i in range(req_count)]
        )
        for shift in range(1, req_count)
    ]
    returned_blocks = [
        attend(outgoing[0], keys_here, values_here, token_count)
    ]
    if req_count > 1:
        returned_blocks[0], arrived_blocks[1] = lax.optimization_barrier(
            (returned_blocks[0], arrived_blocks[1])
        )
    for shift in range(1, req_count):
        mixed_block = attend(arrived_blocks[shift], keys_here, values_here, token_count)
        mixed_block = lax.ppermute(
            mixed_block, "req", [(i, (i - shift) % req_count) for i in range(req_count)]
        )
        returned_blocks.append(mixed_block)
    returned = jnp.stack(returned_blocks).reshape(
        req_count, kv_count, per_kv, capacity, head_dim
    )
    returned = returned.transpose(0, 3, 1, 2, 4)
    attended = lax.dot_general(
        dispatch,
        returned.reshape(slot_total, q_cols),
        (((0,), (0,)), ((), ())),
        preferred_element_type=jnp.float32,
    ).astype(jnp.bfloat16)
    def out_part(rows):
        product = jnp.dot(rows, out_weight, preferred_element_type=jnp.float32)
        return product.astype(jnp.bfloat16)

    partial_cols = direct_gather_apply(attended, out_part, "req", req_count, req_index)
    partial_cols = partial_cols.reshape(req_count * local_rows, out_weight.shape[1])
    hs_count = lax.axis_size("head") * sub_count
    hs_index = lax.axis_index("head") * sub_count + sub_index
    head_count = lax.axis_size("head")
    by_group = partial_cols.reshape(sub_count, -1, partial_cols.shape[1])
    sub_sums = exchange_sum(by_group, "sub", sub_count, sub_index)
    per_hs = req_count // hs_count
    out_block = partial_cols.shape[1]
    sub_sums = sub_sums.reshape(head_count, per_hs, local_rows, out_block)
    head_index = lax.axis_index("head")
    head_total = jnp.zeros((local_rows, per_hs * out_block), jnp.float32)
    for step in range(per_hs):
        gathered = None
        for turn in range(head_count):
            group = (head_index + turn) % head_count
            chunk = lax.dynamic_index_in_dim(sub_sums, group, 0, keepdims=False)
            chunk = lax.dynamic_index_in_dim(
                chunk, (req_index + step) % per_hs, 0, keepdims=False
            )
            pairs = []
            for c in range(req_count):
                for h in range(head_count):
                    for u in range(sub_count):
                        g = (h + turn) % head_count
                        k = (u * head_count + g) * per_hs + (c + step) % per_hs
                        src = c * hs_count + h * sub_count + u
                        pairs.append((src, k * hs_count + c // per_hs))
            got = lax.ppermute(chunk, ("req", "head", "sub"), pairs).astype(jnp.float32)
            gathered = got if gathered is None else gathered + got
        head_total = lax.dynamic_update_slice_in_dim(
            head_total, gathered, ((req_index % per_hs - step) % per_hs) * out_block, 1
        )
    head_total = head_total.astype(jnp.float32)
    out_width = head_total.shape[1]
    residual = lax.dynamic_slice_in_dim(hidden_in, hs_index * out_width, out_width, 1)
    return (residual.astype(jnp.float32) + head_total).astype(jnp.bfloat16)


def solution(mesh):
    in_specs = (
        P(("groups", "req"), None),
        P("req", ("head", "sub")),
        P(),
        P(("groups", "req"), None, "head"),
        P(("groups", "req"), None, "head"),
        P(("head", "sub"), "req"),
        P(("groups", "req")),
        P(("groups", "req")),
        P("groups"),
    )
    out_specs = P(("groups", "req"), ("head", "sub"))
    return jax.shard_map(local, mesh=mesh, in_specs=in_specs, out_specs=out_specs, check_vma=False)
```

```python
import functools

import jax
import jax.numpy as jnp
from jax import lax
from jax.sharding import PartitionSpec as P
from jax.experimental import pallas as pl

HQ = 64
KVH = 8


def normalize_heads(queries, q_gain, head_dim):
    row_count = queries.shape[0]
    per_head = queries.astype(jnp.float32).reshape(row_count, -1, head_dim)
    inv_rms = lax.rsqrt(jnp.mean(per_head * per_head, axis=2, keepdims=True) + 1e-05)
    return (per_head * inv_rms * q_gain).reshape(row_count, -1).astype(jnp.bfloat16)


def direct_gather_apply(block, apply, axis, count, index):
    own = apply(block)
    placed = jnp.zeros((count,) + own.shape, own.dtype)
    placed = lax.dynamic_update_index_in_dim(placed, own, index, 0)
    for shift in range(1, count):
        incoming = lax.ppermute(block, axis, [(i, (i + shift) % count) for i in range(count)])
        placed = lax.dynamic_update_index_in_dim(
            placed, apply(incoming), (index - shift) % count, 0
        )
    return placed


def exchange_sum(parts, axis, count, index):
    total = lax.dynamic_index_in_dim(parts, index, axis=0, keepdims=False).astype(jnp.float32)
    for shift in range(1, count):
        outgoing = lax.dynamic_index_in_dim(parts, (index + shift) % count, axis=0, keepdims=False)
        incoming = lax.ppermute(outgoing, axis, [(i, (i + shift) % count) for i in range(count)])
        total = total + incoming.astype(jnp.float32)
    return total.astype(jnp.bfloat16)


def attend_kernel(q_ref, k_ref, v_ref, o_ref, *, head_dim, token_count):
    padded_tokens = k_ref.shape[1]
    split = (token_count // 128) * 128
    scores = lax.dot_general(
        q_ref[0], k_ref[0], (((1,), (1,)), ((), ())), preferred_element_type=jnp.float32
    ) * (head_dim ** (-0.5))
    pieces = [scores[:, :split]] if split else []
    if split < padded_tokens:
        tail = scores[:, split:]
        valid = lax.broadcasted_iota(jnp.int32, tail.shape, 1) < token_count - split
        pieces.append(jnp.where(valid, tail, -jnp.inf))
    peak = jnp.max(pieces[0], axis=1, keepdims=True)
    for piece in pieces[1:]:
        peak = jnp.maximum(peak, jnp.max(piece, axis=1, keepdims=True))
    weights = [jnp.exp(piece - peak) for piece in pieces]
    total = sum(jnp.sum(w, axis=1, keepdims=True) for w in weights)
    inverse = 1.0 / total
    mixed = None
    start = 0
    for w in weights:
        width = w.shape[1]
        probs = (w * inverse).astype(jnp.bfloat16)
        term = jnp.dot(probs, v_ref[0, start:start + width, :], preferred_element_type=jnp.float32)
        mixed = term if mixed is None else mixed + term
        start += width
    o_ref[0] = mixed.astype(o_ref.dtype)


def attend(stacked, keys, values, token_count):
    kv_count, stacked_rows, head_dim = stacked.shape
    padded_tokens = keys.shape[1]
    kernel = functools.partial(attend_kernel, head_dim=head_dim, token_count=token_count)
    flops = 4 * stacked_rows * padded_tokens * head_dim * kv_count
    moved = 2 * (2 * stacked_rows * head_dim * kv_count + 2 * padded_tokens * head_dim * kv_count)
    return pl.pallas_call(
        kernel,
        grid=(kv_count,),
        in_specs=[
            pl.BlockSpec((1, stacked_rows, head_dim), lambda k: (k, 0, 0)),
            pl.BlockSpec((1, padded_tokens, head_dim), lambda k: (k, 0, 0)),
            pl.BlockSpec((1, padded_tokens, head_dim), lambda k: (k, 0, 0)),
        ],
        out_specs=pl.BlockSpec((1, stacked_rows, head_dim), lambda k: (k, 0, 0)),
        out_shape=jax.ShapeDtypeStruct((kv_count, stacked_rows, head_dim), jnp.bfloat16),
        cost_estimate=pl.CostEstimate(
            flops=flops,
            transcendentals=stacked_rows * padded_tokens * kv_count,
            bytes_accessed=moved,
        ),
    )(stacked, keys, values)


def local(
    hidden_in,
    q_weight,
    q_gain,
    key_cache,
    value_cache,
    out_weight,
    req_image,
    image_count,
    image_home,
):
    req_count = lax.axis_size("req")
    local_rows = hidden_in.shape[0]
    q_cols = q_weight.shape[1]
    head_dim = q_gain.shape[0]
    group_size = HQ // KVH
    heads_here = q_cols // head_dim
    sub_count = lax.axis_size("sub")
    sub_index = lax.axis_index("sub")
    block_width = hidden_in.shape[1] // req_count
    half_rows = local_rows // sub_count
    req_index = lax.axis_index("req")
    my_rows = lax.dynamic_slice_in_dim(hidden_in, sub_index * half_rows, half_rows, 0)

    def my_block(dest):
        return lax.dynamic_slice_in_dim(my_rows, dest * block_width, block_width, 1)

    arrived = [my_block(req_index)]
    for shift in range(1, req_count):
        arrived.append(
            lax.ppermute(
                my_block((req_index + shift) % req_count),
                "req",
                [(i, (i + shift) % req_count) for i in range(req_count)],
            )
        )

    def source_rows(h):
        whole = jnp.zeros((sub_count, half_rows, block_width), hidden_in.dtype)
        whole = lax.dynamic_update_index_in_dim(whole, arrived[h], sub_index, 0)
        for shift in range(1, sub_count):
            other = lax.ppermute(
                arrived[h], "sub", [(i, (i + shift) % sub_count) for i in range(sub_count)]
            )
            whole = lax.dynamic_update_index_in_dim(
                whole, other, (sub_index - shift) % sub_count, 0
            )
        return whole.reshape(local_rows, block_width)

    def query_chunk(shift):
        rows = source_rows((req_count - shift) % req_count)
        product = jnp.dot(rows, q_weight, preferred_element_type=jnp.float32)
        return product.astype(jnp.bfloat16).astype(jnp.float32)

    query_sum = query_chunk(0)
    for shift in range(1, req_count):
        incoming = lax.ppermute(
            query_chunk(shift).astype(jnp.bfloat16),
            "req",
            [(i, (i + shift) % req_count) for i in range(req_count)],
        )
        query_sum = query_sum + incoming.astype(jnp.float32)
    queries = lax.optimization_barrier(query_sum.astype(jnp.bfloat16))
    normalized = normalize_heads(queries, q_gain, head_dim)
    capacity = 2 * local_rows // req_count
    slot_total = req_count * capacity
    table_ids = lax.broadcasted_iota(jnp.int32, (local_rows, image_home.shape[0]), 1)
    home_rows = jnp.sum(jnp.where(req_image[:, None] == table_ids, image_home[None, :], 0), axis=1)
    wanted = image_count == 1
    dest_ids = lax.broadcasted_iota(jnp.int32, (local_rows, req_count), 1)
    to_dest = ((home_rows[:, None] == dest_ids) & wanted[:, None]).astype(jnp.int32)
    earlier = jnp.cumsum(to_dest, axis=0) - to_dest
    position = ((home_rows - req_index) % req_count) * capacity + jnp.sum(
        earlier * to_dest, axis=1
    )
    slot_ids = lax.broadcasted_iota(jnp.int32, (slot_total, local_rows), 0)
    dispatch = ((slot_ids == position[None, :]) & wanted[None, :]).astype(jnp.bfloat16)
    outgoing = jnp.dot(dispatch, normalized, preferred_element_type=jnp.float32).astype(
        jnp.bfloat16
    )
    kv_count = max(1, heads_here // group_size)
    per_kv = heads_here // kv_count
    outgoing = outgoing.reshape(req_count, capacity, kv_count, per_kv, head_dim)
    outgoing = outgoing.transpose(0, 2, 3, 1, 4).reshape(
        req_count, kv_count, per_kv * capacity, head_dim
    )
    kv_first = sub_index * heads_here // group_size
    token_count = key_cache.shape[1]
    padded_tokens = -(-token_count // 128) * 128
    def group_major(cache):
        picked = lax.dynamic_slice_in_dim(cache[0], kv_first * head_dim, kv_count * head_dim, 1)
        picked = jnp.pad(picked, ((0, padded_tokens - token_count), (0, 0)))
        return picked.reshape(padded_tokens, kv_count, head_dim).transpose(1, 0, 2)

    keys_here = group_major(key_cache)
    values_here = group_major(value_cache)
    arrived_blocks = [outgoing[0]] + [
        lax.ppermute(
            outgoing[shift], "req", [(i, (i + shift) % req_count) for i in range(req_count)]
        )
        for shift in range(1, req_count)
    ]
    returned_blocks = [
        attend(outgoing[0], keys_here, values_here, token_count)
    ]
    if req_count > 1:
        returned_blocks[0], arrived_blocks[1] = lax.optimization_barrier(
            (returned_blocks[0], arrived_blocks[1])
        )
    for shift in range(1, req_count):
        mixed_block = attend(arrived_blocks[shift], keys_here, values_here, token_count)
        mixed_block = lax.ppermute(
            mixed_block, "req", [(i, (i - shift) % req_count) for i in range(req_count)]
        )
        returned_blocks.append(mixed_block)
    returned = jnp.stack(returned_blocks).reshape(
        req_count, kv_count, per_kv, capacity, head_dim
    )
    returned = returned.transpose(0, 3, 1, 2, 4)
    attended = lax.dot_general(
        dispatch,
        returned.reshape(slot_total, q_cols),
        (((0,), (0,)), ((), ())),
        preferred_element_type=jnp.float32,
    ).astype(jnp.bfloat16)
    def out_part(rows):
        product = jnp.dot(rows, out_weight, preferred_element_type=jnp.float32)
        return product.astype(jnp.bfloat16)

    partial_cols = direct_gather_apply(attended, out_part, "req", req_count, req_index)
    partial_cols = partial_cols.reshape(req_count * local_rows, out_weight.shape[1])
    hs_count = lax.axis_size("head") * sub_count
    hs_index = lax.axis_index("head") * sub_count + sub_index
    head_count = lax.axis_size("head")
    by_group = partial_cols.reshape(sub_count, -1, partial_cols.shape[1])
    sub_sums = exchange_sum(by_group, "sub", sub_count, sub_index)
    per_hs = req_count // hs_count
    out_block = partial_cols.shape[1]
    sub_sums = sub_sums.reshape(head_count, per_hs, local_rows, out_block)
    head_index = lax.axis_index("head")
    head_total = jnp.zeros((local_rows, per_hs * out_block), jnp.float32)
    for step in range(per_hs):
        gathered = None
        for turn in range(head_count):
            group = (head_index + turn) % head_count
            chunk = lax.dynamic_index_in_dim(sub_sums, group, 0, keepdims=False)
            chunk = lax.dynamic_index_in_dim(
                chunk, (req_index + step) % per_hs, 0, keepdims=False
            )
            pairs = []
            for c in range(req_count):
                for h in range(head_count):
                    for u in range(sub_count):
                        g = (h + turn) % head_count
                        k = (u * head_count + g) * per_hs + (c + step) % per_hs
                        src = c * hs_count + h * sub_count + u
                        pairs.append((src, k * hs_count + c // per_hs))
            got = lax.ppermute(chunk, ("req", "head", "sub"), pairs).astype(jnp.float32)
            gathered = got if gathered is None else gathered + got
        head_total = lax.dynamic_update_slice_in_dim(
            head_total, gathered, ((req_index % per_hs - step) % per_hs) * out_block, 1
        )
    head_total = head_total.astype(jnp.float32)
    out_width = head_total.shape[1]
    residual = lax.dynamic_slice_in_dim(hidden_in, hs_index * out_width, out_width, 1)
    return (residual.astype(jnp.float32) + head_total).astype(jnp.bfloat16)


def solution(mesh):
    in_specs = (
        P(("groups", "req"), None),
        P("req", ("head", "sub")),
        P(),
        P(("groups", "req"), None, "head"),
        P(("groups", "req"), None, "head"),
        P(("head", "sub"), "req"),
        P(("groups", "req")),
        P(("groups", "req")),
        P("groups"),
    )
    out_specs = P(("groups", "req"), ("head", "sub"))
    return jax.shard_map(local, mesh=mesh, in_specs=in_specs, out_specs=out_specs, check_vma=False)
```

```python
import functools

import jax
import jax.numpy as jnp
from jax import lax
from jax.sharding import PartitionSpec as P
from jax.experimental import pallas as pl

HQ = 64
KVH = 8


def normalize_heads(queries, q_gain, head_dim):
    row_count = queries.shape[0]
    per_head = queries.astype(jnp.float32).reshape(row_count, -1, head_dim)
    inv_rms = lax.rsqrt(jnp.mean(per_head * per_head, axis=2, keepdims=True) + 1e-05)
    return (per_head * inv_rms * q_gain).reshape(row_count, -1).astype(jnp.bfloat16)


def direct_reduce_scatter(chunk_of, axis, count, index):
    total = None
    for shift in range(1, count):
        outgoing = chunk_of((index + shift) % count).astype(jnp.bfloat16)
        incoming = lax.ppermute(outgoing, axis, [(i, (i + shift) % count) for i in range(count)])
        incoming = incoming.astype(jnp.float32)
        total = incoming if total is None else total + incoming
    own = chunk_of(index)
    return own if total is None else own + total


def direct_gather_apply(block, apply, axis, count, index):
    own = apply(block)
    placed = jnp.zeros((count,) + own.shape, own.dtype)
    placed = lax.dynamic_update_index_in_dim(placed, own, index, 0)
    for shift in range(1, count):
        incoming = lax.ppermute(block, axis, [(i, (i + shift) % count) for i in range(count)])
        placed = lax.dynamic_update_index_in_dim(
            placed, apply(incoming), (index - shift) % count, 0
        )
    return placed


def exchange_sum(parts, axis, count, index):
    total = lax.dynamic_index_in_dim(parts, index, axis=0, keepdims=False).astype(jnp.float32)
    for shift in range(1, count):
        outgoing = lax.dynamic_index_in_dim(parts, (index + shift) % count, axis=0, keepdims=False)
        incoming = lax.ppermute(outgoing, axis, [(i, (i + shift) % count) for i in range(count)])
        total = total + incoming.astype(jnp.float32)
    return total.astype(jnp.bfloat16)


def attend_kernel(q_ref, k_ref, v_ref, o_ref, *, head_dim, token_count):
    padded_tokens = k_ref.shape[1]
    split = (token_count // 128) * 128
    scores = lax.dot_general(
        q_ref[0], k_ref[0], (((1,), (1,)), ((), ())), preferred_element_type=jnp.float32
    ) * (head_dim ** (-0.5))
    pieces = [scores[:, :split]] if split else []
    if split < padded_tokens:
        tail = scores[:, split:]
        valid = lax.broadcasted_iota(jnp.int32, tail.shape, 1) < token_count - split
        pieces.append(jnp.where(valid, tail, -jnp.inf))
    peak = jnp.max(pieces[0], axis=1, keepdims=True)
    for piece in pieces[1:]:
        peak = jnp.maximum(peak, jnp.max(piece, axis=1, keepdims=True))
    weights = [jnp.exp(piece - peak) for piece in pieces]
    total = sum(jnp.sum(w, axis=1, keepdims=True) for w in weights)
    inverse = 1.0 / total
    mixed = None
    start = 0
    for w in weights:
        width = w.shape[1]
        probs = (w * inverse).astype(jnp.bfloat16)
        term = jnp.dot(probs, v_ref[0, start:start + width, :], preferred_element_type=jnp.float32)
        mixed = term if mixed is None else mixed + term
        start += width
    o_ref[0] = mixed.astype(o_ref.dtype)


def attend(stacked, keys, values, token_count):
    kv_count, stacked_rows, head_dim = stacked.shape
    padded_tokens = keys.shape[1]
    kernel = functools.partial(attend_kernel, head_dim=head_dim, token_count=token_count)
    flops = 4 * stacked_rows * padded_tokens * head_dim * kv_count
    moved = 2 * (2 * stacked_rows * head_dim * kv_count + 2 * padded_tokens * head_dim * kv_count)
    return pl.pallas_call(
        kernel,
        grid=(kv_count,),
        in_specs=[
            pl.BlockSpec((1, stacked_rows, head_dim), lambda k: (k, 0, 0)),
            pl.BlockSpec((1, padded_tokens, head_dim), lambda k: (k, 0, 0)),
            pl.BlockSpec((1, padded_tokens, head_dim), lambda k: (k, 0, 0)),
        ],
        out_specs=pl.BlockSpec((1, stacked_rows, head_dim), lambda k: (k, 0, 0)),
        out_shape=jax.ShapeDtypeStruct((kv_count, stacked_rows, head_dim), jnp.bfloat16),
        cost_estimate=pl.CostEstimate(
            flops=flops,
            transcendentals=stacked_rows * padded_tokens * kv_count,
            bytes_accessed=moved,
        ),
    )(stacked, keys, values)


def local(
    hidden_in,
    q_weight,
    q_gain,
    key_cache,
    value_cache,
    out_weight,
    req_image,
    image_count,
    image_home,
):
    req_count = lax.axis_size("req")
    local_rows = hidden_in.shape[0]
    q_cols = q_weight.shape[1]
    head_dim = q_gain.shape[0]
    group_size = HQ // KVH
    heads_here = q_cols // head_dim
    sub_count = lax.axis_size("sub")
    sub_index = lax.axis_index("sub")
    block_width = hidden_in.shape[1] // req_count
    half_rows = local_rows // sub_count
    req_index = lax.axis_index("req")
    my_rows = lax.dynamic_slice_in_dim(hidden_in, sub_index * half_rows, half_rows, 0)

    def my_block(dest):
        return lax.dynamic_slice_in_dim(my_rows, dest * block_width, block_width, 1)

    spread_part = jnp.zeros((req_count, half_rows, block_width), hidden_in.dtype)
    spread_part = lax.dynamic_update_index_in_dim(spread_part, my_block(req_index), req_index, 0)
    for shift in range(1, req_count):
        arrived_part = lax.ppermute(
            my_block((req_index + shift) % req_count),
            "req",
            [(i, (i + shift) % req_count) for i in range(req_count)],
        )
        spread_part = lax.dynamic_update_index_in_dim(
            spread_part, arrived_part, (req_index - shift) % req_count, 0
        )
    spread_cols = jnp.zeros((req_count, sub_count, half_rows, block_width), hidden_in.dtype)
    spread_cols = lax.dynamic_update_index_in_dim(spread_cols, spread_part, sub_index, 1)
    for shift in range(1, sub_count):
        other_part = lax.ppermute(
            spread_part, "sub", [(i, (i + shift) % sub_count) for i in range(sub_count)]
        )
        spread_cols = lax.dynamic_update_index_in_dim(
            spread_cols, other_part, (sub_index - shift) % sub_count, 1
        )
    spread_cols = spread_cols.reshape(req_count * local_rows, block_width)
    def query_chunk(owner):
        rows = lax.dynamic_slice_in_dim(spread_cols, owner * local_rows, local_rows, 0)
        product = jnp.dot(rows, q_weight, preferred_element_type=jnp.float32)
        return product.astype(jnp.bfloat16).astype(jnp.float32)

    query_sum = direct_reduce_scatter(query_chunk, "req", req_count, req_index)
    queries = lax.optimization_barrier(query_sum.astype(jnp.bfloat16))
    normalized = normalize_heads(queries, q_gain, head_dim)
    capacity = 2 * local_rows // req_count
    slot_total = req_count * capacity
    table_ids = lax.broadcasted_iota(jnp.int32, (local_rows, image_home.shape[0]), 1)
    home_rows = jnp.sum(jnp.where(req_image[:, None] == table_ids, image_home[None, :], 0), axis=1)
    wanted = image_count == 1
    dest_ids = lax.broadcasted_iota(jnp.int32, (local_rows, req_count), 1)
    to_dest = ((home_rows[:, None] == dest_ids) & wanted[:, None]).astype(jnp.int32)
    earlier = jnp.cumsum(to_dest, axis=0) - to_dest
    position = ((home_rows - req_index) % req_count) * capacity + jnp.sum(
        earlier * to_dest, axis=1
    )
    slot_ids = lax.broadcasted_iota(jnp.int32, (slot_total, local_rows), 0)
    dispatch = ((slot_ids == position[None, :]) & wanted[None, :]).astype(jnp.bfloat16)
    outgoing = jnp.dot(dispatch, normalized, preferred_element_type=jnp.float32).astype(
        jnp.bfloat16
    )
    kv_count = max(1, heads_here // group_size)
    per_kv = heads_here // kv_count
    outgoing = outgoing.reshape(req_count, capacity, kv_count, per_kv, head_dim)
    outgoing = outgoing.transpose(0, 2, 3, 1, 4).reshape(
        req_count, kv_count, per_kv * capacity, head_dim
    )
    kv_first = sub_index * heads_here // group_size
    token_count = key_cache.shape[1]
    padded_tokens = -(-token_count // 128) * 128
    def group_major(cache):
        picked = lax.dynamic_slice_in_dim(cache[0], kv_first * head_dim, kv_count * head_dim, 1)
        picked = jnp.pad(picked, ((0, padded_tokens - token_count), (0, 0)))
        return picked.reshape(padded_tokens, kv_count, head_dim).transpose(1, 0, 2)

    keys_here = group_major(key_cache)
    values_here = group_major(value_cache)
    arrived_blocks = [outgoing[0]] + [
        lax.ppermute(
            outgoing[shift], "req", [(i, (i + shift) % req_count) for i in range(req_count)]
        )
        for shift in range(1, req_count)
    ]
    returned_blocks = [
        attend(outgoing[0], keys_here, values_here, token_count)
    ]
    if req_count > 1:
        returned_blocks[0], arrived_blocks[1] = lax.optimization_barrier(
            (returned_blocks[0], arrived_blocks[1])
        )
    for shift in range(1, req_count):
        mixed_block = attend(arrived_blocks[shift], keys_here, values_here, token_count)
        mixed_block = lax.ppermute(
            mixed_block, "req", [(i, (i - shift) % req_count) for i in range(req_count)]
        )
        returned_blocks.append(mixed_block)
    returned = jnp.stack(returned_blocks).reshape(
        req_count, kv_count, per_kv, capacity, head_dim
    )
    returned = returned.transpose(0, 3, 1, 2, 4)
    attended = lax.dot_general(
        dispatch,
        returned.reshape(slot_total, q_cols),
        (((0,), (0,)), ((), ())),
        preferred_element_type=jnp.float32,
    ).astype(jnp.bfloat16)
    def out_part(rows):
        product = jnp.dot(rows, out_weight, preferred_element_type=jnp.float32)
        return product.astype(jnp.bfloat16)

    partial_cols = direct_gather_apply(attended, out_part, "req", req_count, req_index)
    partial_cols = partial_cols.reshape(req_count * local_rows, out_weight.shape[1])
    hs_count = lax.axis_size("head") * sub_count
    hs_index = lax.axis_index("head") * sub_count + sub_index
    head_count = lax.axis_size("head")
    by_group = partial_cols.reshape(sub_count, -1, partial_cols.shape[1])
    owner_sums = exchange_sum(by_group, "sub", sub_count, sub_index)
    owner_sums = owner_sums.reshape(head_count, -1, partial_cols.shape[1])
    owner_sums = exchange_sum(owner_sums, "head", head_count, lax.axis_index("head"))
    per_hs = req_count // hs_count
    out_block = partial_cols.shape[1]
    owner_sums = owner_sums.reshape(per_hs, local_rows, out_block)
    head_total = jnp.zeros((local_rows, per_hs * out_block), jnp.float32)
    for step in range(per_hs):
        chunk = lax.dynamic_index_in_dim(
            owner_sums, (req_index + step) % per_hs, axis=0, keepdims=False
        )
        pairs = []
        for c in range(req_count):
            for h in range(head_count):
                for u in range(sub_count):
                    j = u * head_count + h
                    k = j * per_hs + (c + step) % per_hs
                    src = c * hs_count + h * sub_count + u
                    pairs.append((src, k * hs_count + c // per_hs))
        got = lax.ppermute(chunk, ("req", "head", "sub"), pairs).astype(jnp.float32)
        head_total = lax.dynamic_update_slice_in_dim(
            head_total, got, ((req_index % per_hs - step) % per_hs) * out_block, 1
        )
    head_total = head_total.astype(jnp.float32)
    out_width = head_total.shape[1]
    residual = lax.dynamic_slice_in_dim(hidden_in, hs_index * out_width, out_width, 1)
    return (residual.astype(jnp.float32) + head_total).astype(jnp.bfloat16)


def solution(mesh):
    in_specs = (
        P(("groups", "req"), None),
        P("req", ("head", "sub")),
        P(),
        P(("groups", "req"), None, "head"),
        P(("groups", "req"), None, "head"),
        P(("head", "sub"), "req"),
        P(("groups", "req")),
        P(("groups", "req")),
        P("groups"),
    )
    out_specs = P(("groups", "req"), ("head", "sub"))
    return jax.shard_map(local, mesh=mesh, in_specs=in_specs, out_specs=out_specs, check_vma=False)
```

```python
import functools

import jax
import jax.numpy as jnp
from jax import lax
from jax.sharding import PartitionSpec as P
from jax.experimental import pallas as pl

HQ = 64
KVH = 8


def normalize_heads(queries, q_gain, head_dim):
    row_count = queries.shape[0]
    per_head = queries.astype(jnp.float32).reshape(row_count, -1, head_dim)
    inv_rms = lax.rsqrt(jnp.mean(per_head * per_head, axis=2, keepdims=True) + 1e-05)
    return (per_head * inv_rms * q_gain).reshape(row_count, -1).astype(jnp.bfloat16)


def direct_reduce_scatter(chunk_of, axis, count, index):
    total = None
    for shift in range(1, count):
        outgoing = chunk_of((index + shift) % count).astype(jnp.bfloat16)
        incoming = lax.ppermute(outgoing, axis, [(i, (i + shift) % count) for i in range(count)])
        incoming = incoming.astype(jnp.float32)
        total = incoming if total is None else total + incoming
    own = chunk_of(index)
    return own if total is None else own + total


def direct_gather_apply(block, apply, axis, count, index):
    own = apply(block)
    placed = jnp.zeros((count,) + own.shape, own.dtype)
    placed = lax.dynamic_update_index_in_dim(placed, own, index, 0)
    for shift in range(1, count):
        incoming = lax.ppermute(block, axis, [(i, (i + shift) % count) for i in range(count)])
        placed = lax.dynamic_update_index_in_dim(
            placed, apply(incoming), (index - shift) % count, 0
        )
    return placed


def exchange_sum(parts, axis, count, index):
    total = lax.dynamic_index_in_dim(parts, index, axis=0, keepdims=False).astype(jnp.float32)
    for shift in range(1, count):
        outgoing = lax.dynamic_index_in_dim(parts, (index + shift) % count, axis=0, keepdims=False)
        incoming = lax.ppermute(outgoing, axis, [(i, (i + shift) % count) for i in range(count)])
        total = total + incoming.astype(jnp.float32)
    return total.astype(jnp.bfloat16)


def attend_kernel(q_ref, k_ref, v_ref, o_ref, *, head_dim, token_count):
    padded_tokens = k_ref.shape[1]
    split = (token_count // 128) * 128
    scores = lax.dot_general(
        q_ref[0], k_ref[0], (((1,), (1,)), ((), ())), preferred_element_type=jnp.float32
    ) * (head_dim ** (-0.5))
    pieces = [scores[:, :split]] if split else []
    if split < padded_tokens:
        tail = scores[:, split:]
        valid = lax.broadcasted_iota(jnp.int32, tail.shape, 1) < token_count - split
        pieces.append(jnp.where(valid, tail, -jnp.inf))
    peak = jnp.max(pieces[0], axis=1, keepdims=True)
    for piece in pieces[1:]:
        peak = jnp.maximum(peak, jnp.max(piece, axis=1, keepdims=True))
    weights = [jnp.exp(piece - peak) for piece in pieces]
    total = sum(jnp.sum(w, axis=1, keepdims=True) for w in weights)
    inverse = 1.0 / total
    mixed = None
    start = 0
    for w in weights:
        width = w.shape[1]
        probs = (w * inverse).astype(jnp.bfloat16)
        term = jnp.dot(probs, v_ref[0, start:start + width, :], preferred_element_type=jnp.float32)
        mixed = term if mixed is None else mixed + term
        start += width
    o_ref[0] = mixed.astype(o_ref.dtype)


def attend(stacked, keys, values, token_count):
    kv_count, stacked_rows, head_dim = stacked.shape
    padded_tokens = keys.shape[1]
    kernel = functools.partial(attend_kernel, head_dim=head_dim, token_count=token_count)
    flops = 4 * stacked_rows * padded_tokens * head_dim * kv_count
    moved = 2 * (2 * stacked_rows * head_dim * kv_count + 2 * padded_tokens * head_dim * kv_count)
    return pl.pallas_call(
        kernel,
        grid=(kv_count,),
        in_specs=[
            pl.BlockSpec((1, stacked_rows, head_dim), lambda k: (k, 0, 0)),
            pl.BlockSpec((1, padded_tokens, head_dim), lambda k: (k, 0, 0)),
            pl.BlockSpec((1, padded_tokens, head_dim), lambda k: (k, 0, 0)),
        ],
        out_specs=pl.BlockSpec((1, stacked_rows, head_dim), lambda k: (k, 0, 0)),
        out_shape=jax.ShapeDtypeStruct((kv_count, stacked_rows, head_dim), jnp.bfloat16),
        cost_estimate=pl.CostEstimate(
            flops=flops,
            transcendentals=stacked_rows * padded_tokens * kv_count,
            bytes_accessed=moved,
        ),
    )(stacked, keys, values)


def local(
    hidden_in,
    q_weight,
    q_gain,
    key_cache,
    value_cache,
    out_weight,
    req_image,
    image_count,
    image_home,
):
    req_count = lax.axis_size("req")
    local_rows = hidden_in.shape[0]
    q_cols = q_weight.shape[1]
    head_dim = q_gain.shape[0]
    group_size = HQ // KVH
    heads_here = q_cols // head_dim
    sub_count = lax.axis_size("sub")
    sub_index = lax.axis_index("sub")
    block_width = hidden_in.shape[1] // req_count
    half_rows = local_rows // sub_count
    req_index = lax.axis_index("req")
    my_rows = lax.dynamic_slice_in_dim(hidden_in, sub_index * half_rows, half_rows, 0)

    def my_block(dest):
        return lax.dynamic_slice_in_dim(my_rows, dest * block_width, block_width, 1)

    spread_part = jnp.zeros((req_count, half_rows, block_width), hidden_in.dtype)
    spread_part = lax.dynamic_update_index_in_dim(spread_part, my_block(req_index), req_index, 0)
    for shift in range(1, req_count):
        arrived_part = lax.ppermute(
            my_block((req_index + shift) % req_count),
            "req",
            [(i, (i + shift) % req_count) for i in range(req_count)],
        )
        spread_part = lax.dynamic_update_index_in_dim(
            spread_part, arrived_part, (req_index - shift) % req_count, 0
        )
    spread_cols = jnp.zeros((req_count, sub_count, half_rows, block_width), hidden_in.dtype)
    spread_cols = lax.dynamic_update_index_in_dim(spread_cols, spread_part, sub_index, 1)
    for shift in range(1, sub_count):
        other_part = lax.ppermute(
            spread_part, "sub", [(i, (i + shift) % sub_count) for i in range(sub_count)]
        )
        spread_cols = lax.dynamic_update_index_in_dim(
            spread_cols, other_part, (sub_index - shift) % sub_count, 1
        )
    spread_cols = spread_cols.reshape(req_count * local_rows, block_width)
    def query_chunk(owner):
        rows = lax.dynamic_slice_in_dim(spread_cols, owner * local_rows, local_rows, 0)
        product = jnp.dot(rows, q_weight, preferred_element_type=jnp.float32)
        return product.astype(jnp.bfloat16).astype(jnp.float32)

    query_sum = direct_reduce_scatter(query_chunk, "req", req_count, req_index)
    queries = lax.optimization_barrier(query_sum.astype(jnp.bfloat16))
    normalized = normalize_heads(queries, q_gain, head_dim)
    capacity = 2 * local_rows // req_count
    slot_total = req_count * capacity
    table_ids = lax.broadcasted_iota(jnp.int32, (local_rows, image_home.shape[0]), 1)
    home_rows = jnp.sum(jnp.where(req_image[:, None] == table_ids, image_home[None, :], 0), axis=1)
    wanted = image_count == 1
    dest_ids = lax.broadcasted_iota(jnp.int32, (local_rows, req_count), 1)
    to_dest = ((home_rows[:, None] == dest_ids) & wanted[:, None]).astype(jnp.int32)
    earlier = jnp.cumsum(to_dest, axis=0) - to_dest
    position = ((home_rows - req_index) % req_count) * capacity + jnp.sum(
        earlier * to_dest, axis=1
    )
    slot_ids = lax.broadcasted_iota(jnp.int32, (slot_total, local_rows), 0)
    dispatch = ((slot_ids == position[None, :]) & wanted[None, :]).astype(jnp.bfloat16)
    outgoing = jnp.dot(dispatch, normalized, preferred_element_type=jnp.float32).astype(
        jnp.bfloat16
    )
    kv_count = max(1, heads_here // group_size)
    per_kv = heads_here // kv_count
    outgoing = outgoing.reshape(req_count, capacity, kv_count, per_kv, head_dim)
    outgoing = outgoing.transpose(0, 2, 3, 1, 4).reshape(
        req_count, kv_count, per_kv * capacity, head_dim
    )
    kv_first = sub_index * heads_here // group_size
    token_count = key_cache.shape[1]
    padded_tokens = -(-token_count // 128) * 128
    def group_major(cache):
        picked = lax.dynamic_slice_in_dim(cache[0], kv_first * head_dim, kv_count * head_dim, 1)
        picked = jnp.pad(picked, ((0, padded_tokens - token_count), (0, 0)))
        return picked.reshape(padded_tokens, kv_count, head_dim).transpose(1, 0, 2)

    keys_here = group_major(key_cache)
    values_here = group_major(value_cache)
    arrived_blocks = [outgoing[0]] + [
        lax.ppermute(
            outgoing[shift], "req", [(i, (i + shift) % req_count) for i in range(req_count)]
        )
        for shift in range(1, req_count)
    ]
    returned_blocks = [
        attend(outgoing[0], keys_here, values_here, token_count)
    ]
    if req_count > 1:
        returned_blocks[0], arrived_blocks[1] = lax.optimization_barrier(
            (returned_blocks[0], arrived_blocks[1])
        )
    for shift in range(1, req_count):
        mixed_block = attend(arrived_blocks[shift], keys_here, values_here, token_count)
        mixed_block = lax.ppermute(
            mixed_block, "req", [(i, (i - shift) % req_count) for i in range(req_count)]
        )
        returned_blocks.append(mixed_block)
    returned = jnp.stack(returned_blocks).reshape(
        req_count, kv_count, per_kv, capacity, head_dim
    )
    returned = returned.transpose(0, 3, 1, 2, 4)
    attended = lax.dot_general(
        dispatch,
        returned.reshape(slot_total, q_cols),
        (((0,), (0,)), ((), ())),
        preferred_element_type=jnp.float32,
    ).astype(jnp.bfloat16)
    def out_part(rows):
        product = jnp.dot(rows, out_weight, preferred_element_type=jnp.float32)
        return product.astype(jnp.bfloat16)

    partial_cols = direct_gather_apply(attended, out_part, "req", req_count, req_index)
    partial_cols = partial_cols.reshape(req_count * local_rows, out_weight.shape[1])
    hs_count = lax.axis_size("head") * sub_count
    hs_index = lax.axis_index("head") * sub_count + sub_index
    head_count = lax.axis_size("head")
    by_group = partial_cols.reshape(sub_count, -1, partial_cols.shape[1])
    sub_sums = exchange_sum(by_group, "sub", sub_count, sub_index)
    per_hs = req_count // hs_count
    out_block = partial_cols.shape[1]
    sub_sums = sub_sums.reshape(head_count, per_hs, local_rows, out_block)
    head_index = lax.axis_index("head")
    out_width = per_hs * out_block
    residual = lax.dynamic_slice_in_dim(hidden_in, hs_index * out_width, out_width, 1)
    head_total = jnp.zeros((local_rows, out_width), jnp.float32)
    for step in range(per_hs):
        offset = ((req_index % per_hs - step) % per_hs) * out_block
        gathered = lax.dynamic_slice_in_dim(residual, offset, out_block, 1).astype(jnp.float32)
        for turn in range(head_count):
            group = (head_index + turn) % head_count
            chunk = lax.dynamic_index_in_dim(sub_sums, group, 0, keepdims=False)
            chunk = lax.dynamic_index_in_dim(
                chunk, (req_index + step) % per_hs, 0, keepdims=False
            )
            pairs = []
            for c in range(req_count):
                for h in range(head_count):
                    for u in range(sub_count):
                        g = (h + turn) % head_count
                        k = (u * head_count + g) * per_hs + (c + step) % per_hs
                        src = c * hs_count + h * sub_count + u
                        pairs.append((src, k * hs_count + c // per_hs))
            got = lax.ppermute(chunk, ("req", "head", "sub"), pairs).astype(jnp.float32)
            gathered = gathered + got
        head_total = lax.dynamic_update_slice_in_dim(head_total, gathered, offset, 1)
    return head_total.astype(jnp.bfloat16)


def solution(mesh):
    in_specs = (
        P(("groups", "req"), None),
        P("req", ("head", "sub")),
        P(),
        P(("groups", "req"), None, "head"),
        P(("groups", "req"), None, "head"),
        P(("head", "sub"), "req"),
        P(("groups", "req")),
        P(("groups", "req")),
        P("groups"),
    )
    out_specs = P(("groups", "req"), ("head", "sub"))
    return jax.shard_map(local, mesh=mesh, in_specs=in_specs, out_specs=out_specs, check_vma=False)
```

```python
import functools

import jax
import jax.numpy as jnp
from jax import lax
from jax.sharding import PartitionSpec as P
from jax.experimental import pallas as pl

HQ = 64
KVH = 8


def normalize_heads(queries, q_gain, head_dim):
    row_count = queries.shape[0]
    per_head = queries.astype(jnp.float32).reshape(row_count, -1, head_dim)
    inv_rms = lax.rsqrt(jnp.mean(per_head * per_head, axis=2, keepdims=True) + 1e-05)
    return (per_head * inv_rms * q_gain).reshape(row_count, -1).astype(jnp.bfloat16)


def direct_reduce_scatter(chunk_of, axis, count, index):
    own = chunk_of(index)
    total = None
    for shift in range(1, count):
        outgoing = chunk_of((index + shift) % count).astype(jnp.bfloat16)
        if shift == count - 1:
            own, outgoing = lax.optimization_barrier((own, outgoing))
        incoming = lax.ppermute(outgoing, axis, [(i, (i + shift) % count) for i in range(count)])
        incoming = incoming.astype(jnp.float32)
        total = incoming if total is None else total + incoming
    return own if total is None else own + total


def direct_gather_apply(block, apply, axis, count, index):
    own = apply(block)
    placed = jnp.zeros((count,) + own.shape, own.dtype)
    placed = lax.dynamic_update_index_in_dim(placed, own, index, 0)
    for shift in range(1, count):
        incoming = lax.ppermute(block, axis, [(i, (i + shift) % count) for i in range(count)])
        placed = lax.dynamic_update_index_in_dim(
            placed, apply(incoming), (index - shift) % count, 0
        )
    return placed


def exchange_sum(parts, axis, count, index):
    total = lax.dynamic_index_in_dim(parts, index, axis=0, keepdims=False).astype(jnp.float32)
    for shift in range(1, count):
        outgoing = lax.dynamic_index_in_dim(parts, (index + shift) % count, axis=0, keepdims=False)
        incoming = lax.ppermute(outgoing, axis, [(i, (i + shift) % count) for i in range(count)])
        total = total + incoming.astype(jnp.float32)
    return total.astype(jnp.bfloat16)


def attend_kernel(q_ref, k_ref, v_ref, o_ref, *, head_dim, token_count):
    padded_tokens = k_ref.shape[1]
    split = (token_count // 128) * 128
    scores = lax.dot_general(
        q_ref[0], k_ref[0], (((1,), (1,)), ((), ())), preferred_element_type=jnp.float32
    ) * (head_dim ** (-0.5))
    pieces = [scores[:, :split]] if split else []
    if split < padded_tokens:
        tail = scores[:, split:]
        valid = lax.broadcasted_iota(jnp.int32, tail.shape, 1) < token_count - split
        pieces.append(jnp.where(valid, tail, -jnp.inf))
    peak = jnp.max(pieces[0], axis=1, keepdims=True)
    for piece in pieces[1:]:
        peak = jnp.maximum(peak, jnp.max(piece, axis=1, keepdims=True))
    weights = [jnp.exp(piece - peak) for piece in pieces]
    total = sum(jnp.sum(w, axis=1, keepdims=True) for w in weights)
    inverse = 1.0 / total
    mixed = None
    start = 0
    for w in weights:
        width = w.shape[1]
        probs = (w * inverse).astype(jnp.bfloat16)
        term = jnp.dot(probs, v_ref[0, start:start + width, :], preferred_element_type=jnp.float32)
        mixed = term if mixed is None else mixed + term
        start += width
    o_ref[0] = mixed.astype(o_ref.dtype)


def attend(stacked, keys, values, token_count):
    kv_count, stacked_rows, head_dim = stacked.shape
    padded_tokens = keys.shape[1]
    kernel = functools.partial(attend_kernel, head_dim=head_dim, token_count=token_count)
    flops = 4 * stacked_rows * padded_tokens * head_dim * kv_count
    moved = 2 * (2 * stacked_rows * head_dim * kv_count + 2 * padded_tokens * head_dim * kv_count)
    return pl.pallas_call(
        kernel,
        grid=(kv_count,),
        in_specs=[
            pl.BlockSpec((1, stacked_rows, head_dim), lambda k: (k, 0, 0)),
            pl.BlockSpec((1, padded_tokens, head_dim), lambda k: (k, 0, 0)),
            pl.BlockSpec((1, padded_tokens, head_dim), lambda k: (k, 0, 0)),
        ],
        out_specs=pl.BlockSpec((1, stacked_rows, head_dim), lambda k: (k, 0, 0)),
        out_shape=jax.ShapeDtypeStruct((kv_count, stacked_rows, head_dim), jnp.bfloat16),
        cost_estimate=pl.CostEstimate(
            flops=flops,
            transcendentals=stacked_rows * padded_tokens * kv_count,
            bytes_accessed=moved,
        ),
    )(stacked, keys, values)


def local(
    hidden_in,
    q_weight,
    q_gain,
    key_cache,
    value_cache,
    out_weight,
    req_image,
    image_count,
    image_home,
):
    req_count = lax.axis_size("req")
    local_rows = hidden_in.shape[0]
    q_cols = q_weight.shape[1]
    head_dim = q_gain.shape[0]
    group_size = HQ // KVH
    heads_here = q_cols // head_dim
    sub_count = lax.axis_size("sub")
    sub_index = lax.axis_index("sub")
    block_width = hidden_in.shape[1] // req_count
    half_rows = local_rows // sub_count
    req_index = lax.axis_index("req")
    my_rows = lax.dynamic_slice_in_dim(hidden_in, sub_index * half_rows, half_rows, 0)

    def my_block(dest):
        return lax.dynamic_slice_in_dim(my_rows, dest * block_width, block_width, 1)

    spread_part = jnp.zeros((req_count, half_rows, block_width), hidden_in.dtype)
    spread_part = lax.dynamic_update_index_in_dim(spread_part, my_block(req_index), req_index, 0)
    for shift in range(1, req_count):
        arrived_part = lax.ppermute(
            my_block((req_index + shift) % req_count),
            "req",
            [(i, (i + shift) % req_count) for i in range(req_count)],
        )
        spread_part = lax.dynamic_update_index_in_dim(
            spread_part, arrived_part, (req_index - shift) % req_count, 0
        )
    spread_cols = jnp.zeros((req_count, sub_count, half_rows, block_width), hidden_in.dtype)
    spread_cols = lax.dynamic_update_index_in_dim(spread_cols, spread_part, sub_index, 1)
    for shift in range(1, sub_count):
        other_part = lax.ppermute(
            spread_part, "sub", [(i, (i + shift) % sub_count) for i in range(sub_count)]
        )
        spread_cols = lax.dynamic_update_index_in_dim(
            spread_cols, other_part, (sub_index - shift) % sub_count, 1
        )
    spread_cols = spread_cols.reshape(req_count * local_rows, block_width)
    def query_chunk(owner):
        rows = lax.dynamic_slice_in_dim(spread_cols, owner * local_rows, local_rows, 0)
        product = jnp.dot(rows, q_weight, preferred_element_type=jnp.float32)
        return product.astype(jnp.bfloat16).astype(jnp.float32)

    query_sum = direct_reduce_scatter(query_chunk, "req", req_count, req_index)
    queries = lax.optimization_barrier(query_sum.astype(jnp.bfloat16))
    normalized = normalize_heads(queries, q_gain, head_dim)
    capacity = 2 * local_rows // req_count
    slot_total = req_count * capacity
    table_ids = lax.broadcasted_iota(jnp.int32, (local_rows, image_home.shape[0]), 1)
    home_rows = jnp.sum(jnp.where(req_image[:, None] == table_ids, image_home[None, :], 0), axis=1)
    wanted = image_count == 1
    dest_ids = lax.broadcasted_iota(jnp.int32, (local_rows, req_count), 1)
    to_dest = ((home_rows[:, None] == dest_ids) & wanted[:, None]).astype(jnp.int32)
    earlier = jnp.cumsum(to_dest, axis=0) - to_dest
    position = ((home_rows - req_index) % req_count) * capacity + jnp.sum(
        earlier * to_dest, axis=1
    )
    slot_ids = lax.broadcasted_iota(jnp.int32, (slot_total, local_rows), 0)
    dispatch = ((slot_ids == position[None, :]) & wanted[None, :]).astype(jnp.bfloat16)
    outgoing = jnp.dot(dispatch, normalized, preferred_element_type=jnp.float32).astype(
        jnp.bfloat16
    )
    kv_count = max(1, heads_here // group_size)
    per_kv = heads_here // kv_count
    outgoing = outgoing.reshape(req_count, capacity, kv_count, per_kv, head_dim)
    outgoing = outgoing.transpose(0, 2, 3, 1, 4).reshape(
        req_count, kv_count, per_kv * capacity, head_dim
    )
    kv_first = sub_index * heads_here // group_size
    token_count = key_cache.shape[1]
    padded_tokens = -(-token_count // 128) * 128
    def group_major(cache):
        picked = lax.dynamic_slice_in_dim(cache[0], kv_first * head_dim, kv_count * head_dim, 1)
        picked = jnp.pad(picked, ((0, padded_tokens - token_count), (0, 0)))
        return picked.reshape(padded_tokens, kv_count, head_dim).transpose(1, 0, 2)

    keys_here = group_major(key_cache)
    values_here = group_major(value_cache)
    arrived_blocks = [outgoing[0]] + [
        lax.ppermute(
            outgoing[shift], "req", [(i, (i + shift) % req_count) for i in range(req_count)]
        )
        for shift in range(1, req_count)
    ]
    returned_blocks = [
        attend(outgoing[0], keys_here, values_here, token_count)
    ]
    if req_count > 1:
        returned_blocks[0], arrived_blocks[1] = lax.optimization_barrier(
            (returned_blocks[0], arrived_blocks[1])
        )
    for shift in range(1, req_count):
        mixed_block = attend(arrived_blocks[shift], keys_here, values_here, token_count)
        mixed_block = lax.ppermute(
            mixed_block, "req", [(i, (i - shift) % req_count) for i in range(req_count)]
        )
        returned_blocks.append(mixed_block)
    returned = jnp.stack(returned_blocks).reshape(
        req_count, kv_count, per_kv, capacity, head_dim
    )
    returned = returned.transpose(0, 3, 1, 2, 4)
    attended = lax.dot_general(
        dispatch,
        returned.reshape(slot_total, q_cols),
        (((0,), (0,)), ((), ())),
        preferred_element_type=jnp.float32,
    ).astype(jnp.bfloat16)
    def out_part(rows):
        product = jnp.dot(rows, out_weight, preferred_element_type=jnp.float32)
        return product.astype(jnp.bfloat16)

    partial_cols = direct_gather_apply(attended, out_part, "req", req_count, req_index)
    partial_cols = partial_cols.reshape(req_count * local_rows, out_weight.shape[1])
    hs_count = lax.axis_size("head") * sub_count
    hs_index = lax.axis_index("head") * sub_count + sub_index
    head_count = lax.axis_size("head")
    by_group = partial_cols.reshape(sub_count, -1, partial_cols.shape[1])
    sub_sums = exchange_sum(by_group, "sub", sub_count, sub_index)
    per_hs = req_count // hs_count
    out_block = partial_cols.shape[1]
    sub_sums = sub_sums.reshape(head_count, per_hs, local_rows, out_block)
    head_index = lax.axis_index("head")
    head_total = jnp.zeros((local_rows, per_hs * out_block), jnp.float32)
    for step in range(per_hs):
        gathered = None
        for turn in range(head_count):
            group = (head_index + turn) % head_count
            chunk = lax.dynamic_index_in_dim(sub_sums, group, 0, keepdims=False)
            chunk = lax.dynamic_index_in_dim(
                chunk, (req_index + step) % per_hs, 0, keepdims=False
            )
            pairs = []
            for c in range(req_count):
                for h in range(head_count):
                    for u in range(sub_count):
                        g = (h + turn) % head_count
                        k = (u * head_count + g) * per_hs + (c + step) % per_hs
                        src = c * hs_count + h * sub_count + u
                        pairs.append((src, k * hs_count + c // per_hs))
            got = lax.ppermute(chunk, ("req", "head", "sub"), pairs).astype(jnp.float32)
            gathered = got if gathered is None else gathered + got
        head_total = lax.dynamic_update_slice_in_dim(
            head_total, gathered, ((req_index % per_hs - step) % per_hs) * out_block, 1
        )
    head_total = head_total.astype(jnp.float32)
    out_width = head_total.shape[1]
    residual = lax.dynamic_slice_in_dim(hidden_in, hs_index * out_width, out_width, 1)
    return (residual.astype(jnp.float32) + head_total).astype(jnp.bfloat16)


def solution(mesh):
    in_specs = (
        P(("groups", "req"), None),
        P("req", ("head", "sub")),
        P(),
        P(("groups", "req"), None, "head"),
        P(("groups", "req"), None, "head"),
        P(("head", "sub"), "req"),
        P(("groups", "req")),
        P(("groups", "req")),
        P("groups"),
    )
    out_specs = P(("groups", "req"), ("head", "sub"))
    return jax.shard_map(local, mesh=mesh, in_specs=in_specs, out_specs=out_specs, check_vma=False)
```

```python
import functools

import jax
import jax.numpy as jnp
from jax import lax
from jax.sharding import PartitionSpec as P
from jax.experimental import pallas as pl

HQ = 64
KVH = 8


def normalize_heads(queries, q_gain, head_dim):
    row_count = queries.shape[0]
    per_head = queries.astype(jnp.float32).reshape(row_count, -1, head_dim)
    inv_rms = lax.rsqrt(jnp.mean(per_head * per_head, axis=2, keepdims=True) + 1e-05)
    return (per_head * inv_rms * q_gain).reshape(row_count, -1).astype(jnp.bfloat16)


def direct_reduce_scatter(chunk_of, axis, count, index):
    total = None
    for shift in range(1, count):
        outgoing = chunk_of((index + shift) % count).astype(jnp.bfloat16)
        incoming = lax.ppermute(outgoing, axis, [(i, (i + shift) % count) for i in range(count)])
        incoming = incoming.astype(jnp.float32)
        total = incoming if total is None else total + incoming
    own = chunk_of(index)
    return own if total is None else own + total


def direct_gather_apply(block, apply, axis, count, index):
    own = apply(block)
    placed = jnp.zeros((count,) + own.shape, own.dtype)
    placed = lax.dynamic_update_index_in_dim(placed, own, index, 0)
    for shift in range(1, count):
        incoming = lax.ppermute(block, axis, [(i, (i + shift) % count) for i in range(count)])
        placed = lax.dynamic_update_index_in_dim(
            placed, apply(incoming), (index - shift) % count, 0
        )
    return placed


def exchange_sum(parts, axis, count, index):
    total = lax.dynamic_index_in_dim(parts, index, axis=0, keepdims=False).astype(jnp.float32)
    for shift in range(1, count):
        outgoing = lax.dynamic_index_in_dim(parts, (index + shift) % count, axis=0, keepdims=False)
        incoming = lax.ppermute(outgoing, axis, [(i, (i + shift) % count) for i in range(count)])
        total = total + incoming.astype(jnp.float32)
    return total.astype(jnp.bfloat16)


def attend_kernel(q_ref, k_ref, v_ref, o_ref, *, head_dim, token_count):
    padded_tokens = k_ref.shape[1]
    split = (token_count // 128) * 128
    scores = lax.dot_general(
        q_ref[0], k_ref[0], (((1,), (1,)), ((), ())), preferred_element_type=jnp.float32
    ) * (head_dim ** (-0.5))
    pieces = [scores[:, :split]] if split else []
    if split < padded_tokens:
        tail = scores[:, split:]
        valid = lax.broadcasted_iota(jnp.int32, tail.shape, 1) < token_count - split
        pieces.append(jnp.where(valid, tail, -jnp.inf))
    peak = jnp.max(pieces[0], axis=1, keepdims=True)
    for piece in pieces[1:]:
        peak = jnp.maximum(peak, jnp.max(piece, axis=1, keepdims=True))
    weights = [jnp.exp(piece - peak) for piece in pieces]
    total = sum(jnp.sum(w, axis=1, keepdims=True) for w in weights)
    inverse = 1.0 / total
    mixed = None
    start = 0
    for w in weights:
        width = w.shape[1]
        probs = (w * inverse).astype(jnp.bfloat16)
        term = jnp.dot(probs, v_ref[0, start:start + width, :], preferred_element_type=jnp.float32)
        mixed = term if mixed is None else mixed + term
        start += width
    o_ref[0] = mixed.astype(o_ref.dtype)


def attend(stacked, keys, values, token_count):
    kv_count, stacked_rows, head_dim = stacked.shape
    padded_tokens = keys.shape[1]
    kernel = functools.partial(attend_kernel, head_dim=head_dim, token_count=token_count)
    flops = 4 * stacked_rows * padded_tokens * head_dim * kv_count
    moved = 2 * (2 * stacked_rows * head_dim * kv_count + 2 * padded_tokens * head_dim * kv_count)
    return pl.pallas_call(
        kernel,
        grid=(kv_count,),
        in_specs=[
            pl.BlockSpec((1, stacked_rows, head_dim), lambda k: (k, 0, 0)),
            pl.BlockSpec((1, padded_tokens, head_dim), lambda k: (k, 0, 0)),
            pl.BlockSpec((1, padded_tokens, head_dim), lambda k: (k, 0, 0)),
        ],
        out_specs=pl.BlockSpec((1, stacked_rows, head_dim), lambda k: (k, 0, 0)),
        out_shape=jax.ShapeDtypeStruct((kv_count, stacked_rows, head_dim), jnp.bfloat16),
        cost_estimate=pl.CostEstimate(
            flops=flops,
            transcendentals=stacked_rows * padded_tokens * kv_count,
            bytes_accessed=moved,
        ),
    )(stacked, keys, values)


def local(
    hidden_in,
    q_weight,
    q_gain,
    key_cache,
    value_cache,
    out_weight,
    req_image,
    image_count,
    image_home,
):
    req_count = lax.axis_size("req")
    local_rows = hidden_in.shape[0]
    q_cols = q_weight.shape[1]
    head_dim = q_gain.shape[0]
    group_size = HQ // KVH
    heads_here = q_cols // head_dim
    sub_count = lax.axis_size("sub")
    sub_index = lax.axis_index("sub")
    block_width = hidden_in.shape[1] // req_count
    half_rows = local_rows // sub_count
    req_index = lax.axis_index("req")
    my_rows = lax.dynamic_slice_in_dim(hidden_in, sub_index * half_rows, half_rows, 0)

    def my_block(dest):
        return lax.dynamic_slice_in_dim(my_rows, dest * block_width, block_width, 1)

    spread_part = jnp.zeros((req_count, half_rows, block_width), hidden_in.dtype)
    spread_part = lax.dynamic_update_index_in_dim(spread_part, my_block(req_index), req_index, 0)
    for shift in range(1, req_count):
        arrived_part = lax.ppermute(
            my_block((req_index + shift) % req_count),
            "req",
            [(i, (i + shift) % req_count) for i in range(req_count)],
        )
        spread_part = lax.dynamic_update_index_in_dim(
            spread_part, arrived_part, (req_index - shift) % req_count, 0
        )
    spread_cols = jnp.zeros((req_count, sub_count, half_rows, block_width), hidden_in.dtype)
    spread_cols = lax.dynamic_update_index_in_dim(spread_cols, spread_part, sub_index, 1)
    for shift in range(1, sub_count):
        other_part = lax.ppermute(
            spread_part, "sub", [(i, (i + shift) % sub_count) for i in range(sub_count)]
        )
        spread_cols = lax.dynamic_update_index_in_dim(
            spread_cols, other_part, (sub_index - shift) % sub_count, 1
        )
    spread_cols = spread_cols.reshape(req_count * local_rows, block_width)
    def query_chunk(owner):
        rows = lax.dynamic_slice_in_dim(spread_cols, owner * local_rows, local_rows, 0)
        product = jnp.dot(rows, q_weight, preferred_element_type=jnp.float32)
        return product.astype(jnp.bfloat16).astype(jnp.float32)

    query_sum = direct_reduce_scatter(query_chunk, "req", req_count, req_index)
    queries = query_sum.astype(jnp.bfloat16)
    normalized = normalize_heads(queries, q_gain, head_dim)
    capacity = 2 * local_rows // req_count
    slot_total = req_count * capacity
    table_ids = lax.broadcasted_iota(jnp.int32, (local_rows, image_home.shape[0]), 1)
    home_rows = jnp.sum(jnp.where(req_image[:, None] == table_ids, image_home[None, :], 0), axis=1)
    wanted = image_count == 1
    dest_ids = lax.broadcasted_iota(jnp.int32, (local_rows, req_count), 1)
    to_dest = ((home_rows[:, None] == dest_ids) & wanted[:, None]).astype(jnp.int32)
    earlier = jnp.cumsum(to_dest, axis=0) - to_dest
    position = ((home_rows - req_index) % req_count) * capacity + jnp.sum(
        earlier * to_dest, axis=1
    )
    slot_ids = lax.broadcasted_iota(jnp.int32, (slot_total, local_rows), 0)
    dispatch = ((slot_ids == position[None, :]) & wanted[None, :]).astype(jnp.bfloat16)
    outgoing = jnp.dot(dispatch, normalized, preferred_element_type=jnp.float32).astype(
        jnp.bfloat16
    )
    kv_count = max(1, heads_here // group_size)
    per_kv = heads_here // kv_count
    outgoing = outgoing.reshape(req_count, capacity, kv_count, per_kv, head_dim)
    outgoing = outgoing.transpose(0, 2, 3, 1, 4).reshape(
        req_count, kv_count, per_kv * capacity, head_dim
    )
    kv_first = sub_index * heads_here // group_size
    token_count = key_cache.shape[1]
    padded_tokens = -(-token_count // 128) * 128
    def group_major(cache):
        picked = lax.dynamic_slice_in_dim(cache[0], kv_first * head_dim, kv_count * head_dim, 1)
        picked = jnp.pad(picked, ((0, padded_tokens - token_count), (0, 0)))
        return picked.reshape(padded_tokens, kv_count, head_dim).transpose(1, 0, 2)

    keys_here = group_major(key_cache)
    values_here = group_major(value_cache)
    arrived_blocks = [outgoing[0]] + [
        lax.ppermute(
            outgoing[shift], "req", [(i, (i + shift) % req_count) for i in range(req_count)]
        )
        for shift in range(1, req_count)
    ]
    returned_blocks = [
        attend(outgoing[0], keys_here, values_here, token_count)
    ]
    if req_count > 1:
        returned_blocks[0], arrived_blocks[1] = lax.optimization_barrier(
            (returned_blocks[0], arrived_blocks[1])
        )
    for shift in range(1, req_count):
        mixed_block = attend(arrived_blocks[shift], keys_here, values_here, token_count)
        mixed_block = lax.ppermute(
            mixed_block, "req", [(i, (i - shift) % req_count) for i in range(req_count)]
        )
        returned_blocks.append(mixed_block)
    returned = jnp.stack(returned_blocks).reshape(
        req_count, kv_count, per_kv, capacity, head_dim
    )
    returned = returned.transpose(0, 3, 1, 2, 4)
    attended = lax.dot_general(
        dispatch,
        returned.reshape(slot_total, q_cols),
        (((0,), (0,)), ((), ())),
        preferred_element_type=jnp.float32,
    ).astype(jnp.bfloat16)
    def out_part(rows):
        product = jnp.dot(rows, out_weight, preferred_element_type=jnp.float32)
        return product.astype(jnp.bfloat16)

    partial_cols = direct_gather_apply(attended, out_part, "req", req_count, req_index)
    partial_cols = partial_cols.reshape(req_count * local_rows, out_weight.shape[1])
    hs_count = lax.axis_size("head") * sub_count
    hs_index = lax.axis_index("head") * sub_count + sub_index
    head_count = lax.axis_size("head")
    by_group = partial_cols.reshape(sub_count, -1, partial_cols.shape[1])
    sub_sums = exchange_sum(by_group, "sub", sub_count, sub_index)
    per_hs = req_count // hs_count
    out_block = partial_cols.shape[1]
    sub_sums = sub_sums.reshape(head_count, per_hs, local_rows, out_block)
    head_index = lax.axis_index("head")
    head_total = jnp.zeros((local_rows, per_hs * out_block), jnp.float32)
    for step in range(per_hs):
        gathered = None
        for turn in range(head_count):
            group = (head_index + turn) % head_count
            chunk = lax.dynamic_index_in_dim(sub_sums, group, 0, keepdims=False)
            chunk = lax.dynamic_index_in_dim(
                chunk, (req_index + step) % per_hs, 0, keepdims=False
            )
            pairs = []
            for c in range(req_count):
                for h in range(head_count):
                    for u in range(sub_count):
                        g = (h + turn) % head_count
                        k = (u * head_count + g) * per_hs + (c + step) % per_hs
                        src = c * hs_count + h * sub_count + u
                        pairs.append((src, k * hs_count + c // per_hs))
            got = lax.ppermute(chunk, ("req", "head", "sub"), pairs).astype(jnp.float32)
            gathered = got if gathered is None else gathered + got
        head_total = lax.dynamic_update_slice_in_dim(
            head_total, gathered, ((req_index % per_hs - step) % per_hs) * out_block, 1
        )
    head_total = head_total.astype(jnp.float32)
    out_width = head_total.shape[1]
    residual = lax.dynamic_slice_in_dim(hidden_in, hs_index * out_width, out_width, 1)
    return (residual.astype(jnp.float32) + head_total).astype(jnp.bfloat16)


def solution(mesh):
    in_specs = (
        P(("groups", "req"), None),
        P("req", ("head", "sub")),
        P(),
        P(("groups", "req"), None, "head"),
        P(("groups", "req"), None, "head"),
        P(("head", "sub"), "req"),
        P(("groups", "req")),
        P(("groups", "req")),
        P("groups"),
    )
    out_specs = P(("groups", "req"), ("head", "sub"))
    return jax.shard_map(local, mesh=mesh, in_specs=in_specs, out_specs=out_specs, check_vma=False)
```

```python
import functools

import jax
import jax.numpy as jnp
from jax import lax
from jax.sharding import PartitionSpec as P
from jax.experimental import pallas as pl

HQ = 64
KVH = 8


def normalize_heads(queries, q_gain, head_dim):
    row_count = queries.shape[0]
    per_head = queries.astype(jnp.float32).reshape(row_count, -1, head_dim)
    inv_rms = lax.rsqrt(jnp.mean(per_head * per_head, axis=2, keepdims=True) + 1e-05)
    return (per_head * inv_rms * q_gain).reshape(row_count, -1).astype(jnp.bfloat16)


def direct_reduce_scatter(chunk_of, axis, count, index):
    total = None
    for shift in range(1, count):
        outgoing = chunk_of((index + shift) % count).astype(jnp.bfloat16)
        incoming = lax.ppermute(outgoing, axis, [(i, (i + shift) % count) for i in range(count)])
        incoming = incoming.astype(jnp.float32)
        total = incoming if total is None else total + incoming
    own = chunk_of(index)
    return own if total is None else own + total


def direct_gather_apply(block, apply, axis, count, index):
    own = apply(block)
    placed = jnp.zeros((count,) + own.shape, own.dtype)
    placed = lax.dynamic_update_index_in_dim(placed, own, index, 0)
    for shift in range(1, count):
        incoming = lax.ppermute(block, axis, [(i, (i + shift) % count) for i in range(count)])
        placed = lax.dynamic_update_index_in_dim(
            placed, apply(incoming), (index - shift) % count, 0
        )
    return placed


def exchange_sum(parts, axis, count, index):
    total = lax.dynamic_index_in_dim(parts, index, axis=0, keepdims=False).astype(jnp.float32)
    for shift in range(1, count):
        outgoing = lax.dynamic_index_in_dim(parts, (index + shift) % count, axis=0, keepdims=False)
        incoming = lax.ppermute(outgoing, axis, [(i, (i + shift) % count) for i in range(count)])
        total = total + incoming.astype(jnp.float32)
    return total.astype(jnp.bfloat16)


def attend_kernel(q_ref, k_ref, v_ref, o_ref, *, head_dim, token_count):
    padded_tokens = k_ref.shape[1]
    split = (token_count // 128) * 128
    scores = lax.dot_general(
        q_ref[0], k_ref[0], (((1,), (1,)), ((), ())), preferred_element_type=jnp.float32
    ) * (head_dim ** (-0.5))
    pieces = [scores[:, :split]] if split else []
    if split < padded_tokens:
        tail = scores[:, split:]
        valid = lax.broadcasted_iota(jnp.int32, tail.shape, 1) < token_count - split
        pieces.append(jnp.where(valid, tail, -jnp.inf))
    peak = jnp.max(pieces[0], axis=1, keepdims=True)
    for piece in pieces[1:]:
        peak = jnp.maximum(peak, jnp.max(piece, axis=1, keepdims=True))
    weights = [jnp.exp(piece - peak) for piece in pieces]
    total = sum(jnp.sum(w, axis=1, keepdims=True) for w in weights)
    inverse = 1.0 / total
    mixed = None
    start = 0
    for w in weights:
        width = w.shape[1]
        probs = (w * inverse).astype(jnp.bfloat16)
        term = jnp.dot(probs, v_ref[0, start:start + width, :], preferred_element_type=jnp.float32)
        mixed = term if mixed is None else mixed + term
        start += width
    o_ref[0] = mixed.astype(o_ref.dtype)


def attend(stacked, keys, values, token_count):
    kv_count, stacked_rows, head_dim = stacked.shape
    padded_tokens = keys.shape[1]
    kernel = functools.partial(attend_kernel, head_dim=head_dim, token_count=token_count)
    flops = 4 * stacked_rows * padded_tokens * head_dim * kv_count
    moved = 2 * (2 * stacked_rows * head_dim * kv_count + 2 * padded_tokens * head_dim * kv_count)
    return pl.pallas_call(
        kernel,
        grid=(kv_count,),
        in_specs=[
            pl.BlockSpec((1, stacked_rows, head_dim), lambda k: (k, 0, 0)),
            pl.BlockSpec((1, padded_tokens, head_dim), lambda k: (k, 0, 0)),
            pl.BlockSpec((1, padded_tokens, head_dim), lambda k: (k, 0, 0)),
        ],
        out_specs=pl.BlockSpec((1, stacked_rows, head_dim), lambda k: (k, 0, 0)),
        out_shape=jax.ShapeDtypeStruct((kv_count, stacked_rows, head_dim), jnp.bfloat16),
        cost_estimate=pl.CostEstimate(
            flops=flops,
            transcendentals=stacked_rows * padded_tokens * kv_count,
            bytes_accessed=moved,
        ),
    )(stacked, keys, values)


def local(
    hidden_in,
    q_weight,
    q_gain,
    key_cache,
    value_cache,
    out_weight,
    req_image,
    image_count,
    image_home,
):
    req_count = lax.axis_size("req")
    local_rows = hidden_in.shape[0]
    q_cols = q_weight.shape[1]
    head_dim = q_gain.shape[0]
    group_size = HQ // KVH
    heads_here = q_cols // head_dim
    sub_count = lax.axis_size("sub")
    sub_index = lax.axis_index("sub")
    block_width = hidden_in.shape[1] // req_count
    half_rows = local_rows // sub_count
    req_index = lax.axis_index("req")
    my_rows = lax.dynamic_slice_in_dim(hidden_in, sub_index * half_rows, half_rows, 0)

    def my_block(dest):
        return lax.dynamic_slice_in_dim(my_rows, dest * block_width, block_width, 1)

    spread_part = jnp.zeros((req_count, half_rows, block_width), hidden_in.dtype)
    spread_part = lax.dynamic_update_index_in_dim(spread_part, my_block(req_index), req_index, 0)
    for shift in range(1, req_count):
        arrived_part = lax.ppermute(
            my_block((req_index + shift) % req_count),
            "req",
            [(i, (i + shift) % req_count) for i in range(req_count)],
        )
        spread_part = lax.dynamic_update_index_in_dim(
            spread_part, arrived_part, (req_index - shift) % req_count, 0
        )
    spread_cols = jnp.zeros((req_count, sub_count, half_rows, block_width), hidden_in.dtype)
    spread_cols = lax.dynamic_update_index_in_dim(spread_cols, spread_part, sub_index, 1)
    for shift in range(1, sub_count):
        other_part = lax.ppermute(
            spread_part, "sub", [(i, (i + shift) % sub_count) for i in range(sub_count)]
        )
        spread_cols = lax.dynamic_update_index_in_dim(
            spread_cols, other_part, (sub_index - shift) % sub_count, 1
        )
    spread_cols = spread_cols.reshape(req_count * local_rows, block_width)
    def query_chunk(owner):
        rows = lax.dynamic_slice_in_dim(spread_cols, owner * local_rows, local_rows, 0)
        product = jnp.dot(rows, q_weight, preferred_element_type=jnp.float32)
        return product.astype(jnp.bfloat16).astype(jnp.float32)

    query_sum = direct_reduce_scatter(query_chunk, "req", req_count, req_index)
    queries = lax.optimization_barrier(query_sum.astype(jnp.bfloat16))
    normalized = normalize_heads(queries, q_gain, head_dim)
    capacity = 2 * local_rows // req_count
    slot_total = req_count * capacity
    table_ids = lax.broadcasted_iota(jnp.int32, (local_rows, image_home.shape[0]), 1)
    home_rows = jnp.sum(jnp.where(req_image[:, None] == table_ids, image_home[None, :], 0), axis=1)
    wanted = image_count == 1
    dest_ids = lax.broadcasted_iota(jnp.int32, (local_rows, req_count), 1)
    to_dest = ((home_rows[:, None] == dest_ids) & wanted[:, None]).astype(jnp.int32)
    earlier = jnp.cumsum(to_dest, axis=0) - to_dest
    position = ((home_rows - req_index) % req_count) * capacity + jnp.sum(
        earlier * to_dest, axis=1
    )
    slot_ids = lax.broadcasted_iota(jnp.int32, (slot_total, local_rows), 0)
    dispatch = ((slot_ids == position[None, :]) & wanted[None, :]).astype(jnp.bfloat16)
    outgoing = jnp.dot(dispatch, normalized, preferred_element_type=jnp.bfloat16)
    kv_count = max(1, heads_here // group_size)
    per_kv = heads_here // kv_count
    outgoing = outgoing.reshape(req_count, capacity, kv_count, per_kv, head_dim)
    outgoing = outgoing.transpose(0, 2, 3, 1, 4).reshape(
        req_count, kv_count, per_kv * capacity, head_dim
    )
    kv_first = sub_index * heads_here // group_size
    token_count = key_cache.shape[1]
    padded_tokens = -(-token_count // 128) * 128
    def group_major(cache):
        picked = lax.dynamic_slice_in_dim(cache[0], kv_first * head_dim, kv_count * head_dim, 1)
        picked = jnp.pad(picked, ((0, padded_tokens - token_count), (0, 0)))
        return picked.reshape(padded_tokens, kv_count, head_dim).transpose(1, 0, 2)

    keys_here = group_major(key_cache)
    values_here = group_major(value_cache)
    arrived_blocks = [outgoing[0]] + [
        lax.ppermute(
            outgoing[shift], "req", [(i, (i + shift) % req_count) for i in range(req_count)]
        )
        for shift in range(1, req_count)
    ]
    returned_blocks = [
        attend(outgoing[0], keys_here, values_here, token_count)
    ]
    if req_count > 1:
        returned_blocks[0], arrived_blocks[1] = lax.optimization_barrier(
            (returned_blocks[0], arrived_blocks[1])
        )
    for shift in range(1, req_count):
        mixed_block = attend(arrived_blocks[shift], keys_here, values_here, token_count)
        mixed_block = lax.ppermute(
            mixed_block, "req", [(i, (i - shift) % req_count) for i in range(req_count)]
        )
        returned_blocks.append(mixed_block)
    returned = jnp.stack(returned_blocks).reshape(
        req_count, kv_count, per_kv, capacity, head_dim
    )
    returned = returned.transpose(0, 3, 1, 2, 4)
    attended = lax.dot_general(
        dispatch,
        returned.reshape(slot_total, q_cols),
        (((0,), (0,)), ((), ())),
        preferred_element_type=jnp.bfloat16,
    )
    def out_part(rows):
        product = jnp.dot(rows, out_weight, preferred_element_type=jnp.float32)
        return product.astype(jnp.bfloat16)

    partial_cols = direct_gather_apply(attended, out_part, "req", req_count, req_index)
    partial_cols = partial_cols.reshape(req_count * local_rows, out_weight.shape[1])
    hs_count = lax.axis_size("head") * sub_count
    hs_index = lax.axis_index("head") * sub_count + sub_index
    head_count = lax.axis_size("head")
    by_group = partial_cols.reshape(sub_count, -1, partial_cols.shape[1])
    sub_sums = exchange_sum(by_group, "sub", sub_count, sub_index)
    per_hs = req_count // hs_count
    out_block = partial_cols.shape[1]
    sub_sums = sub_sums.reshape(head_count, per_hs, local_rows, out_block)
    head_index = lax.axis_index("head")
    head_total = jnp.zeros((local_rows, per_hs * out_block), jnp.float32)
    for step in range(per_hs):
        gathered = None
        for turn in range(head_count):
            group = (head_index + turn) % head_count
            chunk = lax.dynamic_index_in_dim(sub_sums, group, 0, keepdims=False)
            chunk = lax.dynamic_index_in_dim(
                chunk, (req_index + step) % per_hs, 0, keepdims=False
            )
            pairs = []
            for c in range(req_count):
                for h in range(head_count):
                    for u in range(sub_count):
                        g = (h + turn) % head_count
                        k = (u * head_count + g) * per_hs + (c + step) % per_hs
                        src = c * hs_count + h * sub_count + u
                        pairs.append((src, k * hs_count + c // per_hs))
            got = lax.ppermute(chunk, ("req", "head", "sub"), pairs).astype(jnp.float32)
            gathered = got if gathered is None else gathered + got
        head_total = lax.dynamic_update_slice_in_dim(
            head_total, gathered, ((req_index % per_hs - step) % per_hs) * out_block, 1
        )
    head_total = head_total.astype(jnp.float32)
    out_width = head_total.shape[1]
    residual = lax.dynamic_slice_in_dim(hidden_in, hs_index * out_width, out_width, 1)
    return (residual.astype(jnp.float32) + head_total).astype(jnp.bfloat16)


def solution(mesh):
    in_specs = (
        P(("groups", "req"), None),
        P("req", ("head", "sub")),
        P(),
        P(("groups", "req"), None, "head"),
        P(("groups", "req"), None, "head"),
        P(("head", "sub"), "req"),
        P(("groups", "req")),
        P(("groups", "req")),
        P("groups"),
    )
    out_specs = P(("groups", "req"), ("head", "sub"))
    return jax.shard_map(local, mesh=mesh, in_specs=in_specs, out_specs=out_specs, check_vma=False)
```
